32 devices in a mesh: seq: 8 (over z, y), grp: 4 (over x, core).
Axes of the slice: x: 2, y: 2, z: 4, core: 2. Of those that a mesh axis runs over, the one named last changes fastest.
Arguments:
- query_rows: bfloat16 [4096, 8192], P(('seq', 'grp')), may hold values from -6 to 6
- key_matrix: bfloat16 [4096, 1024], P(('seq', 'grp')), may hold values from -6 to 6
- value_matrix: bfloat16 [4096, 1024], P(('seq', 'grp')), may hold values from -6 to 6
- vertical: int32 [64, 3], replicated, may hold values from 0 to 63, as said below
- slash_offsets: int32 [64, 3], replicated, may hold values from 0 to 8, as said below
Outputs:
- attended: bfloat16 [4096, 8192], P(('seq', 'grp'))
The draws below stay inside these ranges and needn't reach their ends.
Inputs may be any that keep to these rules, and one draw needn't show every extreme that they name: Each head's vertical blocks are distinct and rise along the row. `slash_offsets`: column 0 is 0; each head's offsets are distinct and rise along the row.
All inputs are finite; a program needn't handle non-finite values.
Results may differ from the reference program's by a relative error of at most 0.0043.
Values may be sent and summed in bfloat16 or wider, within the bound.
No kernel may reach another device: no remote copies, remote signals or barrier semaphores. Data moves between devices by JAX's collectives and lax.ppermute only.
A program may use at most 64 MiB of HBM per device.

```python
import jax
import jax.numpy as jnp
from jax import lax

QUERY_HEADS = 64
KEY_VALUE_HEADS = 8
HEAD_DIMENSION = 128
MASK_BLOCK_SIZE = 64
SEQUENCE_TOKENS = 4096
BLOCK_TOTAL = 64
GB = 8


def starting_region(key, salt, width):
    field_key = jax.random.fold_in(key, salt)
    return jnp.clip(jax.random.normal(field_key, (SEQUENCE_TOKENS, width), jnp.float32), -6.0, 6.0)


def draw_query_rows(key, part):
    region_span = starting_region(key, 1, QUERY_HEADS * HEAD_DIMENSION)
    return region_span.astype(jnp.bfloat16)


def draw_key_matrix(key, part):
    region_span = starting_region(key, 2, KEY_VALUE_HEADS * HEAD_DIMENSION)
    return region_span.astype(jnp.bfloat16)


def draw_vertical(key, part):
    one_third = BLOCK_TOTAL // 3
    subkeys = jax.random.split(key, 3)
    earliest = jax.random.randint(subkeys[0], (QUERY_HEADS,), 0, one_third)
    central = jax.random.randint(subkeys[1], (QUERY_HEADS,), one_third, 2 * one_third)
    latest = jax.random.randint(subkeys[2], (QUERY_HEADS,), 0, one_third)
    earliest = earliest - jnp.min(earliest)
    latest = BLOCK_TOTAL - 1 - (latest - jnp.min(latest))
    return jnp.stack([earliest, central, latest], 1).astype(jnp.int32)


def draw_slash_offsets(key, part):
    half_span = GB // 2
    subkeys = jax.random.split(key, 2)
    closer_side = jax.random.randint(subkeys[0], (QUERY_HEADS,), 0, half_span)
    farther = jax.random.randint(subkeys[1], (QUERY_HEADS,), 0, GB - half_span)
    closer_side = 1 + closer_side - jnp.min(closer_side)
    farther = GB - (farther - jnp.min(farther))
    return jnp.stack([jnp.zeros((QUERY_HEADS,), jnp.int32), closer_side, farther], 1).astype(jnp.int32)


def block_levels(stream_key, shape, cuts, smallest, high):
    level = 1.0
    for axis_at, parts in cuts:
        draws = jax.random.uniform(jax.random.fold_in(jax.random.fold_in(stream_key, 6), axis_at), (parts,), jnp.float32, smallest / len(cuts), high / len(cuts))
        level = level * jnp.repeat(jnp.exp(draws), shape[axis_at] // parts).reshape((-1,) + (1,) * (len(shape) - 1 - axis_at))
    return level


def noise(stream_key, shape, scale, reach, cuts=(), held_as=jnp.bfloat16):
    level = block_levels(stream_key, shape, cuts, -0.22, 0.18) if cuts else 1.0
    values = jax.random.normal(stream_key, shape, jnp.float32) * scale * level
    return jnp.minimum(jnp.maximum(values, -reach), reach).astype(held_as)


def setup_inputs(seed: int = 0) -> dict:
    key_of = jax.random.split(jax.random.key(seed), 6)
    query_rows = draw_query_rows(jax.random.fold_in(key_of[5], 71), 0)
    key_matrix = draw_key_matrix(jax.random.fold_in(key_of[5], 71), 0)
    value_matrix = noise(key_of[2], (SEQUENCE_TOKENS, KEY_VALUE_HEADS * HEAD_DIMENSION), 1.0, 6.0, ((0, 32),))
    vertical = draw_vertical(jax.random.fold_in(key_of[5], 71), 0)
    slash_offsets = draw_slash_offsets(jax.random.fold_in(key_of[5], 71), 0)
    return dict(query_rows=query_rows, key_matrix=key_matrix, value_matrix=value_matrix, vertical=vertical, slash_offsets=slash_offsets)


def head_attention(query_block, slash_keys, slash_values, vert_keys, vert_values, offsets, vert_blocks, first_block):
    block_count, block_size, head_size = query_block.shape
    vert_tiled = jnp.broadcast_to(vert_keys[None], (block_count,) + vert_keys.shape)
    vert_vtiled = jnp.broadcast_to(vert_values[None], (block_count,) + vert_values.shape)
    all_keys = jnp.concatenate([slash_keys, vert_tiled], 1).reshape(block_count, -1, head_size)
    all_values = jnp.concatenate([slash_values, vert_vtiled], 1).reshape(block_count, -1, head_size)
    scores = jnp.einsum("qid,qkd->qik", query_block.astype(jnp.float32), all_keys.astype(jnp.float32)) * (head_size ** -0.5)
    query_index = first_block + jnp.arange(block_count, dtype=jnp.int32)
    slash_block = query_index[:, None] - offsets[None, :]
    slash_good = slash_block >= 0
    vert_good = (vert_blocks[None, :] <= query_index[:, None]) & jnp.all(
        query_index[:, None, None] - vert_blocks[None, :, None] != offsets[None, None, :], axis=2)
    block_ids = jnp.concatenate([slash_block, jnp.broadcast_to(vert_blocks[None, :], (block_count, vert_blocks.shape[0]))], 1)
    block_good = jnp.concatenate([slash_good, vert_good], 1)
    position = jnp.arange(block_size, dtype=jnp.int32)
    key_pos = (block_ids[:, :, None] * block_size + position[None, None, :]).reshape(block_count, -1)
    query_pos = query_index[:, None] * block_size + position[None, :]
    allowed = jnp.repeat(block_good, block_size, axis=1)[:, None, :] & (key_pos[:, None, :] <= query_pos[:, :, None])
    masked = jnp.where(allowed, scores, -1e30)
    row_top = jnp.max(masked, axis=2, keepdims=True)
    weight = jnp.where(allowed, jnp.exp(masked - row_top), 0.0)
    row_total = jnp.sum(weight, axis=2, keepdims=True)
    rounded = lax.optimization_barrier(weight.astype(jnp.bfloat16))
    result = jnp.einsum("qik,qkd->qid", rounded.astype(jnp.float32), all_values.astype(jnp.float32)) / row_total
    return result.astype(jnp.bfloat16)


def reference(query_rows, key_matrix, value_matrix, vertical, slash_offsets):
    group_sharing_factor = QUERY_HEADS // KEY_VALUE_HEADS
    blocked_keys = key_matrix.reshape(BLOCK_TOTAL, MASK_BLOCK_SIZE, KEY_VALUE_HEADS, HEAD_DIMENSION)
    blocked_values = value_matrix.reshape(BLOCK_TOTAL, MASK_BLOCK_SIZE, KEY_VALUE_HEADS, HEAD_DIMENSION)
    blocks = jnp.arange(BLOCK_TOTAL, dtype=jnp.int32)

    def one_head(head_id):
        query_block = lax.dynamic_slice_in_dim(query_rows, head_id * HEAD_DIMENSION, HEAD_DIMENSION, 1).reshape(BLOCK_TOTAL, MASK_BLOCK_SIZE, HEAD_DIMENSION)
        kv_index = head_id // group_sharing_factor
        head_keys = lax.dynamic_index_in_dim(blocked_keys, kv_index, 2, keepdims=False)
        head_values = lax.dynamic_index_in_dim(blocked_values, kv_index, 2, keepdims=False)
        offsets = slash_offsets[head_id]
        vert_blocks = vertical[head_id]
        source = jnp.maximum(blocks[:, None] - offsets[None, :], 0).astype(jnp.int32)
        return head_attention(query_block, head_keys[source], head_values[source], head_keys[vert_blocks],
                              head_values[vert_blocks], offsets, vert_blocks, jnp.zeros((), jnp.int32))

    outputs = lax.map(one_head, jnp.arange(QUERY_HEADS, dtype=jnp.int32))
    return outputs.transpose(1, 2, 0, 3).reshape(SEQUENCE_TOKENS, QUERY_HEADS * HEAD_DIMENSION)
```

```python
import jax
import jax.numpy as jnp
from jax import lax
from jax.experimental import pallas as pl
from jax.experimental.pallas import tpu as pltpu
from jax.sharding import PartitionSpec as P

HEAD_DIMENSION = 128
MASK_BLOCK_SIZE = 64
SLASH_COUNT = 3
VERT_COUNT = 3


def passed_along(shard, axis, by):
    length = lax.axis_size(axis)
    pairs = [(i, i + by) for i in range(length) if 0 <= i + by < length]
    return lax.ppermute(shard, axis, pairs)


def attention_kernel(local_heads, group_blocks, sharing):
    block = MASK_BLOCK_SIZE
    key_count = (SLASH_COUNT + VERT_COUNT) * block
    scale = HEAD_DIMENSION ** (-0.5)

    def kernel(meta_ref, q_ref, k_ref, v_ref, vk_ref, vv_ref, o_ref):
        h = pl.program_id(0)
        first = meta_ref[2 * local_heads * SLASH_COUNT]
        offs = [meta_ref[h * SLASH_COUNT + j] for j in range(SLASH_COUNT)]
        verts = [meta_ref[local_heads * SLASH_COUNT + h * VERT_COUNT + j] for j in range(VERT_COUNT)]
        vert_keys = vk_ref[0]
        vert_values = vv_ref[0]
        col = lax.broadcasted_iota(jnp.int32, (block, key_count), 1)
        row = lax.broadcasted_iota(jnp.int32, (block, key_count), 0)
        col_block = col // block
        col_pos = col % block
        for b in range(group_blocks):
            qb = first + b
            q = q_ref[pl.ds(b * block, block), :]
            starts = [pl.multiple_of((group_blocks + b - offs[j]) * block, block) for j in range(SLASH_COUNT)]
            keys = jnp.concatenate([k_ref[pl.ds(s, block), :] for s in starts] + [vert_keys], 0)
            values = jnp.concatenate([v_ref[pl.ds(s, block), :] for s in starts] + [vert_values], 0)
            ids = [qb - offs[j] for j in range(SLASH_COUNT)] + verts
            goods = [qb - offs[j] >= 0 for j in range(SLASH_COUNT)]
            for v in verts:
                ok = v <= qb
                for o in offs:
                    ok = jnp.logical_and(ok, qb - v != o)
                goods.append(ok)
            block_id = jnp.full((block, key_count), ids[-1], jnp.int32)
            goods = [g.astype(jnp.int32) for g in goods]
            block_good = jnp.full((block, key_count), goods[-1], jnp.int32)
            for i in range(len(ids) - 2, -1, -1):
                here = col_block == i
                block_id = jnp.where(here, ids[i], block_id)
                block_good = jnp.where(here, goods[i], block_good)
            allowed = jnp.logical_and(block_good > 0, block_id * block + col_pos <= qb * block + row)
            scores = lax.dot_general(
                q, keys, (((1,), (1,)), ((), ())), preferred_element_type=jnp.float32
            ) * scale
            masked = jnp.where(allowed, scores, -1e30)
            top = jnp.max(masked, axis=1, keepdims=True)
            weight = jnp.where(allowed, jnp.exp(masked - top), 0.0)
            total = jnp.sum(weight, axis=1, keepdims=True)
            rounded = weight.astype(jnp.bfloat16)
            acc = jnp.dot(rounded, values, preferred_element_type=jnp.float32)
            o_ref[pl.ds(b * block, block), :] = (acc / total).astype(o_ref.dtype)

    return kernel


def attend(meta, queries, key_window, value_window, vert_keys, vert_values, local_heads, sharing):
    group_rows = queries.shape[0]
    group_blocks = group_rows // MASK_BLOCK_SIZE
    head_size = HEAD_DIMENSION
    window_rows = key_window.shape[0]
    vert_rows = vert_keys.shape[1]
    grid_spec = pltpu.PrefetchScalarGridSpec(
        num_scalar_prefetch=1,
        grid=(local_heads,),
        in_specs=[
            pl.BlockSpec((group_rows, head_size), lambda h, m: (0, h)),
            pl.BlockSpec((window_rows, head_size), lambda h, m: (0, h // sharing)),
            pl.BlockSpec((window_rows, head_size), lambda h, m: (0, h // sharing)),
            pl.BlockSpec((1, vert_rows, head_size), lambda h, m: (h, 0, 0)),
            pl.BlockSpec((1, vert_rows, head_size), lambda h, m: (h, 0, 0)),
        ],
        out_specs=pl.BlockSpec((group_rows, head_size), lambda h, m: (0, h)),
    )
    return pl.pallas_call(
        attention_kernel(local_heads, group_blocks, sharing),
        grid_spec=grid_spec,
        out_shape=jax.ShapeDtypeStruct(queries.shape, queries.dtype),
    )(meta, queries, key_window, value_window, vert_keys, vert_values)


def per_device(query_rows, key_matrix, value_matrix, vertical, slash_offsets):
    tok_rows = query_rows.shape[0]
    grp_count = lax.axis_size("grp")
    head_size = HEAD_DIMENSION
    block_size = MASK_BLOCK_SIZE
    local_heads = query_rows.shape[1] // (grp_count * head_size)
    local_kv = key_matrix.shape[1] // (grp_count * head_size)
    group_sharing_factor = local_heads // local_kv
    query_split = query_rows.reshape(tok_rows, grp_count, local_heads * head_size)
    key_split = key_matrix.reshape(tok_rows, grp_count, local_kv * head_size)
    value_split = value_matrix.reshape(tok_rows, grp_count, local_kv * head_size)
    query_group, key_group, value_group = (
        lax.all_to_all(query_split, "grp", split_axis=1, concat_axis=0, tiled=True),
        lax.all_to_all(key_split, "grp", split_axis=1, concat_axis=0, tiled=True),
        lax.all_to_all(value_split, "grp", split_axis=1, concat_axis=0, tiled=True),
    )
    group_rows = tok_rows * grp_count
    group_blocks = group_rows // block_size
    key_local = key_group.reshape(group_rows, local_kv * head_size)
    value_local = value_group.reshape(group_rows, local_kv * head_size)
    key_before, value_before = passed_along((key_local, value_local), "seq", 1)
    key_window = jnp.concatenate([key_before, key_local], 0)
    value_window = jnp.concatenate([value_before, value_local], 0)
    seq_index = lax.axis_index("seq")
    grp_index = lax.axis_index("grp")
    head_offsets = lax.dynamic_slice_in_dim(slash_offsets, grp_index * local_heads, local_heads, 0)
    head_verts = lax.dynamic_slice_in_dim(vertical, grp_index * local_heads, local_heads, 0)
    kv_index = jnp.arange(local_heads, dtype=jnp.int32) // group_sharing_factor
    owner_seq = head_verts // group_blocks
    local_block = head_verts % group_blocks
    key_blocks = key_local.reshape(group_blocks, block_size, local_kv, head_size)
    value_blocks = value_local.reshape(group_blocks, block_size, local_kv, head_size)
    picked_keys = key_blocks[local_block, :, kv_index[:, None], :]
    picked_values = value_blocks[local_block, :, kv_index[:, None], :]
    owned = (owner_seq == seq_index)[:, :, None, None]
    nothing = jnp.zeros((), picked_keys.dtype)
    summed_keys, summed_values = lax.psum(
        (jnp.where(owned, picked_keys, nothing), jnp.where(owned, picked_values, nothing)),
        "seq",
    )
    vert_keys = summed_keys.reshape(local_heads, -1, head_size)
    vert_values = summed_values.reshape(local_heads, -1, head_size)
    first_block = (seq_index * group_blocks).astype(jnp.int32)
    meta = jnp.concatenate(
        [
            head_offsets.reshape(-1).astype(jnp.int32),
            head_verts.reshape(-1).astype(jnp.int32),
            first_block[None],
        ]
    )
    queries = query_group.reshape(group_rows, local_heads * head_size)
    results = attend(
        meta, queries, key_window, value_window, vert_keys, vert_values, local_heads,
        group_sharing_factor,
    )
    merged = results.reshape(group_rows, 1, local_heads * head_size)
    returned = lax.all_to_all(merged, "grp", split_axis=0, concat_axis=1, tiled=True)
    return returned.reshape(tok_rows, grp_count * local_heads * head_size)


def solution(mesh):
    return jax.shard_map(
        per_device,
        mesh=mesh,
        in_specs=(
            P(("seq", "grp"), None),
            P(("seq", "grp"), None),
            P(("seq", "grp"), None),
            P(),
            P(),
        ),
        out_specs=P(("seq", "grp"), None),
        check_vma=False,
    )
```

```python
import jax
import jax.numpy as jnp
from jax import lax
from jax.experimental import pallas as pl
from jax.experimental.pallas import tpu as pltpu
from jax.sharding import PartitionSpec as P

HEAD_DIMENSION = 128
MASK_BLOCK_SIZE = 64
SLASH_COUNT = 3
VERT_COUNT = 3


def passed_along(shard, axis, by):
    length = lax.axis_size(axis)
    pairs = [(i, i + by) for i in range(length) if 0 <= i + by < length]
    return lax.ppermute(shard, axis, pairs)


def attention_kernel(local_heads, group_blocks, sharing):
    block = MASK_BLOCK_SIZE
    key_count = (SLASH_COUNT + VERT_COUNT) * block
    scale = HEAD_DIMENSION ** (-0.5)

    def kernel(meta_ref, q_ref, k_ref, v_ref, vk_ref, vv_ref, o_ref):
        h = pl.program_id(0)
        first = meta_ref[2 * local_heads * SLASH_COUNT]
        offs = [meta_ref[h * SLASH_COUNT + j] for j in range(SLASH_COUNT)]
        verts = [meta_ref[local_heads * SLASH_COUNT + h * VERT_COUNT + j] for j in range(VERT_COUNT)]
        vert_keys = vk_ref[0]
        vert_values = vv_ref[0]
        col = lax.broadcasted_iota(jnp.int32, (block, key_count), 1)
        row = lax.broadcasted_iota(jnp.int32, (block, key_count), 0)
        reach = col % block - row
        lane = lax.broadcasted_iota(jnp.int32, (1, key_count), 1) // block
        never = jnp.int32(-4 * block)
        for b in range(group_blocks):
            qb = first + b
            q = q_ref[pl.ds(b * block, block), :]
            starts = [pl.multiple_of((group_blocks + b - offs[j]) * block, block) for j in range(SLASH_COUNT)]
            keys = jnp.concatenate([k_ref[pl.ds(s, block), :] for s in starts] + [vert_keys], 0)
            values = jnp.concatenate([v_ref[pl.ds(s, block), :] for s in starts] + [vert_values], 0)
            limits = [jnp.where(qb - offs[j] >= 0, offs[j] * block, never) for j in range(SLASH_COUNT)]
            for v in verts:
                ok = v <= qb
                for o in offs:
                    ok = jnp.logical_and(ok, qb - v != o)
                limits.append(jnp.where(ok, (qb - v) * block, never))
            limit = jnp.full((1, key_count), limits[-1], jnp.int32)
            for i in range(len(limits) - 2, -1, -1):
                limit = jnp.where(lane == i, limits[i], limit)
            allowed = reach <= limit
            scores = lax.dot_general(
                q, keys, (((1,), (1,)), ((), ())), preferred_element_type=jnp.float32
            ) * scale
            masked = jnp.where(allowed, scores, -1e30)
            top = jnp.max(masked, axis=1, keepdims=True)
            weight = jnp.exp(masked - top)
            total = jnp.sum(weight, axis=1, keepdims=True)
            rounded = weight.astype(jnp.bfloat16)
            acc = jnp.dot(rounded, values, preferred_element_type=jnp.float32)
            o_ref[pl.ds(b * block, block), :] = (acc / total).astype(o_ref.dtype)

    return kernel


def attend(meta, queries, key_window, value_window, vert_keys, vert_values, local_heads, sharing):
    group_rows = queries.shape[0]
    group_blocks = group_rows // MASK_BLOCK_SIZE
    head_size = HEAD_DIMENSION
    window_rows = key_window.shape[0]
    vert_rows = vert_keys.shape[1]
    grid_spec = pltpu.PrefetchScalarGridSpec(
        num_scalar_prefetch=1,
        grid=(local_heads,),
        in_specs=[
            pl.BlockSpec((group_rows, head_size), lambda h, m: (0, h)),
            pl.BlockSpec((window_rows, head_size), lambda h, m: (0, h // sharing)),
            pl.BlockSpec((window_rows, head_size), lambda h, m: (0, h // sharing)),
            pl.BlockSpec((1, vert_rows, head_size), lambda h, m: (h, 0, 0)),
            pl.BlockSpec((1, vert_rows, head_size), lambda h, m: (h, 0, 0)),
        ],
        out_specs=pl.BlockSpec((group_rows, head_size), lambda h, m: (0, h)),
    )
    return pl.pallas_call(
        attention_kernel(local_heads, group_blocks, sharing),
        grid_spec=grid_spec,
        out_shape=jax.ShapeDtypeStruct(queries.shape, queries.dtype),
    )(meta, queries, key_window, value_window, vert_keys, vert_values)


def per_device(query_rows, key_matrix, value_matrix, vertical, slash_offsets):
    tok_rows = query_rows.shape[0]
    grp_count = lax.axis_size("grp")
    head_size = HEAD_DIMENSION
    block_size = MASK_BLOCK_SIZE
    local_heads = query_rows.shape[1] // (grp_count * head_size)
    local_kv = key_matrix.shape[1] // (grp_count * head_size)
    group_sharing_factor = local_heads // local_kv
    query_split = query_rows.reshape(tok_rows, grp_count, local_heads * head_size)
    key_split = key_matrix.reshape(tok_rows, grp_count, local_kv * head_size)
    value_split = value_matrix.reshape(tok_rows, grp_count, local_kv * head_size)
    query_group, key_group, value_group = (
        lax.all_to_all(query_split, "grp", split_axis=1, concat_axis=0, tiled=True),
        lax.all_to_all(key_split, "grp", split_axis=1, concat_axis=0, tiled=True),
        lax.all_to_all(value_split, "grp", split_axis=1, concat_axis=0, tiled=True),
    )
    group_rows = tok_rows * grp_count
    group_blocks = group_rows // block_size
    key_local = key_group.reshape(group_rows, local_kv * head_size)
    value_local = value_group.reshape(group_rows, local_kv * head_size)
    key_before, value_before = passed_along((key_local, value_local), "seq", 1)
    key_window = jnp.concatenate([key_before, key_local], 0)
    value_window = jnp.concatenate([value_before, value_local], 0)
    seq_index = lax.axis_index("seq")
    grp_index = lax.axis_index("grp")
    head_offsets = lax.dynamic_slice_in_dim(slash_offsets, grp_index * local_heads, local_heads, 0)
    head_verts = lax.dynamic_slice_in_dim(vertical, grp_index * local_heads, local_heads, 0)
    kv_index = jnp.arange(local_heads, dtype=jnp.int32) // group_sharing_factor
    owner_seq = head_verts // group_blocks
    local_block = head_verts % group_blocks
    key_blocks = key_local.reshape(group_blocks, block_size, local_kv, head_size)
    value_blocks = value_local.reshape(group_blocks, block_size, local_kv, head_size)
    picked_keys = key_blocks[local_block, :, kv_index[:, None], :]
    picked_values = value_blocks[local_block, :, kv_index[:, None], :]
    owned = (owner_seq == seq_index)[:, :, None, None]
    nothing = jnp.zeros((), picked_keys.dtype)
    summed_keys, summed_values = lax.psum(
        (jnp.where(owned, picked_keys, nothing), jnp.where(owned, picked_values, nothing)),
        "seq",
    )
    vert_keys = summed_keys.reshape(local_heads, -1, head_size)
    vert_values = summed_values.reshape(local_heads, -1, head_size)
    first_block = (seq_index * group_blocks).astype(jnp.int32)
    meta = jnp.concatenate(
        [
            head_offsets.reshape(-1).astype(jnp.int32),
            head_verts.reshape(-1).astype(jnp.int32),
            first_block[None],
        ]
    )
    queries = query_group.reshape(group_rows, local_heads * head_size)
    results = attend(
        meta, queries, key_window, value_window, vert_keys, vert_values, local_heads,
        group_sharing_factor,
    )
    merged = results.reshape(grp_count, tok_rows, local_heads * head_size)
    returned = lax.all_to_all(merged, "grp", split_axis=0, concat_axis=0, tiled=True)
    return returned.transpose(1, 0, 2).reshape(tok_rows, grp_count * local_heads * head_size)


def solution(mesh):
    return jax.shard_map(
        per_device,
        mesh=mesh,
        in_specs=(
            P(("seq", "grp"), None),
            P(("seq", "grp"), None),
            P(("seq", "grp"), None),
            P(),
            P(),
        ),
        out_specs=P(("seq", "grp"), None),
        check_vma=False,
    )
```

```python
import jax
import jax.numpy as jnp
from jax import lax
from jax.experimental import pallas as pl
from jax.experimental.pallas import tpu as pltpu
from jax.sharding import PartitionSpec as P

HEAD_DIMENSION = 128
MASK_BLOCK_SIZE = 64
SLASH_COUNT = 3
VERT_COUNT = 3
CHUNKS = 2


def passed_along(shard, axis, by):
    length = lax.axis_size(axis)
    pairs = [(i, i + by) for i in range(length) if 0 <= i + by < length]
    return lax.ppermute(shard, axis, pairs)


def attention_kernel(local_heads, group_blocks, base):
    block = MASK_BLOCK_SIZE
    key_count = (SLASH_COUNT + VERT_COUNT) * block
    scale = HEAD_DIMENSION ** (-0.5)

    def kernel(meta_ref, q_ref, k_ref, v_ref, vk_ref, vv_ref, o_ref):
        h = pl.program_id(0) + base
        first = meta_ref[2 * local_heads * SLASH_COUNT]
        offs = [meta_ref[h * SLASH_COUNT + j] for j in range(SLASH_COUNT)]
        verts = [meta_ref[local_heads * SLASH_COUNT + h * VERT_COUNT + j] for j in range(VERT_COUNT)]
        vert_keys = vk_ref[0]
        vert_values = vv_ref[0]
        col = lax.broadcasted_iota(jnp.int32, (block, key_count), 1)
        row = lax.broadcasted_iota(jnp.int32, (block, key_count), 0)
        reach = col % block - row
        lane = lax.broadcasted_iota(jnp.int32, (1, key_count), 1) // block
        never = jnp.int32(-4 * block)
        for b in range(group_blocks):
            qb = first + b
            q = q_ref[pl.ds(b * block, block), :]
            starts = [pl.multiple_of((group_blocks + b - offs[j]) * block, block) for j in range(SLASH_COUNT)]
            keys = jnp.concatenate([k_ref[pl.ds(s, block), :] for s in starts] + [vert_keys], 0)
            values = jnp.concatenate([v_ref[pl.ds(s, block), :] for s in starts] + [vert_values], 0)
            limits = [jnp.where(qb - offs[j] >= 0, offs[j] * block, never) for j in range(SLASH_COUNT)]
            for v in verts:
                ok = v <= qb
                for o in offs:
                    ok = jnp.logical_and(ok, qb - v != o)
                limits.append(jnp.where(ok, (qb - v) * block, never))
            limit = jnp.full((1, key_count), limits[-1], jnp.int32)
            for i in range(len(limits) - 2, -1, -1):
                limit = jnp.where(lane == i, limits[i], limit)
            allowed = reach <= limit
            scores = lax.dot_general(
                q, keys, (((1,), (1,)), ((), ())), preferred_element_type=jnp.float32
            ) * scale
            masked = jnp.where(allowed, scores, -1e30)
            top = jnp.max(masked, axis=1, keepdims=True)
            weight = jnp.exp(masked - top)
            total = jnp.sum(weight, axis=1, keepdims=True)
            rounded = weight.astype(jnp.bfloat16)
            acc = jnp.dot(rounded, values, preferred_element_type=jnp.float32)
            o_ref[pl.ds(b * block, block), :] = (acc / total).astype(o_ref.dtype)

    return kernel


def attend(meta, queries, key_window, value_window, vert_keys, vert_values, local_heads, sharing, base):
    group_rows = queries.shape[0]
    group_blocks = group_rows // MASK_BLOCK_SIZE
    head_size = HEAD_DIMENSION
    window_rows = key_window.shape[0]
    chunk_heads, vert_rows = vert_keys.shape[:2]
    grid_spec = pltpu.PrefetchScalarGridSpec(
        num_scalar_prefetch=1,
        grid=(chunk_heads,),
        in_specs=[
            pl.BlockSpec((group_rows, head_size), lambda h, m: (0, h + base)),
            pl.BlockSpec((window_rows, head_size), lambda h, m: (0, (h + base) // sharing)),
            pl.BlockSpec((window_rows, head_size), lambda h, m: (0, (h + base) // sharing)),
            pl.BlockSpec((1, vert_rows, head_size), lambda h, m: (h, 0, 0)),
            pl.BlockSpec((1, vert_rows, head_size), lambda h, m: (h, 0, 0)),
        ],
        out_specs=pl.BlockSpec((group_rows, head_size), lambda h, m: (0, h)),
    )
    return pl.pallas_call(
        attention_kernel(local_heads, group_blocks, base),
        grid_spec=grid_spec,
        out_shape=jax.ShapeDtypeStruct((group_rows, chunk_heads * head_size), queries.dtype),
    )(meta, queries, key_window, value_window, vert_keys, vert_values)


def per_device(query_rows, key_matrix, value_matrix, vertical, slash_offsets):
    tok_rows = query_rows.shape[0]
    grp_count = lax.axis_size("grp")
    head_size = HEAD_DIMENSION
    block_size = MASK_BLOCK_SIZE
    local_heads = query_rows.shape[1] // (grp_count * head_size)
    local_kv = key_matrix.shape[1] // (grp_count * head_size)
    group_sharing_factor = local_heads // local_kv
    query_split = query_rows.reshape(tok_rows, grp_count, local_heads * head_size)
    key_split = key_matrix.reshape(tok_rows, grp_count, local_kv * head_size)
    value_split = value_matrix.reshape(tok_rows, grp_count, local_kv * head_size)
    query_group, key_group, value_group = (
        lax.all_to_all(query_split, "grp", split_axis=1, concat_axis=0, tiled=True),
        lax.all_to_all(key_split, "grp", split_axis=1, concat_axis=0, tiled=True),
        lax.all_to_all(value_split, "grp", split_axis=1, concat_axis=0, tiled=True),
    )
    group_rows = tok_rows * grp_count
    group_blocks = group_rows // block_size
    key_local = key_group.reshape(group_rows, local_kv * head_size)
    value_local = value_group.reshape(group_rows, local_kv * head_size)
    key_before, value_before = passed_along((key_local, value_local), "seq", 1)
    key_window = jnp.concatenate([key_before, key_local], 0)
    value_window = jnp.concatenate([value_before, value_local], 0)
    seq_index = lax.axis_index("seq")
    grp_index = lax.axis_index("grp")
    head_offsets = lax.dynamic_slice_in_dim(slash_offsets, grp_index * local_heads, local_heads, 0)
    head_verts = lax.dynamic_slice_in_dim(vertical, grp_index * local_heads, local_heads, 0)
    kv_index = jnp.arange(local_heads, dtype=jnp.int32) // group_sharing_factor
    owner_seq = head_verts // group_blocks
    local_block = head_verts % group_blocks
    key_blocks = key_local.reshape(group_blocks, block_size, local_kv, head_size)
    value_blocks = value_local.reshape(group_blocks, block_size, local_kv, head_size)
    picked_keys = key_blocks[local_block, :, kv_index[:, None], :]
    picked_values = value_blocks[local_block, :, kv_index[:, None], :]
    owned = (owner_seq == seq_index)[:, :, None, None]
    nothing = jnp.zeros((), picked_keys.dtype)
    mine_keys = jnp.where(owned, picked_keys, nothing)
    mine_values = jnp.where(owned, picked_values, nothing)
    first_block = (seq_index * group_blocks).astype(jnp.int32)
    meta = jnp.concatenate(
        [
            head_offsets.reshape(-1).astype(jnp.int32),
            head_verts.reshape(-1).astype(jnp.int32),
            first_block[None],
        ]
    )
    queries = query_group.reshape(group_rows, local_heads * head_size)
    chunk_heads = local_heads // CHUNKS
    pieces = []
    summed = ()
    for c in range(CHUNKS):
        heads = slice(c * chunk_heads, (c + 1) * chunk_heads)
        chunk_keys, chunk_values, _ = lax.optimization_barrier(
            (mine_keys[heads], mine_values[heads], summed)
        )
        summed = lax.psum((chunk_keys, chunk_values), "seq")
        summed_keys, summed_values = summed
        results = attend(
            meta, queries, key_window, value_window,
            summed_keys.reshape(chunk_heads, -1, head_size),
            summed_values.reshape(chunk_heads, -1, head_size),
            local_heads, group_sharing_factor, c * chunk_heads,
        )
        merged = results.reshape(grp_count, tok_rows, chunk_heads * head_size)
        pieces.append(lax.all_to_all(merged, "grp", split_axis=0, concat_axis=0, tiled=True))
    returned = jnp.stack(pieces, 1)
    return returned.transpose(2, 0, 1, 3).reshape(tok_rows, grp_count * local_heads * head_size)


def solution(mesh):
    return jax.shard_map(
        per_device,
        mesh=mesh,
        in_specs=(
            P(("seq", "grp"), None),
            P(("seq", "grp"), None),
            P(("seq", "grp"), None),
            P(),
            P(),
        ),
        out_specs=P(("seq", "grp"), None),
        check_vma=False,
    )
```

```python
import jax
import jax.numpy as jnp
from jax import lax
from jax.experimental import pallas as pl
from jax.experimental.pallas import tpu as pltpu
from jax.sharding import PartitionSpec as P

HEAD_DIMENSION = 128
MASK_BLOCK_SIZE = 64
SLASH_COUNT = 3
VERT_COUNT = 3


def passed_along(shard, axis, by):
    length = lax.axis_size(axis)
    pairs = [(i, i + by) for i in range(length) if 0 <= i + by < length]
    return lax.ppermute(shard, axis, pairs)


def attention_kernel(local_heads, group_blocks, base):
    block = MASK_BLOCK_SIZE
    key_count = (SLASH_COUNT + VERT_COUNT) * block
    scale = HEAD_DIMENSION ** (-0.5)

    def kernel(meta_ref, q_ref, k_ref, v_ref, vk_ref, vv_ref, o_ref):
        h = pl.program_id(0) + base
        first = meta_ref[2 * local_heads * SLASH_COUNT]
        offs = [meta_ref[h * SLASH_COUNT + j] for j in range(SLASH_COUNT)]
        verts = [meta_ref[local_heads * SLASH_COUNT + h * VERT_COUNT + j] for j in range(VERT_COUNT)]
        vert_keys = vk_ref[0]
        vert_values = vv_ref[0]
        col = lax.broadcasted_iota(jnp.int32, (block, key_count), 1)
        row = lax.broadcasted_iota(jnp.int32, (block, key_count), 0)
        reach = col % block - row
        lane = lax.broadcasted_iota(jnp.int32, (1, key_count), 1) // block
        never = jnp.int32(-4 * block)
        for b in range(group_blocks):
            qb = first + b
            q = q_ref[pl.ds(b * block, block), :]
            starts = [pl.multiple_of((group_blocks + b - offs[j]) * block, block) for j in range(SLASH_COUNT)]
            keys = jnp.concatenate([k_ref[pl.ds(s, block), :] for s in starts] + [vert_keys], 0)
            values = jnp.concatenate([v_ref[pl.ds(s, block), :] for s in starts] + [vert_values], 0)
            limits = [jnp.where(qb - offs[j] >= 0, offs[j] * block, never) for j in range(SLASH_COUNT)]
            for v in verts:
                ok = v <= qb
                for o in offs:
                    ok = jnp.logical_and(ok, qb - v != o)
                limits.append(jnp.where(ok, (qb - v) * block, never))
            limit = jnp.full((1, key_count), limits[-1], jnp.int32)
            for i in range(len(limits) - 2, -1, -1):
                limit = jnp.where(lane == i, limits[i], limit)
            allowed = reach <= limit
            scores = lax.dot_general(
                q, keys, (((1,), (1,)), ((), ())), preferred_element_type=jnp.float32
            ) * scale
            masked = jnp.where(allowed, scores, -1e30)
            top = jnp.max(masked, axis=1, keepdims=True)
            weight = jnp.exp(masked - top)
            total = jnp.sum(weight, axis=1, keepdims=True)
            rounded = weight.astype(jnp.bfloat16)
            acc = jnp.dot(rounded, values, preferred_element_type=jnp.float32)
            o_ref[pl.ds(b * block, block), :] = (acc / total).astype(o_ref.dtype)

    return kernel


def attend(meta, queries, key_window, value_window, vert_keys, vert_values, local_heads, sharing, base):
    group_rows = queries.shape[0]
    group_blocks = group_rows // MASK_BLOCK_SIZE
    head_size = HEAD_DIMENSION
    window_rows = key_window.shape[0]
    chunk_heads, vert_rows = vert_keys.shape[:2]
    grid_spec = pltpu.PrefetchScalarGridSpec(
        num_scalar_prefetch=1,
        grid=(chunk_heads,),
        in_specs=[
            pl.BlockSpec((group_rows, head_size), lambda h, m: (0, h + base)),
            pl.BlockSpec((window_rows, head_size), lambda h, m: (0, (h + base) // sharing)),
            pl.BlockSpec((window_rows, head_size), lambda h, m: (0, (h + base) // sharing)),
            pl.BlockSpec((1, vert_rows, head_size), lambda h, m: (h, 0, 0)),
            pl.BlockSpec((1, vert_rows, head_size), lambda h, m: (h, 0, 0)),
        ],
        out_specs=pl.BlockSpec((group_rows, head_size), lambda h, m: (0, h)),
    )
    return pl.pallas_call(
        attention_kernel(local_heads, group_blocks, base),
        grid_spec=grid_spec,
        out_shape=jax.ShapeDtypeStruct((group_rows, chunk_heads * head_size), queries.dtype),
    )(meta, queries, key_window, value_window, vert_keys, vert_values)


def per_device(query_rows, key_matrix, value_matrix, vertical, slash_offsets):
    tok_rows = query_rows.shape[0]
    grp_count = lax.axis_size("grp")
    head_size = HEAD_DIMENSION
    block_size = MASK_BLOCK_SIZE
    local_heads = query_rows.shape[1] // (grp_count * head_size)
    local_kv = key_matrix.shape[1] // (grp_count * head_size)
    group_sharing_factor = local_heads // local_kv
    query_split = query_rows.reshape(tok_rows, grp_count, local_heads * head_size)
    key_split = key_matrix.reshape(tok_rows, grp_count, local_kv * head_size)
    value_split = value_matrix.reshape(tok_rows, grp_count, local_kv * head_size)
    query_group, key_group, value_group = (
        lax.all_to_all(query_split, "grp", split_axis=1, concat_axis=0, tiled=True),
        lax.all_to_all(key_split, "grp", split_axis=1, concat_axis=0, tiled=True),
        lax.all_to_all(value_split, "grp", split_axis=1, concat_axis=0, tiled=True),
    )
    group_rows = tok_rows * grp_count
    group_blocks = group_rows // block_size
    key_local = key_group.reshape(group_rows, local_kv * head_size)
    value_local = value_group.reshape(group_rows, local_kv * head_size)
    key_before, value_before = passed_along((key_local, value_local), "seq", 1)
    key_window = jnp.concatenate([key_before, key_local], 0)
    value_window = jnp.concatenate([value_before, value_local], 0)
    seq_index = lax.axis_index("seq")
    grp_index = lax.axis_index("grp")
    head_offsets = lax.dynamic_slice_in_dim(slash_offsets, grp_index * local_heads, local_heads, 0)
    head_verts = lax.dynamic_slice_in_dim(vertical, grp_index * local_heads, local_heads, 0)
    kv_index = jnp.arange(local_heads, dtype=jnp.int32) // group_sharing_factor
    owner_seq = head_verts // group_blocks
    local_block = head_verts % group_blocks
    key_blocks = key_local.reshape(group_blocks, block_size, local_kv, head_size)
    value_blocks = value_local.reshape(group_blocks, block_size, local_kv, head_size)
    picked_keys = key_blocks[local_block, :, kv_index[:, None], :]
    picked_values = value_blocks[local_block, :, kv_index[:, None], :]
    owned = (owner_seq == seq_index)[:, :, None, None]
    nothing = jnp.zeros((), picked_keys.dtype)
    seq_count = lax.axis_size("seq")
    mine = jnp.stack(
        [jnp.where(owned, picked_keys, nothing), jnp.where(owned, picked_values, nothing)]
    ).reshape(2, seq_count, -1, head_size).transpose(1, 0, 2, 3)
    part = lax.all_to_all(mine, "seq", split_axis=0, concat_axis=0, tiled=True).sum(
        0, dtype=picked_keys.dtype
    )
    spread = jnp.broadcast_to(part[None], (seq_count,) + part.shape)
    gathered = lax.all_to_all(spread, "seq", split_axis=0, concat_axis=0, tiled=True)
    vert = gathered.transpose(1, 0, 2, 3).reshape(2, local_heads, -1, head_size)
    first_block = (seq_index * group_blocks).astype(jnp.int32)
    meta = jnp.concatenate(
        [
            head_offsets.reshape(-1).astype(jnp.int32),
            head_verts.reshape(-1).astype(jnp.int32),
            first_block[None],
        ]
    )
    queries = query_group.reshape(group_rows, local_heads * head_size)
    results = attend(
        meta, queries, key_window, value_window, vert[0], vert[1],
        local_heads, group_sharing_factor, 0,
    )
    merged = results.reshape(grp_count, tok_rows, local_heads * head_size)
    returned = lax.all_to_all(merged, "grp", split_axis=0, concat_axis=0, tiled=True)
    return returned.transpose(1, 0, 2).reshape(tok_rows, grp_count * local_heads * head_size)


def solution(mesh):
    return jax.shard_map(
        per_device,
        mesh=mesh,
        in_specs=(
            P(("seq", "grp"), None),
            P(("seq", "grp"), None),
            P(("seq", "grp"), None),
            P(),
            P(),
        ),
        out_specs=P(("seq", "grp"), None),
        check_vma=False,
    )
```

```python
import jax
import jax.numpy as jnp
from jax import lax
from jax.experimental import pallas as pl
from jax.experimental.pallas import tpu as pltpu
from jax.sharding import PartitionSpec as P

HEAD_DIMENSION = 128
MASK_BLOCK_SIZE = 64
SLASH_COUNT = 3
VERT_COUNT = 3


def passed_along(shard, axis, by):
    length = lax.axis_size(axis)
    pairs = [(i, i + by) for i in range(length) if 0 <= i + by < length]
    return lax.ppermute(shard, axis, pairs)


def attention_kernel(local_heads, group_blocks, base):
    block = MASK_BLOCK_SIZE
    key_count = (SLASH_COUNT + VERT_COUNT) * block
    scale = HEAD_DIMENSION ** (-0.5)

    def kernel(meta_ref, q_ref, k_ref, v_ref, vk_ref, vv_ref, o_ref):
        h = pl.program_id(0) + base
        first = meta_ref[2 * local_heads * SLASH_COUNT]
        offs = [meta_ref[h * SLASH_COUNT + j] for j in range(SLASH_COUNT)]
        verts = [meta_ref[local_heads * SLASH_COUNT + h * VERT_COUNT + j] for j in range(VERT_COUNT)]
        vert_keys = vk_ref[0]
        vert_values = vv_ref[0]
        col = lax.broadcasted_iota(jnp.int32, (block, key_count), 1)
        row = lax.broadcasted_iota(jnp.int32, (block, key_count), 0)
        reach = col % block - row
        lane = lax.broadcasted_iota(jnp.int32, (1, key_count), 1) // block
        never = jnp.int32(-4 * block)
        for b in range(group_blocks):
            qb = first + b
            q = q_ref[pl.ds(b * block, block), :]
            starts = [pl.multiple_of((group_blocks + b - offs[j]) * block, block) for j in range(SLASH_COUNT)]
            keys = jnp.concatenate([k_ref[pl.ds(s, block), :] for s in starts] + [vert_keys], 0)
            values = jnp.concatenate([v_ref[pl.ds(s, block), :] for s in starts] + [vert_values], 0)
            limits = [jnp.where(qb - offs[j] >= 0, offs[j] * block, never) for j in range(SLASH_COUNT)]
            for v in verts:
                ok = v <= qb
                for o in offs:
                    ok = jnp.logical_and(ok, qb - v != o)
                limits.append(jnp.where(ok, (qb - v) * block, never))
            limit = jnp.full((1, key_count), limits[-1], jnp.int32)
            for i in range(len(limits) - 2, -1, -1):
                limit = jnp.where(lane == i, limits[i], limit)
            allowed = reach <= limit
            scores = lax.dot_general(
                q, keys, (((1,), (1,)), ((), ())), preferred_element_type=jnp.float32
            ) * scale
            masked = jnp.where(allowed, scores, -1e30)
            top = jnp.max(masked, axis=1, keepdims=True)
            weight = jnp.exp(masked - top)
            total = jnp.sum(weight, axis=1, keepdims=True)
            rounded = weight.astype(jnp.bfloat16)
            acc = jnp.dot(rounded, values, preferred_element_type=jnp.float32)
            o_ref[pl.ds(b * block, block), :] = (acc / total).astype(o_ref.dtype)

    return kernel


def attend(meta, queries, key_window, value_window, vert_keys, vert_values, local_heads, sharing, base):
    group_rows = queries.shape[0]
    group_blocks = group_rows // MASK_BLOCK_SIZE
    head_size = HEAD_DIMENSION
    window_rows = key_window.shape[0]
    chunk_heads, vert_rows = vert_keys.shape[:2]
    grid_spec = pltpu.PrefetchScalarGridSpec(
        num_scalar_prefetch=1,
        grid=(chunk_heads,),
        in_specs=[
            pl.BlockSpec((group_rows, head_size), lambda h, m: (0, h + base)),
            pl.BlockSpec((window_rows, head_size), lambda h, m: (0, (h + base) // sharing)),
            pl.BlockSpec((window_rows, head_size), lambda h, m: (0, (h + base) // sharing)),
            pl.BlockSpec((1, vert_rows, head_size), lambda h, m: (h, 0, 0)),
            pl.BlockSpec((1, vert_rows, head_size), lambda h, m: (h, 0, 0)),
        ],
        out_specs=pl.BlockSpec((group_rows, head_size), lambda h, m: (0, h)),
    )
    return pl.pallas_call(
        attention_kernel(local_heads, group_blocks, base),
        grid_spec=grid_spec,
        out_shape=jax.ShapeDtypeStruct((group_rows, chunk_heads * head_size), queries.dtype),
    )(meta, queries, key_window, value_window, vert_keys, vert_values)


def per_device(query_rows, key_matrix, value_matrix, vertical, slash_offsets):
    tok_rows = query_rows.shape[0]
    grp_count = lax.axis_size("grp")
    head_size = HEAD_DIMENSION
    block_size = MASK_BLOCK_SIZE
    local_heads = query_rows.shape[1] // (grp_count * head_size)
    local_kv = key_matrix.shape[1] // (grp_count * head_size)
    group_sharing_factor = local_heads // local_kv
    query_split = query_rows.reshape(tok_rows, grp_count, local_heads * head_size)
    key_split = key_matrix.reshape(tok_rows, grp_count, local_kv * head_size)
    value_split = value_matrix.reshape(tok_rows, grp_count, local_kv * head_size)
    query_group, key_group, value_group = (
        lax.all_to_all(query_split, "grp", split_axis=1, concat_axis=0, tiled=True),
        lax.all_to_all(key_split, "grp", split_axis=1, concat_axis=0, tiled=True),
        lax.all_to_all(value_split, "grp", split_axis=1, concat_axis=0, tiled=True),
    )
    group_rows = tok_rows * grp_count
    group_blocks = group_rows // block_size
    key_local = key_group.reshape(group_rows, local_kv * head_size)
    value_local = value_group.reshape(group_rows, local_kv * head_size)
    seq_index = lax.axis_index("seq")
    grp_index = lax.axis_index("grp")
    head_offsets = lax.dynamic_slice_in_dim(slash_offsets, grp_index * local_heads, local_heads, 0)
    head_verts = lax.dynamic_slice_in_dim(vertical, grp_index * local_heads, local_heads, 0)
    kv_index = jnp.arange(local_heads, dtype=jnp.int32) // group_sharing_factor
    owner_seq = head_verts // group_blocks
    local_block = head_verts % group_blocks
    key_blocks = key_local.reshape(group_blocks, block_size, local_kv, head_size)
    value_blocks = value_local.reshape(group_blocks, block_size, local_kv, head_size)
    picked_keys = key_blocks[local_block, :, kv_index[:, None], :]
    picked_values = value_blocks[local_block, :, kv_index[:, None], :]
    owned = (owner_seq == seq_index)[:, :, None, None]
    nothing = jnp.zeros((), picked_keys.dtype)
    seq_count = lax.axis_size("seq")
    mine = jnp.stack(
        [jnp.where(owned, picked_keys, nothing), jnp.where(owned, picked_values, nothing)]
    ).reshape(2, seq_count, -1, head_size).transpose(1, 0, 2, 3)
    query_group, mine = lax.optimization_barrier((query_group, mine))
    part = lax.all_to_all(mine, "seq", split_axis=0, concat_axis=0, tiled=True).sum(
        0, dtype=picked_keys.dtype
    )
    key_sent, value_sent, part = lax.optimization_barrier((key_local, value_local, part))
    key_before, value_before = passed_along((key_sent, value_sent), "seq", 1)
    key_window = jnp.concatenate([key_before, key_local], 0)
    value_window = jnp.concatenate([value_before, value_local], 0)
    spread = jnp.broadcast_to(part[None], (seq_count,) + part.shape)
    gathered = lax.all_to_all(spread, "seq", split_axis=0, concat_axis=0, tiled=True)
    vert = gathered.transpose(1, 0, 2, 3).reshape(2, local_heads, -1, head_size)
    first_block = (seq_index * group_blocks).astype(jnp.int32)
    meta = jnp.concatenate(
        [
            head_offsets.reshape(-1).astype(jnp.int32),
            head_verts.reshape(-1).astype(jnp.int32),
            first_block[None],
        ]
    )
    queries = query_group.reshape(group_rows, local_heads * head_size)
    results = attend(
        meta, queries, key_window, value_window, vert[0], vert[1],
        local_heads, group_sharing_factor, 0,
    )
    merged = results.reshape(grp_count, tok_rows, local_heads * head_size)
    returned = lax.all_to_all(merged, "grp", split_axis=0, concat_axis=0, tiled=True)
    return returned.transpose(1, 0, 2).reshape(tok_rows, grp_count * local_heads * head_size)


def solution(mesh):
    return jax.shard_map(
        per_device,
        mesh=mesh,
        in_specs=(
            P(("seq", "grp"), None),
            P(("seq", "grp"), None),
            P(("seq", "grp"), None),
            P(),
            P(),
        ),
        out_specs=P(("seq", "grp"), None),
        check_vma=False,
    )
```

```python
import jax
import jax.numpy as jnp
from jax import lax
from jax.experimental import pallas as pl
from jax.experimental.pallas import tpu as pltpu
from jax.sharding import Mesh, PartitionSpec as P

HEAD_DIMENSION = 128
MASK_BLOCK_SIZE = 64
SLASH_COUNT = 3
VERT_COUNT = 3
SLASH_REACH = 8


def passed_along(shard, axis, by):
    length = lax.axis_size(axis)
    pairs = [(i, i + by) for i in range(length) if 0 <= i + by < length]
    return lax.ppermute(shard, axis, pairs)


def attention_kernel(local_heads, group_blocks, back, base):
    block = MASK_BLOCK_SIZE
    key_count = (SLASH_COUNT + VERT_COUNT) * block
    scale = HEAD_DIMENSION ** (-0.5)

    def kernel(meta_ref, q_ref, k_ref, v_ref, vk_ref, vv_ref, o_ref):
        h = pl.program_id(0) + base
        first = meta_ref[2 * local_heads * SLASH_COUNT]
        offs = [meta_ref[h * SLASH_COUNT + j] for j in range(SLASH_COUNT)]
        verts = [meta_ref[local_heads * SLASH_COUNT + h * VERT_COUNT + j] for j in range(VERT_COUNT)]
        vert_keys = vk_ref[0]
        vert_values = vv_ref[0]
        col = lax.broadcasted_iota(jnp.int32, (block, key_count), 1)
        row = lax.broadcasted_iota(jnp.int32, (block, key_count), 0)
        reach = col % block - row
        lane = lax.broadcasted_iota(jnp.int32, (1, key_count), 1) // block
        never = jnp.int32(-4 * block)
        for b in range(group_blocks):
            qb = first + b
            q = q_ref[pl.ds(b * block, block), :]
            starts = [pl.multiple_of((back + b - offs[j]) * block, block) for j in range(SLASH_COUNT)]
            keys = jnp.concatenate([k_ref[pl.ds(s, block), :] for s in starts] + [vert_keys], 0)
            values = jnp.concatenate([v_ref[pl.ds(s, block), :] for s in starts] + [vert_values], 0)
            limits = [jnp.where(qb - offs[j] >= 0, offs[j] * block, never) for j in range(SLASH_COUNT)]
            for v in verts:
                ok = v <= qb
                for o in offs:
                    ok = jnp.logical_and(ok, qb - v != o)
                limits.append(jnp.where(ok, (qb - v) * block, never))
            limit = jnp.full((1, key_count), limits[-1], jnp.int32)
            for i in range(len(limits) - 2, -1, -1):
                limit = jnp.where(lane == i, limits[i], limit)
            allowed = reach <= limit
            scores = lax.dot_general(
                q, keys, (((1,), (1,)), ((), ())), preferred_element_type=jnp.float32
            ) * scale
            masked = jnp.where(allowed, scores, -1e30)
            top = jnp.max(masked, axis=1, keepdims=True)
            weight = jnp.exp(masked - top)
            total = jnp.sum(weight, axis=1, keepdims=True)
            rounded = weight.astype(jnp.bfloat16)
            acc = jnp.dot(rounded, values, preferred_element_type=jnp.float32)
            o_ref[pl.ds(b * block, block), :] = (acc / total).astype(o_ref.dtype)

    return kernel


def attend(meta, queries, key_window, value_window, vert_keys, vert_values, local_heads, sharing, base):
    group_rows = queries.shape[0]
    group_blocks = group_rows // MASK_BLOCK_SIZE
    head_size = HEAD_DIMENSION
    window_rows = key_window.shape[0]
    chunk_heads, vert_rows = vert_keys.shape[:2]
    grid_spec = pltpu.PrefetchScalarGridSpec(
        num_scalar_prefetch=1,
        grid=(chunk_heads,),
        in_specs=[
            pl.BlockSpec((group_rows, head_size), lambda h, m: (0, h + base)),
            pl.BlockSpec((window_rows, head_size), lambda h, m: (0, (h + base) // sharing)),
            pl.BlockSpec((window_rows, head_size), lambda h, m: (0, (h + base) // sharing)),
            pl.BlockSpec((1, vert_rows, head_size), lambda h, m: (h, 0, 0)),
            pl.BlockSpec((1, vert_rows, head_size), lambda h, m: (h, 0, 0)),
        ],
        out_specs=pl.BlockSpec((group_rows, head_size), lambda h, m: (0, h)),
    )
    return pl.pallas_call(
        attention_kernel(local_heads, group_blocks, window_rows // MASK_BLOCK_SIZE - group_blocks, base),
        grid_spec=grid_spec,
        out_shape=jax.ShapeDtypeStruct((group_rows, chunk_heads * head_size), queries.dtype),
    )(meta, queries, key_window, value_window, vert_keys, vert_values)


def per_device(query_rows, key_matrix, value_matrix, vertical, slash_offsets):
    tok_rows = query_rows.shape[0]
    heads_axes = ("inner", "grp")
    head_groups = lax.axis_size("inner") * lax.axis_size("grp")
    head_size = HEAD_DIMENSION
    block_size = MASK_BLOCK_SIZE
    local_heads = query_rows.shape[1] // (head_groups * head_size)
    local_kv = key_matrix.shape[1] // (head_groups * head_size)
    group_sharing_factor = local_heads // local_kv
    query_split = query_rows.reshape(tok_rows, head_groups, local_heads * head_size)
    key_split = key_matrix.reshape(tok_rows, head_groups, local_kv * head_size)
    value_split = value_matrix.reshape(tok_rows, head_groups, local_kv * head_size)
    query_group, key_group, value_group = (
        lax.all_to_all(query_split, heads_axes, split_axis=1, concat_axis=0, tiled=True),
        lax.all_to_all(key_split, heads_axes, split_axis=1, concat_axis=0, tiled=True),
        lax.all_to_all(value_split, heads_axes, split_axis=1, concat_axis=0, tiled=True),
    )
    group_rows = tok_rows * head_groups
    group_blocks = group_rows // block_size
    back = min(SLASH_REACH, group_blocks)
    key_local = key_group.reshape(group_rows, local_kv * head_size)
    value_local = value_group.reshape(group_rows, local_kv * head_size)
    key_before, value_before = passed_along(
        (key_local[group_rows - back * block_size:], value_local[group_rows - back * block_size:]),
        "outer", 1,
    )
    key_window = jnp.concatenate([key_before, key_local], 0)
    value_window = jnp.concatenate([value_before, value_local], 0)
    seq_index = lax.axis_index("outer")
    head_group = lax.axis_index(heads_axes)
    head_offsets = lax.dynamic_slice_in_dim(slash_offsets, head_group * local_heads, local_heads, 0)
    head_verts = lax.dynamic_slice_in_dim(vertical, head_group * local_heads, local_heads, 0)
    kv_index = jnp.arange(local_heads, dtype=jnp.int32) // group_sharing_factor
    owner_seq = head_verts // group_blocks
    local_block = head_verts % group_blocks
    key_blocks = key_local.reshape(group_blocks, block_size, local_kv, head_size)
    value_blocks = value_local.reshape(group_blocks, block_size, local_kv, head_size)
    picked_keys = key_blocks[local_block, :, kv_index[:, None], :]
    picked_values = value_blocks[local_block, :, kv_index[:, None], :]
    owned = (owner_seq == seq_index)[:, :, None, None]
    nothing = jnp.zeros((), picked_keys.dtype)
    seq_count = lax.axis_size("outer")
    mine = jnp.stack(
        [jnp.where(owned, picked_keys, nothing), jnp.where(owned, picked_values, nothing)]
    ).reshape(2, seq_count, -1, head_size).transpose(1, 0, 2, 3)
    part = lax.all_to_all(mine, "outer", split_axis=0, concat_axis=0, tiled=True).sum(
        0, dtype=picked_keys.dtype
    )
    spread = jnp.broadcast_to(part[None], (seq_count,) + part.shape)
    gathered = lax.all_to_all(spread, "outer", split_axis=0, concat_axis=0, tiled=True)
    vert = gathered.transpose(1, 0, 2, 3).reshape(2, local_heads, -1, head_size)
    first_block = (seq_index * group_blocks).astype(jnp.int32)
    meta = jnp.concatenate(
        [
            head_offsets.reshape(-1).astype(jnp.int32),
            head_verts.reshape(-1).astype(jnp.int32),
            first_block[None],
        ]
    )
    queries = query_group.reshape(group_rows, local_heads * head_size)
    results = attend(
        meta, queries, key_window, value_window, vert[0], vert[1],
        local_heads, group_sharing_factor, 0,
    )
    merged = results.reshape(head_groups, tok_rows, local_heads * head_size)
    returned = lax.all_to_all(merged, heads_axes, split_axis=0, concat_axis=0, tiled=True)
    return returned.transpose(1, 0, 2).reshape(tok_rows, head_groups * local_heads * head_size)


def solution(mesh):
    seq_count = mesh.shape["seq"]
    inner = 2 if seq_count % 2 == 0 else 1
    work_mesh = Mesh(
        mesh.devices.reshape(seq_count // inner, inner, mesh.shape["grp"]), ("outer", "inner", "grp")
    )
    rows = P(("outer", "inner", "grp"), None)
    return jax.shard_map(
        per_device,
        mesh=work_mesh,
        in_specs=(rows, rows, rows, P(), P()),
        out_specs=rows,
        check_vma=False,
    )
```

```python
import jax
import jax.numpy as jnp
from jax import lax
from jax.experimental import pallas as pl
from jax.experimental.pallas import tpu as pltpu
from jax.sharding import Mesh, PartitionSpec as P

HEAD_DIMENSION = 128
MASK_BLOCK_SIZE = 64
SLASH_COUNT = 3
VERT_COUNT = 3
SLASH_REACH = 8


def passed_along(shard, axis, by):
    length = lax.axis_size(axis)
    pairs = [(i, i + by) for i in range(length) if 0 <= i + by < length]
    return lax.ppermute(shard, axis, pairs)


def attention_kernel(local_heads, group_blocks, back, base):
    block = MASK_BLOCK_SIZE
    key_count = (SLASH_COUNT + VERT_COUNT) * block
    scale = HEAD_DIMENSION ** (-0.5)

    def kernel(meta_ref, q_ref, k_ref, v_ref, vk_ref, vv_ref, o_ref):
        h = pl.program_id(0) + base
        first = meta_ref[2 * local_heads * SLASH_COUNT]
        offs = [meta_ref[h * SLASH_COUNT + j] for j in range(SLASH_COUNT)]
        verts = [meta_ref[local_heads * SLASH_COUNT + h * VERT_COUNT + j] for j in range(VERT_COUNT)]
        vert_keys = vk_ref[0]
        vert_values = vv_ref[0]
        col = lax.broadcasted_iota(jnp.int32, (block, key_count), 1)
        row = lax.broadcasted_iota(jnp.int32, (block, key_count), 0)
        reach = col % block - row
        lane = lax.broadcasted_iota(jnp.int32, (1, key_count), 1) // block
        never = jnp.int32(-4 * block)
        for b in range(group_blocks):
            qb = first + b
            q = q_ref[pl.ds(b * block, block), :]
            starts = [pl.multiple_of((back + b - offs[j]) * block, block) for j in range(SLASH_COUNT)]
            keys = jnp.concatenate([k_ref[pl.ds(s, block), :] for s in starts] + [vert_keys], 0)
            values = jnp.concatenate([v_ref[pl.ds(s, block), :] for s in starts] + [vert_values], 0)
            limits = [jnp.where(qb - offs[j] >= 0, offs[j] * block, never) for j in range(SLASH_COUNT)]
            for v in verts:
                ok = v <= qb
                for o in offs:
                    ok = jnp.logical_and(ok, qb - v != o)
                limits.append(jnp.where(ok, (qb - v) * block, never))
            limit = jnp.full((1, key_count), limits[-1], jnp.int32)
            for i in range(len(limits) - 2, -1, -1):
                limit = jnp.where(lane == i, limits[i], limit)
            allowed = reach <= limit
            scores = lax.dot_general(
                q, keys, (((1,), (1,)), ((), ())), preferred_element_type=jnp.float32
            ) * scale
            masked = jnp.where(allowed, scores, -1e30)
            top = jnp.max(masked, axis=1, keepdims=True)
            weight = jnp.exp(masked - top)
            total = jnp.sum(weight, axis=1, keepdims=True)
            rounded = weight.astype(jnp.bfloat16)
            acc = jnp.dot(rounded, values, preferred_element_type=jnp.float32)
            o_ref[pl.ds(b * block, block), :] = (acc / total).astype(o_ref.dtype)

    return kernel


def attend(meta, queries, key_window, value_window, vert_keys, vert_values, local_heads, sharing, base):
    group_rows = queries.shape[0]
    group_blocks = group_rows // MASK_BLOCK_SIZE
    head_size = HEAD_DIMENSION
    window_rows = key_window.shape[0]
    chunk_heads, vert_rows = vert_keys.shape[:2]
    grid_spec = pltpu.PrefetchScalarGridSpec(
        num_scalar_prefetch=1,
        grid=(chunk_heads,),
        in_specs=[
            pl.BlockSpec((group_rows, head_size), lambda h, m: (0, h + base)),
            pl.BlockSpec((window_rows, head_size), lambda h, m: (0, (h + base) // sharing)),
            pl.BlockSpec((window_rows, head_size), lambda h, m: (0, (h + base) // sharing)),
            pl.BlockSpec((1, vert_rows, head_size), lambda h, m: (h, 0, 0)),
            pl.BlockSpec((1, vert_rows, head_size), lambda h, m: (h, 0, 0)),
        ],
        out_specs=pl.BlockSpec((group_rows, head_size), lambda h, m: (0, h)),
    )
    return pl.pallas_call(
        attention_kernel(local_heads, group_blocks, window_rows // MASK_BLOCK_SIZE - group_blocks, base),
        grid_spec=grid_spec,
        out_shape=jax.ShapeDtypeStruct((group_rows, chunk_heads * head_size), queries.dtype),
    )(meta, queries, key_window, value_window, vert_keys, vert_values)


def per_device(query_rows, key_matrix, value_matrix, vertical, slash_offsets):
    tok_rows = query_rows.shape[0]
    heads_axes = ("inner", "grp")
    head_groups = lax.axis_size("inner") * lax.axis_size("grp")
    head_size = HEAD_DIMENSION
    block_size = MASK_BLOCK_SIZE
    local_heads = query_rows.shape[1] // (head_groups * head_size)
    local_kv = key_matrix.shape[1] // (head_groups * head_size)
    group_sharing_factor = local_heads // local_kv
    query_split = query_rows.reshape(tok_rows, head_groups, local_heads * head_size)
    key_split = key_matrix.reshape(tok_rows, head_groups, local_kv * head_size)
    value_split = value_matrix.reshape(tok_rows, head_groups, local_kv * head_size)
    kv_group = lax.all_to_all(
        jnp.stack([key_split, value_split], 2), heads_axes, split_axis=1, concat_axis=0, tiled=True
    )
    key_group, value_group = kv_group[:, 0, 0], kv_group[:, 0, 1]
    me = lax.axis_index(heads_axes)
    received = [lax.dynamic_index_in_dim(query_split, me, 1, keepdims=False)]
    for shift in range(1, head_groups):
        sent = lax.dynamic_index_in_dim(query_split, (me + shift) % head_groups, 1, keepdims=False)
        received.append(
            lax.ppermute(sent, heads_axes, [(i, (i + shift) % head_groups) for i in range(head_groups)])
        )
    slab_shift = (me - jnp.arange(head_groups, dtype=jnp.int32)) % head_groups
    query_group = jnp.take(jnp.stack(received), slab_shift, axis=0)
    group_rows = tok_rows * head_groups
    group_blocks = group_rows // block_size
    back = min(SLASH_REACH, group_blocks)
    key_local = key_group.reshape(group_rows, local_kv * head_size)
    value_local = value_group.reshape(group_rows, local_kv * head_size)
    key_before, value_before = passed_along(
        (key_local[group_rows - back * block_size:], value_local[group_rows - back * block_size:]),
        "outer", 1,
    )
    key_window = jnp.concatenate([key_before, key_local], 0)
    value_window = jnp.concatenate([value_before, value_local], 0)
    seq_index = lax.axis_index("outer")
    head_group = lax.axis_index(heads_axes)
    head_offsets = lax.dynamic_slice_in_dim(slash_offsets, head_group * local_heads, local_heads, 0)
    head_verts = lax.dynamic_slice_in_dim(vertical, head_group * local_heads, local_heads, 0)
    kv_index = jnp.arange(local_heads, dtype=jnp.int32) // group_sharing_factor
    owner_seq = head_verts // group_blocks
    local_block = head_verts % group_blocks
    key_blocks = key_local.reshape(group_blocks, block_size, local_kv, head_size)
    value_blocks = value_local.reshape(group_blocks, block_size, local_kv, head_size)
    picked_keys = key_blocks[local_block, :, kv_index[:, None], :]
    picked_values = value_blocks[local_block, :, kv_index[:, None], :]
    owned = (owner_seq == seq_index)[:, :, None, None]
    nothing = jnp.zeros((), picked_keys.dtype)
    seq_count = lax.axis_size("outer")
    mine = jnp.stack(
        [jnp.where(owned, picked_keys, nothing), jnp.where(owned, picked_values, nothing)]
    ).reshape(2, seq_count, -1, head_size).transpose(1, 0, 2, 3)
    part = lax.all_to_all(mine, "outer", split_axis=0, concat_axis=0, tiled=True).sum(
        0, dtype=picked_keys.dtype
    )
    spread = jnp.broadcast_to(part[None], (seq_count,) + part.shape)
    gathered = lax.all_to_all(spread, "outer", split_axis=0, concat_axis=0, tiled=True)
    vert = gathered.transpose(1, 0, 2, 3).reshape(2, local_heads, -1, head_size)
    first_block = (seq_index * group_blocks).astype(jnp.int32)
    meta = jnp.concatenate(
        [
            head_offsets.reshape(-1).astype(jnp.int32),
            head_verts.reshape(-1).astype(jnp.int32),
            first_block[None],
        ]
    )
    queries = query_group.reshape(group_rows, local_heads * head_size)
    results = attend(
        meta, queries, key_window, value_window, vert[0], vert[1],
        local_heads, group_sharing_factor, 0,
    )
    merged = results.reshape(head_groups, tok_rows, local_heads * head_size)
    returned = lax.all_to_all(merged, heads_axes, split_axis=0, concat_axis=0, tiled=True)
    return returned.transpose(1, 0, 2).reshape(tok_rows, head_groups * local_heads * head_size)


def solution(mesh):
    seq_count = mesh.shape["seq"]
    inner = 2 if seq_count % 2 == 0 else 1
    work_mesh = Mesh(
        mesh.devices.reshape(seq_count // inner, inner, mesh.shape["grp"]), ("outer", "inner", "grp")
    )
    rows = P(("outer", "inner", "grp"), None)
    return jax.shard_map(
        per_device,
        mesh=work_mesh,
        in_specs=(rows, rows, rows, P(), P()),
        out_specs=rows,
        check_vma=False,
    )
```

```python
import jax
import jax.numpy as jnp
from jax import lax
from jax.experimental import pallas as pl
from jax.experimental.pallas import tpu as pltpu
from jax.sharding import Mesh, PartitionSpec as P

HEAD_DIMENSION = 128
MASK_BLOCK_SIZE = 64
SLASH_COUNT = 3
VERT_COUNT = 3
SLASH_REACH = 8
FULL_GATHER_BYTES = 4 << 20


def passed_along(shard, axis, by):
    length = lax.axis_size(axis)
    pairs = [(i, i + by) for i in range(length) if 0 <= i + by < length]
    return lax.ppermute(shard, axis, pairs)


def attention_kernel(local_heads, group_blocks, back, base):
    block = MASK_BLOCK_SIZE
    key_count = (SLASH_COUNT + VERT_COUNT) * block
    scale = HEAD_DIMENSION ** (-0.5)

    def kernel(meta_ref, q_ref, k_ref, v_ref, vk_ref, vv_ref, o_ref):
        h = pl.program_id(0) + base
        first = meta_ref[2 * local_heads * SLASH_COUNT]
        offs = [meta_ref[h * SLASH_COUNT + j] for j in range(SLASH_COUNT)]
        verts = [meta_ref[local_heads * SLASH_COUNT + h * VERT_COUNT + j] for j in range(VERT_COUNT)]
        vert_keys = vk_ref[0]
        vert_values = vv_ref[0]
        col = lax.broadcasted_iota(jnp.int32, (block, key_count), 1)
        row = lax.broadcasted_iota(jnp.int32, (block, key_count), 0)
        reach = col % block - row
        lane = lax.broadcasted_iota(jnp.int32, (1, key_count), 1) // block
        never = jnp.int32(-4 * block)
        for b in range(group_blocks):
            qb = first + b
            q = q_ref[pl.ds(b * block, block), :]
            starts = [pl.multiple_of((back + b - offs[j]) * block, block) for j in range(SLASH_COUNT)]
            keys = jnp.concatenate([k_ref[pl.ds(s, block), :] for s in starts] + [vert_keys], 0)
            values = jnp.concatenate([v_ref[pl.ds(s, block), :] for s in starts] + [vert_values], 0)
            limits = [jnp.where(qb - offs[j] >= 0, offs[j] * block, never) for j in range(SLASH_COUNT)]
            for v in verts:
                ok = v <= qb
                for o in offs:
                    ok = jnp.logical_and(ok, qb - v != o)
                limits.append(jnp.where(ok, (qb - v) * block, never))
            limit = jnp.full((1, key_count), limits[-1], jnp.int32)
            for i in range(len(limits) - 2, -1, -1):
                limit = jnp.where(lane == i, limits[i], limit)
            allowed = reach <= limit
            scores = lax.dot_general(
                q, keys, (((1,), (1,)), ((), ())), preferred_element_type=jnp.float32
            ) * scale
            masked = jnp.where(allowed, scores, -1e30)
            top = jnp.max(masked, axis=1, keepdims=True)
            weight = jnp.exp(masked - top)
            total = jnp.sum(weight, axis=1, keepdims=True)
            rounded = weight.astype(jnp.bfloat16)
            acc = jnp.dot(rounded, values, preferred_element_type=jnp.float32)
            o_ref[pl.ds(b * block, block), :] = (acc / total).astype(o_ref.dtype)

    return kernel


def full_kernel(local_heads, group_blocks):
    block = MASK_BLOCK_SIZE
    key_count = (SLASH_COUNT + VERT_COUNT) * block
    scale = HEAD_DIMENSION ** (-0.5)

    def kernel(meta_ref, q_ref, k_ref, v_ref, o_ref):
        h = pl.program_id(0)
        first = meta_ref[2 * local_heads * SLASH_COUNT]
        offs = [meta_ref[h * SLASH_COUNT + j] for j in range(SLASH_COUNT)]
        verts = [meta_ref[local_heads * SLASH_COUNT + h * VERT_COUNT + j] for j in range(VERT_COUNT)]
        vert_starts = [pl.multiple_of(v * block, block) for v in verts]
        vert_keys = [k_ref[pl.ds(s, block), :] for s in vert_starts]
        vert_values = [v_ref[pl.ds(s, block), :] for s in vert_starts]
        col = lax.broadcasted_iota(jnp.int32, (block, key_count), 1)
        row = lax.broadcasted_iota(jnp.int32, (block, key_count), 0)
        reach = col % block - row
        lane = lax.broadcasted_iota(jnp.int32, (1, key_count), 1) // block
        never = jnp.int32(-4 * block)
        for b in range(group_blocks):
            qb = first + b
            q = q_ref[pl.ds(b * block, block), :]
            starts = [pl.multiple_of(jnp.maximum(qb - offs[j], 0) * block, block) for j in range(SLASH_COUNT)]
            keys = jnp.concatenate([k_ref[pl.ds(s, block), :] for s in starts] + vert_keys, 0)
            values = jnp.concatenate([v_ref[pl.ds(s, block), :] for s in starts] + vert_values, 0)
            limits = [jnp.where(qb - offs[j] >= 0, offs[j] * block, never) for j in range(SLASH_COUNT)]
            for v in verts:
                ok = v <= qb
                for o in offs:
                    ok = jnp.logical_and(ok, qb - v != o)
                limits.append(jnp.where(ok, (qb - v) * block, never))
            limit = jnp.full((1, key_count), limits[-1], jnp.int32)
            for i in range(len(limits) - 2, -1, -1):
                limit = jnp.where(lane == i, limits[i], limit)
            allowed = reach <= limit
            scores = lax.dot_general(
                q, keys, (((1,), (1,)), ((), ())), preferred_element_type=jnp.float32
            ) * scale
            masked = jnp.where(allowed, scores, -1e30)
            top = jnp.max(masked, axis=1, keepdims=True)
            weight = jnp.exp(masked - top)
            total = jnp.sum(weight, axis=1, keepdims=True)
            rounded = weight.astype(jnp.bfloat16)
            acc = jnp.dot(rounded, values, preferred_element_type=jnp.float32)
            o_ref[pl.ds(b * block, block), :] = (acc / total).astype(o_ref.dtype)

    return kernel


def attend_full(meta, queries, all_keys, all_values, local_heads, sharing):
    group_rows = queries.shape[0]
    group_blocks = group_rows // MASK_BLOCK_SIZE
    head_size = HEAD_DIMENSION
    total_rows = all_keys.shape[0]
    grid_spec = pltpu.PrefetchScalarGridSpec(
        num_scalar_prefetch=1,
        grid=(local_heads,),
        in_specs=[
            pl.BlockSpec((group_rows, head_size), lambda h, m: (0, h)),
            pl.BlockSpec((total_rows, head_size), lambda h, m: (0, h // sharing)),
            pl.BlockSpec((total_rows, head_size), lambda h, m: (0, h // sharing)),
        ],
        out_specs=pl.BlockSpec((group_rows, head_size), lambda h, m: (0, h)),
    )
    return pl.pallas_call(
        full_kernel(local_heads, group_blocks),
        grid_spec=grid_spec,
        out_shape=jax.ShapeDtypeStruct((group_rows, local_heads * head_size), queries.dtype),
    )(meta, queries, all_keys, all_values)


def attend(meta, queries, key_window, value_window, vert_keys, vert_values, local_heads, sharing, base):
    group_rows = queries.shape[0]
    group_blocks = group_rows // MASK_BLOCK_SIZE
    head_size = HEAD_DIMENSION
    window_rows = key_window.shape[0]
    chunk_heads, vert_rows = vert_keys.shape[:2]
    grid_spec = pltpu.PrefetchScalarGridSpec(
        num_scalar_prefetch=1,
        grid=(chunk_heads,),
        in_specs=[
            pl.BlockSpec((group_rows, head_size), lambda h, m: (0, h + base)),
            pl.BlockSpec((window_rows, head_size), lambda h, m: (0, (h + base) // sharing)),
            pl.BlockSpec((window_rows, head_size), lambda h, m: (0, (h + base) // sharing)),
            pl.BlockSpec((1, vert_rows, head_size), lambda h, m: (h, 0, 0)),
            pl.BlockSpec((1, vert_rows, head_size), lambda h, m: (h, 0, 0)),
        ],
        out_specs=pl.BlockSpec((group_rows, head_size), lambda h, m: (0, h)),
    )
    return pl.pallas_call(
        attention_kernel(local_heads, group_blocks, window_rows // MASK_BLOCK_SIZE - group_blocks, base),
        grid_spec=grid_spec,
        out_shape=jax.ShapeDtypeStruct((group_rows, chunk_heads * head_size), queries.dtype),
    )(meta, queries, key_window, value_window, vert_keys, vert_values)


def per_device(query_rows, key_matrix, value_matrix, vertical, slash_offsets):
    tok_rows = query_rows.shape[0]
    heads_axes = ("inner", "grp")
    head_groups = lax.axis_size("inner") * lax.axis_size("grp")
    head_size = HEAD_DIMENSION
    block_size = MASK_BLOCK_SIZE
    local_heads = query_rows.shape[1] // (head_groups * head_size)
    local_kv = key_matrix.shape[1] // (head_groups * head_size)
    group_sharing_factor = local_heads // local_kv
    query_split = query_rows.reshape(tok_rows, head_groups, local_heads * head_size)
    key_split = key_matrix.reshape(tok_rows, head_groups, local_kv * head_size)
    value_split = value_matrix.reshape(tok_rows, head_groups, local_kv * head_size)
    kv_group = lax.all_to_all(
        jnp.stack([key_split, value_split], 2), heads_axes, split_axis=1, concat_axis=0, tiled=True
    )
    key_group, value_group = kv_group[:, 0, 0], kv_group[:, 0, 1]
    me = lax.axis_index(heads_axes)
    received = [lax.dynamic_index_in_dim(query_split, me, 1, keepdims=False)]
    for shift in range(1, head_groups):
        sent = lax.dynamic_index_in_dim(query_split, (me + shift) % head_groups, 1, keepdims=False)
        received.append(
            lax.ppermute(sent, heads_axes, [(i, (i + shift) % head_groups) for i in range(head_groups)])
        )
    slab_shift = (me - jnp.arange(head_groups, dtype=jnp.int32)) % head_groups
    query_group = jnp.take(jnp.stack(received), slab_shift, axis=0)
    group_rows = tok_rows * head_groups
    group_blocks = group_rows // block_size
    back = min(SLASH_REACH, group_blocks)
    key_local = key_group.reshape(group_rows, local_kv * head_size)
    value_local = value_group.reshape(group_rows, local_kv * head_size)
    seq_count = lax.axis_size("outer")
    seq_index = lax.axis_index("outer")
    head_group = lax.axis_index(heads_axes)
    head_offsets = lax.dynamic_slice_in_dim(slash_offsets, head_group * local_heads, local_heads, 0)
    head_verts = lax.dynamic_slice_in_dim(vertical, head_group * local_heads, local_heads, 0)
    first_block = (seq_index * group_blocks).astype(jnp.int32)
    meta = jnp.concatenate(
        [
            head_offsets.reshape(-1).astype(jnp.int32),
            head_verts.reshape(-1).astype(jnp.int32),
            first_block[None],
        ]
    )
    if seq_count * kv_group.size * kv_group.dtype.itemsize <= FULL_GATHER_BYTES:
        own = jnp.stack([key_local, value_local])
        spread = jnp.broadcast_to(own[None], (seq_count,) + own.shape)
        everything = lax.all_to_all(spread, "outer", split_axis=0, concat_axis=0, tiled=True)
        everything = everything.transpose(1, 0, 2, 3).reshape(2, seq_count * group_rows, -1)
        queries = query_group.reshape(group_rows, local_heads * head_size)
        results = attend_full(
            meta, queries, everything[0], everything[1], local_heads, group_sharing_factor
        )
        merged = results.reshape(head_groups, tok_rows, local_heads * head_size)
        returned = lax.all_to_all(merged, heads_axes, split_axis=0, concat_axis=0, tiled=True)
        return returned.transpose(1, 0, 2).reshape(tok_rows, head_groups * local_heads * head_size)
    key_before, value_before = passed_along(
        (key_local[group_rows - back * block_size:], value_local[group_rows - back * block_size:]),
        "outer", 1,
    )
    key_window = jnp.concatenate([key_before, key_local], 0)
    value_window = jnp.concatenate([value_before, value_local], 0)
    kv_index = jnp.arange(local_heads, dtype=jnp.int32) // group_sharing_factor
    owner_seq = head_verts // group_blocks
    local_block = head_verts % group_blocks
    key_blocks = key_local.reshape(group_blocks, block_size, local_kv, head_size)
    value_blocks = value_local.reshape(group_blocks, block_size, local_kv, head_size)
    picked_keys = key_blocks[local_block, :, kv_index[:, None], :]
    picked_values = value_blocks[local_block, :, kv_index[:, None], :]
    owned = (owner_seq == seq_index)[:, :, None, None]
    nothing = jnp.zeros((), picked_keys.dtype)
    mine = jnp.stack(
        [jnp.where(owned, picked_keys, nothing), jnp.where(owned, picked_values, nothing)]
    ).reshape(2, seq_count, -1, head_size).transpose(1, 0, 2, 3)
    part = lax.all_to_all(mine, "outer", split_axis=0, concat_axis=0, tiled=True).sum(
        0, dtype=picked_keys.dtype
    )
    spread = jnp.broadcast_to(part[None], (seq_count,) + part.shape)
    gathered = lax.all_to_all(spread, "outer", split_axis=0, concat_axis=0, tiled=True)
    vert = gathered.transpose(1, 0, 2, 3).reshape(2, local_heads, -1, head_size)
    queries = query_group.reshape(group_rows, local_heads * head_size)
    results = attend(
        meta, queries, key_window, value_window, vert[0], vert[1],
        local_heads, group_sharing_factor, 0,
    )
    merged = results.reshape(head_groups, tok_rows, local_heads * head_size)
    returned = lax.all_to_all(merged, heads_axes, split_axis=0, concat_axis=0, tiled=True)
    return returned.transpose(1, 0, 2).reshape(tok_rows, head_groups * local_heads * head_size)


def solution(mesh):
    seq_count = mesh.shape["seq"]
    inner = 2 if seq_count % 2 == 0 else 1
    work_mesh = Mesh(
        mesh.devices.reshape(seq_count // inner, inner, mesh.shape["grp"]), ("outer", "inner", "grp")
    )
    rows = P(("outer", "inner", "grp"), None)
    return jax.shard_map(
        per_device,
        mesh=work_mesh,
        in_specs=(rows, rows, rows, P(), P()),
        out_specs=rows,
        check_vma=False,
    )
```

```python
import jax
import jax.numpy as jnp
from jax import lax
from jax.experimental import pallas as pl
from jax.experimental.pallas import tpu as pltpu
from jax.sharding import Mesh, PartitionSpec as P

HEAD_DIMENSION = 128
MASK_BLOCK_SIZE = 64
SLASH_COUNT = 3
VERT_COUNT = 3
SLASH_REACH = 8
FULL_GATHER_BYTES = 4 << 20
OUTPUT_CHUNKS = 2


def passed_along(shard, axis, by):
    length = lax.axis_size(axis)
    pairs = [(i, i + by) for i in range(length) if 0 <= i + by < length]
    return lax.ppermute(shard, axis, pairs)


def attention_kernel(local_heads, group_blocks, back, base):
    block = MASK_BLOCK_SIZE
    key_count = (SLASH_COUNT + VERT_COUNT) * block
    scale = HEAD_DIMENSION ** (-0.5)

    def kernel(meta_ref, q_ref, k_ref, v_ref, vk_ref, vv_ref, o_ref):
        h = pl.program_id(0) + base
        first = meta_ref[2 * local_heads * SLASH_COUNT]
        offs = [meta_ref[h * SLASH_COUNT + j] for j in range(SLASH_COUNT)]
        verts = [meta_ref[local_heads * SLASH_COUNT + h * VERT_COUNT + j] for j in range(VERT_COUNT)]
        vert_keys = vk_ref[0]
        vert_values = vv_ref[0]
        col = lax.broadcasted_iota(jnp.int32, (block, key_count), 1)
        row = lax.broadcasted_iota(jnp.int32, (block, key_count), 0)
        reach = col % block - row
        lane = lax.broadcasted_iota(jnp.int32, (1, key_count), 1) // block
        never = jnp.int32(-4 * block)
        for b in range(group_blocks):
            qb = first + b
            q = q_ref[pl.ds(b * block, block), :]
            starts = [pl.multiple_of((back + b - offs[j]) * block, block) for j in range(SLASH_COUNT)]
            keys = jnp.concatenate([k_ref[pl.ds(s, block), :] for s in starts] + [vert_keys], 0)
            values = jnp.concatenate([v_ref[pl.ds(s, block), :] for s in starts] + [vert_values], 0)
            limits = [jnp.where(qb - offs[j] >= 0, offs[j] * block, never) for j in range(SLASH_COUNT)]
            for v in verts:
                ok = v <= qb
                for o in offs:
                    ok = jnp.logical_and(ok, qb - v != o)
                limits.append(jnp.where(ok, (qb - v) * block, never))
            limit = jnp.full((1, key_count), limits[-1], jnp.int32)
            for i in range(len(limits) - 2, -1, -1):
                limit = jnp.where(lane == i, limits[i], limit)
            allowed = reach <= limit
            scores = lax.dot_general(
                q, keys, (((1,), (1,)), ((), ())), preferred_element_type=jnp.float32
            ) * scale
            masked = jnp.where(allowed, scores, -1e30)
            top = jnp.max(masked, axis=1, keepdims=True)
            weight = jnp.exp(masked - top)
            total = jnp.sum(weight, axis=1, keepdims=True)
            rounded = weight.astype(jnp.bfloat16)
            acc = jnp.dot(rounded, values, preferred_element_type=jnp.float32)
            o_ref[pl.ds(b * block, block), :] = (acc / total).astype(o_ref.dtype)

    return kernel


def full_kernel(local_heads, group_blocks, base):
    block = MASK_BLOCK_SIZE
    key_count = (SLASH_COUNT + VERT_COUNT) * block
    scale = HEAD_DIMENSION ** (-0.5)

    def kernel(meta_ref, q_ref, k_ref, v_ref, o_ref):
        h = pl.program_id(0) + base
        first = meta_ref[2 * local_heads * SLASH_COUNT]
        offs = [meta_ref[h * SLASH_COUNT + j] for j in range(SLASH_COUNT)]
        verts = [meta_ref[local_heads * SLASH_COUNT + h * VERT_COUNT + j] for j in range(VERT_COUNT)]
        vert_starts = [pl.multiple_of(v * block, block) for v in verts]
        vert_keys = [k_ref[pl.ds(s, block), :] for s in vert_starts]
        vert_values = [v_ref[pl.ds(s, block), :] for s in vert_starts]
        col = lax.broadcasted_iota(jnp.int32, (block, key_count), 1)
        row = lax.broadcasted_iota(jnp.int32, (block, key_count), 0)
        reach = col % block - row
        lane = lax.broadcasted_iota(jnp.int32, (1, key_count), 1) // block
        never = jnp.int32(-4 * block)
        for b in range(group_blocks):
            qb = first + b
            q = q_ref[pl.ds(b * block, block), :]
            starts = [pl.multiple_of(jnp.maximum(qb - offs[j], 0) * block, block) for j in range(SLASH_COUNT)]
            keys = jnp.concatenate([k_ref[pl.ds(s, block), :] for s in starts] + vert_keys, 0)
            values = jnp.concatenate([v_ref[pl.ds(s, block), :] for s in starts] + vert_values, 0)
            limits = [jnp.where(qb - offs[j] >= 0, offs[j] * block, never) for j in range(SLASH_COUNT)]
            for v in verts:
                ok = v <= qb
                for o in offs:
                    ok = jnp.logical_and(ok, qb - v != o)
                limits.append(jnp.where(ok, (qb - v) * block, never))
            limit = jnp.full((1, key_count), limits[-1], jnp.int32)
            for i in range(len(limits) - 2, -1, -1):
                limit = jnp.where(lane == i, limits[i], limit)
            allowed = reach <= limit
            scores = lax.dot_general(
                q, keys, (((1,), (1,)), ((), ())), preferred_element_type=jnp.float32
            ) * scale
            masked = jnp.where(allowed, scores, -1e30)
            top = jnp.max(masked, axis=1, keepdims=True)
            weight = jnp.exp(masked - top)
            total = jnp.sum(weight, axis=1, keepdims=True)
            rounded = weight.astype(jnp.bfloat16)
            acc = jnp.dot(rounded, values, preferred_element_type=jnp.float32)
            o_ref[pl.ds(b * block, block), :] = (acc / total).astype(o_ref.dtype)

    return kernel


def attend_full(meta, queries, all_keys, all_values, local_heads, sharing, base, chunk_heads):
    group_rows = queries.shape[0]
    group_blocks = group_rows // MASK_BLOCK_SIZE
    head_size = HEAD_DIMENSION
    total_rows = all_keys.shape[0]
    grid_spec = pltpu.PrefetchScalarGridSpec(
        num_scalar_prefetch=1,
        grid=(chunk_heads,),
        in_specs=[
            pl.BlockSpec((group_rows, head_size), lambda h, m: (0, h + base)),
            pl.BlockSpec((total_rows, head_size), lambda h, m: (0, (h + base) // sharing)),
            pl.BlockSpec((total_rows, head_size), lambda h, m: (0, (h + base) // sharing)),
        ],
        out_specs=pl.BlockSpec((group_rows, head_size), lambda h, m: (0, h)),
    )
    return pl.pallas_call(
        full_kernel(local_heads, group_blocks, base),
        grid_spec=grid_spec,
        out_shape=jax.ShapeDtypeStruct((group_rows, chunk_heads * head_size), queries.dtype),
    )(meta, queries, all_keys, all_values)


def attend(meta, queries, key_window, value_window, vert_keys, vert_values, local_heads, sharing, base):
    group_rows = queries.shape[0]
    group_blocks = group_rows // MASK_BLOCK_SIZE
    head_size = HEAD_DIMENSION
    window_rows = key_window.shape[0]
    chunk_heads, vert_rows = vert_keys.shape[:2]
    grid_spec = pltpu.PrefetchScalarGridSpec(
        num_scalar_prefetch=1,
        grid=(chunk_heads,),
        in_specs=[
            pl.BlockSpec((group_rows, head_size), lambda h, m: (0, h + base)),
            pl.BlockSpec((window_rows, head_size), lambda h, m: (0, (h + base) // sharing)),
            pl.BlockSpec((window_rows, head_size), lambda h, m: (0, (h + base) // sharing)),
            pl.BlockSpec((1, vert_rows, head_size), lambda h, m: (h, 0, 0)),
            pl.BlockSpec((1, vert_rows, head_size), lambda h, m: (h, 0, 0)),
        ],
        out_specs=pl.BlockSpec((group_rows, head_size), lambda h, m: (0, h)),
    )
    return pl.pallas_call(
        attention_kernel(local_heads, group_blocks, window_rows // MASK_BLOCK_SIZE - group_blocks, base),
        grid_spec=grid_spec,
        out_shape=jax.ShapeDtypeStruct((group_rows, chunk_heads * head_size), queries.dtype),
    )(meta, queries, key_window, value_window, vert_keys, vert_values)


def per_device(query_rows, key_matrix, value_matrix, vertical, slash_offsets):
    tok_rows = query_rows.shape[0]
    heads_axes = ("inner", "grp")
    head_groups = lax.axis_size("inner") * lax.axis_size("grp")
    head_size = HEAD_DIMENSION
    block_size = MASK_BLOCK_SIZE
    local_heads = query_rows.shape[1] // (head_groups * head_size)
    local_kv = key_matrix.shape[1] // (head_groups * head_size)
    group_sharing_factor = local_heads // local_kv
    query_split = query_rows.reshape(tok_rows, head_groups, local_heads * head_size)
    key_split = key_matrix.reshape(tok_rows, head_groups, local_kv * head_size)
    value_split = value_matrix.reshape(tok_rows, head_groups, local_kv * head_size)
    kv_group = lax.all_to_all(
        jnp.stack([key_split, value_split], 2), heads_axes, split_axis=1, concat_axis=0, tiled=True
    )
    key_group, value_group = kv_group[:, 0, 0], kv_group[:, 0, 1]
    me = lax.axis_index(heads_axes)
    received = [lax.dynamic_index_in_dim(query_split, me, 1, keepdims=False)]
    for shift in range(1, head_groups):
        sent = lax.dynamic_index_in_dim(query_split, (me + shift) % head_groups, 1, keepdims=False)
        received.append(
            lax.ppermute(sent, heads_axes, [(i, (i + shift) % head_groups) for i in range(head_groups)])
        )
    slab_shift = (me - jnp.arange(head_groups, dtype=jnp.int32)) % head_groups
    query_group = jnp.take(jnp.stack(received), slab_shift, axis=0)
    group_rows = tok_rows * head_groups
    group_blocks = group_rows // block_size
    back = min(SLASH_REACH, group_blocks)
    key_local = key_group.reshape(group_rows, local_kv * head_size)
    value_local = value_group.reshape(group_rows, local_kv * head_size)
    seq_count = lax.axis_size("outer")
    seq_index = lax.axis_index("outer")
    head_group = lax.axis_index(heads_axes)
    head_offsets = lax.dynamic_slice_in_dim(slash_offsets, head_group * local_heads, local_heads, 0)
    head_verts = lax.dynamic_slice_in_dim(vertical, head_group * local_heads, local_heads, 0)
    first_block = (seq_index * group_blocks).astype(jnp.int32)
    meta = jnp.concatenate(
        [
            head_offsets.reshape(-1).astype(jnp.int32),
            head_verts.reshape(-1).astype(jnp.int32),
            first_block[None],
        ]
    )
    if seq_count * kv_group.size * kv_group.dtype.itemsize <= FULL_GATHER_BYTES:
        own = jnp.stack([key_local, value_local])
        spread = jnp.broadcast_to(own[None], (seq_count,) + own.shape)
        everything = lax.all_to_all(spread, "outer", split_axis=0, concat_axis=0, tiled=True)
        everything = everything.transpose(1, 0, 2, 3).reshape(2, seq_count * group_rows, -1)
        queries = query_group.reshape(group_rows, local_heads * head_size)
        chunk_heads = local_heads // OUTPUT_CHUNKS
        pieces = []
        for c in range(OUTPUT_CHUNKS):
            results = attend_full(
                meta, queries, everything[0], everything[1], local_heads, group_sharing_factor,
                c * chunk_heads, chunk_heads,
            )
            merged = results.reshape(head_groups, tok_rows, chunk_heads * head_size)
            pieces.append(lax.all_to_all(merged, heads_axes, split_axis=0, concat_axis=0, tiled=True))
        returned = jnp.stack(pieces, 1)
        return returned.transpose(2, 0, 1, 3).reshape(tok_rows, head_groups * local_heads * head_size)
    key_before, value_before = passed_along(
        (key_local[group_rows - back * block_size:], value_local[group_rows - back * block_size:]),
        "outer", 1,
    )
    key_window = jnp.concatenate([key_before, key_local], 0)
    value_window = jnp.concatenate([value_before, value_local], 0)
    kv_index = jnp.arange(local_heads, dtype=jnp.int32) // group_sharing_factor
    owner_seq = head_verts // group_blocks
    local_block = head_verts % group_blocks
    key_blocks = key_local.reshape(group_blocks, block_size, local_kv, head_size)
    value_blocks = value_local.reshape(group_blocks, block_size, local_kv, head_size)
    picked_keys = key_blocks[local_block, :, kv_index[:, None], :]
    picked_values = value_blocks[local_block, :, kv_index[:, None], :]
    owned = (owner_seq == seq_index)[:, :, None, None]
    nothing = jnp.zeros((), picked_keys.dtype)
    mine = jnp.stack(
        [jnp.where(owned, picked_keys, nothing), jnp.where(owned, picked_values, nothing)]
    ).reshape(2, seq_count, -1, head_size).transpose(1, 0, 2, 3)
    part = lax.all_to_all(mine, "outer", split_axis=0, concat_axis=0, tiled=True).sum(
        0, dtype=picked_keys.dtype
    )
    spread = jnp.broadcast_to(part[None], (seq_count,) + part.shape)
    gathered = lax.all_to_all(spread, "outer", split_axis=0, concat_axis=0, tiled=True)
    vert = gathered.transpose(1, 0, 2, 3).reshape(2, local_heads, -1, head_size)
    queries = query_group.reshape(group_rows, local_heads * head_size)
    results = attend(
        meta, queries, key_window, value_window, vert[0], vert[1],
        local_heads, group_sharing_factor, 0,
    )
    merged = results.reshape(head_groups, tok_rows, local_heads * head_size)
    returned = lax.all_to_all(merged, heads_axes, split_axis=0, concat_axis=0, tiled=True)
    return returned.transpose(1, 0, 2).reshape(tok_rows, head_groups * local_heads * head_size)


def solution(mesh):
    seq_count = mesh.shape["seq"]
    inner = 2 if seq_count % 2 == 0 else 1
    work_mesh = Mesh(
        mesh.devices.reshape(seq_count // inner, inner, mesh.shape["grp"]), ("outer", "inner", "grp")
    )
    rows = P(("outer", "inner", "grp"), None)
    return jax.shard_map(
        per_device,
        mesh=work_mesh,
        in_specs=(rows, rows, rows, P(), P()),
        out_specs=rows,
        check_vma=False,
    )
```

```python
import jax
import jax.numpy as jnp
from jax import lax
from jax.experimental import pallas as pl
from jax.experimental.pallas import tpu as pltpu
from jax.sharding import Mesh, PartitionSpec as P

HEAD_DIMENSION = 128
MASK_BLOCK_SIZE = 64
SLASH_COUNT = 3
VERT_COUNT = 3
SLASH_REACH = 8
FULL_GATHER_BYTES = 4 << 20
OUTPUT_CHUNKS = 2


def passed_along(shard, axis, by):
    length = lax.axis_size(axis)
    pairs = [(i, i + by) for i in range(length) if 0 <= i + by < length]
    return lax.ppermute(shard, axis, pairs)


def attention_kernel(local_heads, group_blocks, back, base):
    block = MASK_BLOCK_SIZE
    key_count = (SLASH_COUNT + VERT_COUNT) * block
    scale = HEAD_DIMENSION ** (-0.5)

    def kernel(meta_ref, q_ref, k_ref, v_ref, vk_ref, vv_ref, o_ref):
        h = pl.program_id(0) + base
        first = meta_ref[2 * local_heads * SLASH_COUNT]
        offs = [meta_ref[h * SLASH_COUNT + j] for j in range(SLASH_COUNT)]
        verts = [meta_ref[local_heads * SLASH_COUNT + h * VERT_COUNT + j] for j in range(VERT_COUNT)]
        vert_keys = vk_ref[0]
        vert_values = vv_ref[0]
        col = lax.broadcasted_iota(jnp.int32, (block, key_count), 1)
        row = lax.broadcasted_iota(jnp.int32, (block, key_count), 0)
        reach = col % block - row
        lane = lax.broadcasted_iota(jnp.int32, (1, key_count), 1) // block
        never = jnp.int32(-4 * block)
        for b in range(group_blocks):
            qb = first + b
            q = q_ref[pl.ds(b * block, block), :]
            starts = [pl.multiple_of((back + b - offs[j]) * block, block) for j in range(SLASH_COUNT)]
            keys = jnp.concatenate([k_ref[pl.ds(s, block), :] for s in starts] + [vert_keys], 0)
            values = jnp.concatenate([v_ref[pl.ds(s, block), :] for s in starts] + [vert_values], 0)
            limits = [jnp.where(qb - offs[j] >= 0, offs[j] * block, never) for j in range(SLASH_COUNT)]
            for v in verts:
                ok = v <= qb
                for o in offs:
                    ok = jnp.logical_and(ok, qb - v != o)
                limits.append(jnp.where(ok, (qb - v) * block, never))
            limit = jnp.full((1, key_count), limits[-1], jnp.int32)
            for i in range(len(limits) - 2, -1, -1):
                limit = jnp.where(lane == i, limits[i], limit)
            allowed = reach <= limit
            scores = lax.dot_general(
                q, keys, (((1,), (1,)), ((), ())), preferred_element_type=jnp.float32
            ) * scale
            masked = jnp.where(allowed, scores, -1e30)
            top = jnp.max(masked, axis=1, keepdims=True)
            weight = jnp.exp(masked - top)
            total = jnp.sum(weight, axis=1, keepdims=True)
            rounded = weight.astype(jnp.bfloat16)
            acc = jnp.dot(rounded, values, preferred_element_type=jnp.float32)
            o_ref[pl.ds(b * block, block), :] = (acc / total).astype(o_ref.dtype)

    return kernel


def full_kernel(local_heads, group_blocks, base):
    block = MASK_BLOCK_SIZE
    key_count = (SLASH_COUNT + VERT_COUNT) * block
    scale = HEAD_DIMENSION ** (-0.5)

    def kernel(meta_ref, q_ref, k_ref, v_ref, o_ref):
        h = pl.program_id(0) + base
        first = meta_ref[2 * local_heads * SLASH_COUNT]
        offs = [meta_ref[h * SLASH_COUNT + j] for j in range(SLASH_COUNT)]
        verts = [meta_ref[local_heads * SLASH_COUNT + h * VERT_COUNT + j] for j in range(VERT_COUNT)]
        vert_starts = [pl.multiple_of(v * block, block) for v in verts]
        vert_keys = [k_ref[pl.ds(s, block), :] for s in vert_starts]
        vert_values = [v_ref[pl.ds(s, block), :] for s in vert_starts]
        col = lax.broadcasted_iota(jnp.int32, (block, key_count), 1)
        row = lax.broadcasted_iota(jnp.int32, (block, key_count), 0)
        reach = col % block - row
        lane = lax.broadcasted_iota(jnp.int32, (1, key_count), 1) // block
        never = jnp.int32(-4 * block)
        for b in range(group_blocks):
            qb = first + b
            q = q_ref[pl.ds(b * block, block), :]
            starts = [pl.multiple_of(jnp.maximum(qb - offs[j], 0) * block, block) for j in range(SLASH_COUNT)]
            keys = jnp.concatenate([k_ref[pl.ds(s, block), :] for s in starts] + vert_keys, 0)
            values = jnp.concatenate([v_ref[pl.ds(s, block), :] for s in starts] + vert_values, 0)
            limits = [jnp.where(qb - offs[j] >= 0, offs[j] * block, never) for j in range(SLASH_COUNT)]
            for v in verts:
                ok = v <= qb
                for o in offs:
                    ok = jnp.logical_and(ok, qb - v != o)
                limits.append(jnp.where(ok, (qb - v) * block, never))
            limit = jnp.full((1, key_count), limits[-1], jnp.int32)
            for i in range(len(limits) - 2, -1, -1):
                limit = jnp.where(lane == i, limits[i], limit)
            allowed = reach <= limit
            scores = lax.dot_general(
                q, keys, (((1,), (1,)), ((), ())), preferred_element_type=jnp.float32
            ) * scale
            masked = jnp.where(allowed, scores, -1e30)
            top = jnp.max(masked, axis=1, keepdims=True)
            weight = jnp.exp(masked - top)
            total = jnp.sum(weight, axis=1, keepdims=True)
            rounded = weight.astype(jnp.bfloat16)
            acc = jnp.dot(rounded, values, preferred_element_type=jnp.float32)
            o_ref[pl.ds(b * block, block), :] = (acc / total).astype(o_ref.dtype)

    return kernel


def attend_full(meta, queries, all_keys, all_values, local_heads, sharing, base, chunk_heads):
    group_rows = queries.shape[0]
    group_blocks = group_rows // MASK_BLOCK_SIZE
    head_size = HEAD_DIMENSION
    total_rows = all_keys.shape[0]
    grid_spec = pltpu.PrefetchScalarGridSpec(
        num_scalar_prefetch=1,
        grid=(chunk_heads,),
        in_specs=[
            pl.BlockSpec((group_rows, head_size), lambda h, m: (0, h + base)),
            pl.BlockSpec((total_rows, head_size), lambda h, m: (0, (h + base) // sharing)),
            pl.BlockSpec((total_rows, head_size), lambda h, m: (0, (h + base) // sharing)),
        ],
        out_specs=pl.BlockSpec((group_rows, head_size), lambda h, m: (0, h)),
    )
    return pl.pallas_call(
        full_kernel(local_heads, group_blocks, base),
        grid_spec=grid_spec,
        out_shape=jax.ShapeDtypeStruct((group_rows, chunk_heads * head_size), queries.dtype),
    )(meta, queries, all_keys, all_values)


def attend(meta, queries, key_window, value_window, vert_keys, vert_values, local_heads, sharing, base):
    group_rows = queries.shape[0]
    group_blocks = group_rows // MASK_BLOCK_SIZE
    head_size = HEAD_DIMENSION
    window_rows = key_window.shape[0]
    chunk_heads, vert_rows = vert_keys.shape[:2]
    grid_spec = pltpu.PrefetchScalarGridSpec(
        num_scalar_prefetch=1,
        grid=(chunk_heads,),
        in_specs=[
            pl.BlockSpec((group_rows, head_size), lambda h, m: (0, h + base)),
            pl.BlockSpec((window_rows, head_size), lambda h, m: (0, (h + base) // sharing)),
            pl.BlockSpec((window_rows, head_size), lambda h, m: (0, (h + base) // sharing)),
            pl.BlockSpec((1, vert_rows, head_size), lambda h, m: (h, 0, 0)),
            pl.BlockSpec((1, vert_rows, head_size), lambda h, m: (h, 0, 0)),
        ],
        out_specs=pl.BlockSpec((group_rows, head_size), lambda h, m: (0, h)),
    )
    return pl.pallas_call(
        attention_kernel(local_heads, group_blocks, window_rows // MASK_BLOCK_SIZE - group_blocks, base),
        grid_spec=grid_spec,
        out_shape=jax.ShapeDtypeStruct((group_rows, chunk_heads * head_size), queries.dtype),
    )(meta, queries, key_window, value_window, vert_keys, vert_values)


def per_device(query_rows, key_matrix, value_matrix, vertical, slash_offsets):
    tok_rows = query_rows.shape[0]
    heads_axes = ("inner", "grp")
    head_groups = lax.axis_size("inner") * lax.axis_size("grp")
    head_size = HEAD_DIMENSION
    block_size = MASK_BLOCK_SIZE
    local_heads = query_rows.shape[1] // (head_groups * head_size)
    local_kv = key_matrix.shape[1] // (head_groups * head_size)
    group_sharing_factor = local_heads // local_kv
    query_split = query_rows.reshape(tok_rows, head_groups, local_heads * head_size)
    key_split = key_matrix.reshape(tok_rows, head_groups, local_kv * head_size)
    value_split = value_matrix.reshape(tok_rows, head_groups, local_kv * head_size)
    kv_group = lax.all_to_all(
        jnp.stack([key_split, value_split], 2), heads_axes, split_axis=1, concat_axis=0, tiled=True
    )
    key_group, value_group = kv_group[:, 0, 0], kv_group[:, 0, 1]
    me = lax.axis_index(heads_axes)
    received = [lax.dynamic_index_in_dim(query_split, me, 1, keepdims=False)]
    for shift in range(1, head_groups):
        sent = lax.dynamic_index_in_dim(query_split, (me + shift) % head_groups, 1, keepdims=False)
        received.append(
            lax.ppermute(sent, heads_axes, [(i, (i + shift) % head_groups) for i in range(head_groups)])
        )
    slab_shift = (me - jnp.arange(head_groups, dtype=jnp.int32)) % head_groups
    query_group = jnp.take(jnp.stack(received), slab_shift, axis=0)
    group_rows = tok_rows * head_groups
    group_blocks = group_rows // block_size
    back = min(SLASH_REACH, group_blocks)
    key_local = key_group.reshape(group_rows, local_kv * head_size)
    value_local = value_group.reshape(group_rows, local_kv * head_size)
    seq_count = lax.axis_size("outer")
    seq_index = lax.axis_index("outer")
    head_group = lax.axis_index(heads_axes)
    head_offsets = lax.dynamic_slice_in_dim(slash_offsets, head_group * local_heads, local_heads, 0)
    head_verts = lax.dynamic_slice_in_dim(vertical, head_group * local_heads, local_heads, 0)
    first_block = (seq_index * group_blocks).astype(jnp.int32)
    meta = jnp.concatenate(
        [
            head_offsets.reshape(-1).astype(jnp.int32),
            head_verts.reshape(-1).astype(jnp.int32),
            first_block[None],
        ]
    )
    if seq_count * kv_group.size * kv_group.dtype.itemsize <= FULL_GATHER_BYTES:
        own = jnp.stack([key_local, value_local])
        relayed = [own]
        for _ in range(1, seq_count):
            relayed.append(passed_along(relayed[-1], "outer", 1))
        order = (seq_index - jnp.arange(seq_count, dtype=jnp.int32)) % seq_count
        everything = jnp.take(jnp.stack(relayed), order, axis=0)
        everything = everything.transpose(1, 0, 2, 3).reshape(2, seq_count * group_rows, -1)
        queries = query_group.reshape(group_rows, local_heads * head_size)
        chunk_heads = local_heads // OUTPUT_CHUNKS
        pieces = []
        for c in range(OUTPUT_CHUNKS):
            results = attend_full(
                meta, queries, everything[0], everything[1], local_heads, group_sharing_factor,
                c * chunk_heads, chunk_heads,
            )
            merged = results.reshape(head_groups, tok_rows, chunk_heads * head_size)
            pieces.append(lax.all_to_all(merged, heads_axes, split_axis=0, concat_axis=0, tiled=True))
        returned = jnp.stack(pieces, 1)
        return returned.transpose(2, 0, 1, 3).reshape(tok_rows, head_groups * local_heads * head_size)
    key_before, value_before = passed_along(
        (key_local[group_rows - back * block_size:], value_local[group_rows - back * block_size:]),
        "outer", 1,
    )
    key_window = jnp.concatenate([key_before, key_local], 0)
    value_window = jnp.concatenate([value_before, value_local], 0)
    kv_index = jnp.arange(local_heads, dtype=jnp.int32) // group_sharing_factor
    owner_seq = head_verts // group_blocks
    local_block = head_verts % group_blocks
    key_blocks = key_local.reshape(group_blocks, block_size, local_kv, head_size)
    value_blocks = value_local.reshape(group_blocks, block_size, local_kv, head_size)
    picked_keys = key_blocks[local_block, :, kv_index[:, None], :]
    picked_values = value_blocks[local_block, :, kv_index[:, None], :]
    owned = (owner_seq == seq_index)[:, :, None, None]
    nothing = jnp.zeros((), picked_keys.dtype)
    mine = jnp.stack(
        [jnp.where(owned, picked_keys, nothing), jnp.where(owned, picked_values, nothing)]
    ).reshape(2, seq_count, -1, head_size).transpose(1, 0, 2, 3)
    part = lax.all_to_all(mine, "outer", split_axis=0, concat_axis=0, tiled=True).sum(
        0, dtype=picked_keys.dtype
    )
    spread = jnp.broadcast_to(part[None], (seq_count,) + part.shape)
    gathered = lax.all_to_all(spread, "outer", split_axis=0, concat_axis=0, tiled=True)
    vert = gathered.transpose(1, 0, 2, 3).reshape(2, local_heads, -1, head_size)
    queries = query_group.reshape(group_rows, local_heads * head_size)
    results = attend(
        meta, queries, key_window, value_window, vert[0], vert[1],
        local_heads, group_sharing_factor, 0,
    )
    merged = results.reshape(head_groups, tok_rows, local_heads * head_size)
    returned = lax.all_to_all(merged, heads_axes, split_axis=0, concat_axis=0, tiled=True)
    return returned.transpose(1, 0, 2).reshape(tok_rows, head_groups * local_heads * head_size)


def solution(mesh):
    seq_count = mesh.shape["seq"]
    inner = 2 if seq_count % 2 == 0 else 1
    work_mesh = Mesh(
        mesh.devices.reshape(seq_count // inner, inner, mesh.shape["grp"]), ("outer", "inner", "grp")
    )
    rows = P(("outer", "inner", "grp"), None)
    return jax.shard_map(
        per_device,
        mesh=work_mesh,
        in_specs=(rows, rows, rows, P(), P()),
        out_specs=rows,
        check_vma=False,
    )
```

```python
import jax
import jax.numpy as jnp
from jax import lax
from jax.experimental import pallas as pl
from jax.experimental.pallas import tpu as pltpu
from jax.sharding import Mesh, PartitionSpec as P

HEAD_DIMENSION = 128
MASK_BLOCK_SIZE = 64
SLASH_COUNT = 3
VERT_COUNT = 3
SLASH_REACH = 8
FULL_GATHER_BYTES = 4 << 20


def passed_along(shard, axis, by):
    length = lax.axis_size(axis)
    pairs = [(i, i + by) for i in range(length) if 0 <= i + by < length]
    return lax.ppermute(shard, axis, pairs)


def attention_kernel(local_heads, group_blocks, back, base):
    block = MASK_BLOCK_SIZE
    key_count = (SLASH_COUNT + VERT_COUNT) * block
    scale = HEAD_DIMENSION ** (-0.5)

    def kernel(meta_ref, q_ref, k_ref, v_ref, vk_ref, vv_ref, o_ref):
        h = pl.program_id(0) + base
        first = meta_ref[2 * local_heads * SLASH_COUNT]
        offs = [meta_ref[h * SLASH_COUNT + j] for j in range(SLASH_COUNT)]
        verts = [meta_ref[local_heads * SLASH_COUNT + h * VERT_COUNT + j] for j in range(VERT_COUNT)]
        vert_keys = vk_ref[0]
        vert_values = vv_ref[0]
        col = lax.broadcasted_iota(jnp.int32, (block, key_count), 1)
        row = lax.broadcasted_iota(jnp.int32, (block, key_count), 0)
        reach = col % block - row
        lane = lax.broadcasted_iota(jnp.int32, (1, key_count), 1) // block
        never = jnp.int32(-4 * block)
        for b in range(group_blocks):
            qb = first + b
            q = q_ref[pl.ds(b * block, block), :]
            starts = [pl.multiple_of((back + b - offs[j]) * block, block) for j in range(SLASH_COUNT)]
            keys = jnp.concatenate([k_ref[pl.ds(s, block), :] for s in starts] + [vert_keys], 0)
            values = jnp.concatenate([v_ref[pl.ds(s, block), :] for s in starts] + [vert_values], 0)
            limits = [jnp.where(qb - offs[j] >= 0, offs[j] * block, never) for j in range(SLASH_COUNT)]
            for v in verts:
                ok = v <= qb
                for o in offs:
                    ok = jnp.logical_and(ok, qb - v != o)
                limits.append(jnp.where(ok, (qb - v) * block, never))
            limit = jnp.full((1, key_count), limits[-1], jnp.int32)
            for i in range(len(limits) - 2, -1, -1):
                limit = jnp.where(lane == i, limits[i], limit)
            allowed = reach <= limit
            scores = lax.dot_general(
                q, keys, (((1,), (1,)), ((), ())), preferred_element_type=jnp.float32
            ) * scale
            masked = jnp.where(allowed, scores, -1e30)
            top = jnp.max(masked, axis=1, keepdims=True)
            weight = jnp.exp(masked - top)
            total = jnp.sum(weight, axis=1, keepdims=True)
            rounded = weight.astype(jnp.bfloat16)
            acc = jnp.dot(rounded, values, preferred_element_type=jnp.float32)
            o_ref[pl.ds(b * block, block), :] = (acc / total).astype(o_ref.dtype)

    return kernel


def full_kernel(local_heads, group_blocks):
    block = MASK_BLOCK_SIZE
    key_count = (SLASH_COUNT + VERT_COUNT) * block
    scale = HEAD_DIMENSION ** (-0.5)

    def kernel(meta_ref, q_ref, k_ref, v_ref, o_ref):
        h = pl.program_id(0)
        first = meta_ref[2 * local_heads * SLASH_COUNT]
        offs = [meta_ref[h * SLASH_COUNT + j] for j in range(SLASH_COUNT)]
        verts = [meta_ref[local_heads * SLASH_COUNT + h * VERT_COUNT + j] for j in range(VERT_COUNT)]
        vert_starts = [pl.multiple_of(v * block, block) for v in verts]
        vert_keys = [k_ref[pl.ds(s, block), :] for s in vert_starts]
        vert_values = [v_ref[pl.ds(s, block), :] for s in vert_starts]
        col = lax.broadcasted_iota(jnp.int32, (block, key_count), 1)
        row = lax.broadcasted_iota(jnp.int32, (block, key_count), 0)
        reach = col % block - row
        lane = lax.broadcasted_iota(jnp.int32, (1, key_count), 1) // block
        never = jnp.int32(-4 * block)
        for b in range(group_blocks):
            qb = first + b
            q = q_ref[pl.ds(b * block, block), :]
            starts = [pl.multiple_of(jnp.maximum(qb - offs[j], 0) * block, block) for j in range(SLASH_COUNT)]
            keys = jnp.concatenate([k_ref[pl.ds(s, block), :] for s in starts] + vert_keys, 0)
            values = jnp.concatenate([v_ref[pl.ds(s, block), :] for s in starts] + vert_values, 0)
            limits = [jnp.where(qb - offs[j] >= 0, offs[j] * block, never) for j in range(SLASH_COUNT)]
            for v in verts:
                ok = v <= qb
                for o in offs:
                    ok = jnp.logical_and(ok, qb - v != o)
                limits.append(jnp.where(ok, (qb - v) * block, never))
            limit = jnp.full((1, key_count), limits[-1], jnp.int32)
            for i in range(len(limits) - 2, -1, -1):
                limit = jnp.where(lane == i, limits[i], limit)
            allowed = reach <= limit
            scores = lax.dot_general(
                q, keys, (((1,), (1,)), ((), ())), preferred_element_type=jnp.float32
            ) * scale
            masked = jnp.where(allowed, scores, -1e30)
            top = jnp.max(masked, axis=1, keepdims=True)
            weight = jnp.exp(masked - top)
            total = jnp.sum(weight, axis=1, keepdims=True)
            rounded = weight.astype(jnp.bfloat16)
            acc = jnp.dot(rounded, values, preferred_element_type=jnp.float32)
            o_ref[pl.ds(b * block, block), :] = (acc / total).astype(o_ref.dtype)

    return kernel


def attend_full(meta, queries, all_keys, all_values, local_heads, sharing):
    group_rows = queries.shape[0]
    group_blocks = group_rows // MASK_BLOCK_SIZE
    head_size = HEAD_DIMENSION
    total_rows = all_keys.shape[0]
    grid_spec = pltpu.PrefetchScalarGridSpec(
        num_scalar_prefetch=1,
        grid=(local_heads,),
        in_specs=[
            pl.BlockSpec((group_rows, head_size), lambda h, m: (0, h)),
            pl.BlockSpec((total_rows, head_size), lambda h, m: (0, h // sharing)),
            pl.BlockSpec((total_rows, head_size), lambda h, m: (0, h // sharing)),
        ],
        out_specs=pl.BlockSpec((group_rows, head_size), lambda h, m: (0, h)),
    )
    return pl.pallas_call(
        full_kernel(local_heads, group_blocks),
        grid_spec=grid_spec,
        out_shape=jax.ShapeDtypeStruct((group_rows, local_heads * head_size), queries.dtype),
    )(meta, queries, all_keys, all_values)


def attend(meta, queries, key_window, value_window, vert_keys, vert_values, local_heads, sharing, base):
    group_rows = queries.shape[0]
    group_blocks = group_rows // MASK_BLOCK_SIZE
    head_size = HEAD_DIMENSION
    window_rows = key_window.shape[0]
    chunk_heads, vert_rows = vert_keys.shape[:2]
    grid_spec = pltpu.PrefetchScalarGridSpec(
        num_scalar_prefetch=1,
        grid=(chunk_heads,),
        in_specs=[
            pl.BlockSpec((group_rows, head_size), lambda h, m: (0, h + base)),
            pl.BlockSpec((window_rows, head_size), lambda h, m: (0, (h + base) // sharing)),
            pl.BlockSpec((window_rows, head_size), lambda h, m: (0, (h + base) // sharing)),
            pl.BlockSpec((1, vert_rows, head_size), lambda h, m: (h, 0, 0)),
            pl.BlockSpec((1, vert_rows, head_size), lambda h, m: (h, 0, 0)),
        ],
        out_specs=pl.BlockSpec((group_rows, head_size), lambda h, m: (0, h)),
    )
    return pl.pallas_call(
        attention_kernel(local_heads, group_blocks, window_rows // MASK_BLOCK_SIZE - group_blocks, base),
        grid_spec=grid_spec,
        out_shape=jax.ShapeDtypeStruct((group_rows, chunk_heads * head_size), queries.dtype),
    )(meta, queries, key_window, value_window, vert_keys, vert_values)


def per_device(query_rows, key_matrix, value_matrix, vertical, slash_offsets):
    tok_rows = query_rows.shape[0]
    heads_axes = ("inner", "grp")
    head_groups = lax.axis_size("inner") * lax.axis_size("grp")
    head_size = HEAD_DIMENSION
    block_size = MASK_BLOCK_SIZE
    local_heads = query_rows.shape[1] // (head_groups * head_size)
    local_kv = key_matrix.shape[1] // (head_groups * head_size)
    group_sharing_factor = local_heads // local_kv
    query_split = query_rows.reshape(tok_rows, head_groups, local_heads * head_size)
    key_split = key_matrix.reshape(tok_rows, head_groups, local_kv * head_size)
    value_split = value_matrix.reshape(tok_rows, head_groups, local_kv * head_size)
    seq_count = lax.axis_size("outer")
    kv_split = jnp.stack([key_split, value_split], 2)
    whole = seq_count * head_groups * kv_split.size * kv_split.dtype.itemsize // head_groups
    if whole <= FULL_GATHER_BYTES:
        spread = jnp.broadcast_to(
            kv_split.transpose(1, 0, 2, 3)[None], (seq_count,) + kv_split.transpose(1, 0, 2, 3).shape
        ).reshape((seq_count * head_groups,) + kv_split.transpose(1, 0, 2, 3).shape[1:])
        everything = lax.all_to_all(
            spread, ("outer",) + heads_axes, split_axis=0, concat_axis=0, tiled=True
        )
    else:
        kv_group = lax.all_to_all(kv_split, heads_axes, split_axis=1, concat_axis=0, tiled=True)
        key_group, value_group = kv_group[:, 0, 0], kv_group[:, 0, 1]
    me = lax.axis_index(heads_axes)
    received = [lax.dynamic_index_in_dim(query_split, me, 1, keepdims=False)]
    for shift in range(1, head_groups):
        sent = lax.dynamic_index_in_dim(query_split, (me + shift) % head_groups, 1, keepdims=False)
        received.append(
            lax.ppermute(sent, heads_axes, [(i, (i + shift) % head_groups) for i in range(head_groups)])
        )
    slab_shift = (me - jnp.arange(head_groups, dtype=jnp.int32)) % head_groups
    query_group = jnp.take(jnp.stack(received), slab_shift, axis=0)
    group_rows = tok_rows * head_groups
    group_blocks = group_rows // block_size
    back = min(SLASH_REACH, group_blocks)
    seq_index = lax.axis_index("outer")
    head_group = lax.axis_index(heads_axes)
    head_offsets = lax.dynamic_slice_in_dim(slash_offsets, head_group * local_heads, local_heads, 0)
    head_verts = lax.dynamic_slice_in_dim(vertical, head_group * local_heads, local_heads, 0)
    first_block = (seq_index * group_blocks).astype(jnp.int32)
    meta = jnp.concatenate(
        [
            head_offsets.reshape(-1).astype(jnp.int32),
            head_verts.reshape(-1).astype(jnp.int32),
            first_block[None],
        ]
    )
    if whole <= FULL_GATHER_BYTES:
        everything = everything.reshape(-1, 2, local_kv * head_size).transpose(1, 0, 2)
        queries = query_group.reshape(group_rows, local_heads * head_size)
        results = attend_full(
            meta, queries, everything[0], everything[1], local_heads, group_sharing_factor
        )
        merged = results.reshape(head_groups, tok_rows, local_heads * head_size)
        returned = lax.all_to_all(merged, heads_axes, split_axis=0, concat_axis=0, tiled=True)
        return returned.transpose(1, 0, 2).reshape(tok_rows, head_groups * local_heads * head_size)
    key_local = key_group.reshape(group_rows, local_kv * head_size)
    value_local = value_group.reshape(group_rows, local_kv * head_size)
    key_before, value_before = passed_along(
        (key_local[group_rows - back * block_size:], value_local[group_rows - back * block_size:]),
        "outer", 1,
    )
    key_window = jnp.concatenate([key_before, key_local], 0)
    value_window = jnp.concatenate([value_before, value_local], 0)
    kv_index = jnp.arange(local_heads, dtype=jnp.int32) // group_sharing_factor
    owner_seq = head_verts // group_blocks
    local_block = head_verts % group_blocks
    key_blocks = key_local.reshape(group_blocks, block_size, local_kv, head_size)
    value_blocks = value_local.reshape(group_blocks, block_size, local_kv, head_size)
    picked_keys = key_blocks[local_block, :, kv_index[:, None], :]
    picked_values = value_blocks[local_block, :, kv_index[:, None], :]
    owned = (owner_seq == seq_index)[:, :, None, None]
    nothing = jnp.zeros((), picked_keys.dtype)
    mine = jnp.stack(
        [jnp.where(owned, picked_keys, nothing), jnp.where(owned, picked_values, nothing)]
    ).reshape(2, seq_count, -1, head_size).transpose(1, 0, 2, 3)
    part = lax.all_to_all(mine, "outer", split_axis=0, concat_axis=0, tiled=True).sum(
        0, dtype=picked_keys.dtype
    )
    spread = jnp.broadcast_to(part[None], (seq_count,) + part.shape)
    gathered = lax.all_to_all(spread, "outer", split_axis=0, concat_axis=0, tiled=True)
    vert = gathered.transpose(1, 0, 2, 3).reshape(2, local_heads, -1, head_size)
    queries = query_group.reshape(group_rows, local_heads * head_size)
    results = attend(
        meta, queries, key_window, value_window, vert[0], vert[1],
        local_heads, group_sharing_factor, 0,
    )
    merged = results.reshape(head_groups, tok_rows, local_heads * head_size)
    returned = lax.all_to_all(merged, heads_axes, split_axis=0, concat_axis=0, tiled=True)
    return returned.transpose(1, 0, 2).reshape(tok_rows, head_groups * local_heads * head_size)


def solution(mesh):
    seq_count = mesh.shape["seq"]
    inner = 2 if seq_count % 2 == 0 else 1
    work_mesh = Mesh(
        mesh.devices.reshape(seq_count // inner, inner, mesh.shape["grp"]), ("outer", "inner", "grp")
    )
    rows = P(("outer", "inner", "grp"), None)
    return jax.shard_map(
        per_device,
        mesh=work_mesh,
        in_specs=(rows, rows, rows, P(), P()),
        out_specs=rows,
        check_vma=False,
    )
```

```python
import jax
import jax.numpy as jnp
from jax import lax
from jax.experimental import pallas as pl
from jax.experimental.pallas import tpu as pltpu
from jax.sharding import Mesh, PartitionSpec as P

HEAD_DIMENSION = 128
MASK_BLOCK_SIZE = 64
SLASH_COUNT = 3
VERT_COUNT = 3
SLASH_REACH = 8
FULL_GATHER_BYTES = 4 << 20


def passed_along(shard, axis, by):
    length = lax.axis_size(axis)
    pairs = [(i, i + by) for i in range(length) if 0 <= i + by < length]
    return lax.ppermute(shard, axis, pairs)


def attention_kernel(local_heads, group_blocks, back, base):
    block = MASK_BLOCK_SIZE
    key_count = (SLASH_COUNT + VERT_COUNT) * block
    scale = HEAD_DIMENSION ** (-0.5)

    def kernel(meta_ref, q_ref, k_ref, v_ref, vk_ref, vv_ref, o_ref):
        h = pl.program_id(0) + base
        first = meta_ref[2 * local_heads * SLASH_COUNT]
        offs = [meta_ref[h * SLASH_COUNT + j] for j in range(SLASH_COUNT)]
        verts = [meta_ref[local_heads * SLASH_COUNT + h * VERT_COUNT + j] for j in range(VERT_COUNT)]
        vert_keys = vk_ref[0]
        vert_values = vv_ref[0]
        col = lax.broadcasted_iota(jnp.int32, (block, key_count), 1)
        row = lax.broadcasted_iota(jnp.int32, (block, key_count), 0)
        reach = col % block - row
        lane = lax.broadcasted_iota(jnp.int32, (1, key_count), 1) // block
        never = jnp.int32(-4 * block)
        for b in range(group_blocks):
            qb = first + b
            q = q_ref[pl.ds(b * block, block), :]
            starts = [pl.multiple_of((back + b - offs[j]) * block, block) for j in range(SLASH_COUNT)]
            keys = jnp.concatenate([k_ref[pl.ds(s, block), :] for s in starts] + [vert_keys], 0)
            values = jnp.concatenate([v_ref[pl.ds(s, block), :] for s in starts] + [vert_values], 0)
            limits = [jnp.where(qb - offs[j] >= 0, offs[j] * block, never) for j in range(SLASH_COUNT)]
            for v in verts:
                ok = v <= qb
                for o in offs:
                    ok = jnp.logical_and(ok, qb - v != o)
                limits.append(jnp.where(ok, (qb - v) * block, never))
            limit = jnp.full((1, key_count), limits[-1], jnp.int32)
            for i in range(len(limits) - 2, -1, -1):
                limit = jnp.where(lane == i, limits[i], limit)
            allowed = reach <= limit
            scores = lax.dot_general(
                q, keys, (((1,), (1,)), ((), ())), preferred_element_type=jnp.float32
            ) * scale
            masked = jnp.where(allowed, scores, -1e30)
            top = jnp.max(masked, axis=1, keepdims=True)
            weight = jnp.exp(masked - top)
            total = jnp.sum(weight, axis=1, keepdims=True)
            rounded = weight.astype(jnp.bfloat16)
            acc = jnp.dot(rounded, values, preferred_element_type=jnp.float32)
            o_ref[pl.ds(b * block, block), :] = (acc / total).astype(o_ref.dtype)

    return kernel


def full_kernel(local_heads, group_blocks, slab_rows, slabs):
    block = MASK_BLOCK_SIZE
    key_count = (SLASH_COUNT + VERT_COUNT) * block
    scale = HEAD_DIMENSION ** (-0.5)

    def kernel(meta_ref, q_ref, k_ref, v_ref, o_ref):
        h = pl.program_id(0)
        first = meta_ref[2 * local_heads * SLASH_COUNT]
        me = meta_ref[2 * local_heads * SLASH_COUNT + 1]
        offs = [meta_ref[h * SLASH_COUNT + j] for j in range(SLASH_COUNT)]
        verts = [meta_ref[local_heads * SLASH_COUNT + h * VERT_COUNT + j] for j in range(VERT_COUNT)]
        vert_starts = [pl.multiple_of(v * block, block) for v in verts]
        vert_keys = [k_ref[pl.ds(s, block), :] for s in vert_starts]
        vert_values = [v_ref[pl.ds(s, block), :] for s in vert_starts]
        col = lax.broadcasted_iota(jnp.int32, (block, key_count), 1)
        row = lax.broadcasted_iota(jnp.int32, (block, key_count), 0)
        reach = col % block - row
        lane = lax.broadcasted_iota(jnp.int32, (1, key_count), 1) // block
        never = jnp.int32(-4 * block)
        for b in range(group_blocks):
            qb = first + b
            slab_blocks = slab_rows // block
            slab = (me - b // slab_blocks + slabs) % slabs
            q = q_ref[pl.ds(pl.multiple_of(slab * slab_rows + (b % slab_blocks) * block, block), block), :]
            starts = [pl.multiple_of(jnp.maximum(qb - offs[j], 0) * block, block) for j in range(SLASH_COUNT)]
            keys = jnp.concatenate([k_ref[pl.ds(s, block), :] for s in starts] + vert_keys, 0)
            values = jnp.concatenate([v_ref[pl.ds(s, block), :] for s in starts] + vert_values, 0)
            limits = [jnp.where(qb - offs[j] >= 0, offs[j] * block, never) for j in range(SLASH_COUNT)]
            for v in verts:
                ok = v <= qb
                for o in offs:
                    ok = jnp.logical_and(ok, qb - v != o)
                limits.append(jnp.where(ok, (qb - v) * block, never))
            limit = jnp.full((1, key_count), limits[-1], jnp.int32)
            for i in range(len(limits) - 2, -1, -1):
                limit = jnp.where(lane == i, limits[i], limit)
            allowed = reach <= limit
            scores = lax.dot_general(
                q, keys, (((1,), (1,)), ((), ())), preferred_element_type=jnp.float32
            ) * scale
            masked = jnp.where(allowed, scores, -1e30)
            top = jnp.max(masked, axis=1, keepdims=True)
            weight = jnp.exp(masked - top)
            total = jnp.sum(weight, axis=1, keepdims=True)
            rounded = weight.astype(jnp.bfloat16)
            acc = jnp.dot(rounded, values, preferred_element_type=jnp.float32)
            o_ref[pl.ds(b * block, block), :] = (acc / total).astype(o_ref.dtype)

    return kernel


def attend_full(meta, queries, all_kv, local_heads, sharing, slab_rows):
    group_rows = queries.shape[0]
    group_blocks = group_rows // MASK_BLOCK_SIZE
    head_size = HEAD_DIMENSION
    total_rows = all_kv.shape[0]
    value_base = all_kv.shape[1] // (2 * head_size)
    grid_spec = pltpu.PrefetchScalarGridSpec(
        num_scalar_prefetch=1,
        grid=(local_heads,),
        in_specs=[
            pl.BlockSpec((group_rows, head_size), lambda h, m: (0, h)),
            pl.BlockSpec((total_rows, head_size), lambda h, m: (0, h // sharing)),
            pl.BlockSpec((total_rows, head_size), lambda h, m: (0, value_base + h // sharing)),
        ],
        out_specs=pl.BlockSpec((group_rows, head_size), lambda h, m: (0, h)),
    )
    return pl.pallas_call(
        full_kernel(local_heads, group_blocks, slab_rows, group_rows // slab_rows),
        grid_spec=grid_spec,
        out_shape=jax.ShapeDtypeStruct((group_rows, local_heads * head_size), queries.dtype),
    )(meta, queries, all_kv, all_kv)


def attend(meta, queries, key_window, value_window, vert_keys, vert_values, local_heads, sharing, base):
    group_rows = queries.shape[0]
    group_blocks = group_rows // MASK_BLOCK_SIZE
    head_size = HEAD_DIMENSION
    window_rows = key_window.shape[0]
    chunk_heads, vert_rows = vert_keys.shape[:2]
    grid_spec = pltpu.PrefetchScalarGridSpec(
        num_scalar_prefetch=1,
        grid=(chunk_heads,),
        in_specs=[
            pl.BlockSpec((group_rows, head_size), lambda h, m: (0, h + base)),
            pl.BlockSpec((window_rows, head_size), lambda h, m: (0, (h + base) // sharing)),
            pl.BlockSpec((window_rows, head_size), lambda h, m: (0, (h + base) // sharing)),
            pl.BlockSpec((1, vert_rows, head_size), lambda h, m: (h, 0, 0)),
            pl.BlockSpec((1, vert_rows, head_size), lambda h, m: (h, 0, 0)),
        ],
        out_specs=pl.BlockSpec((group_rows, head_size), lambda h, m: (0, h)),
    )
    return pl.pallas_call(
        attention_kernel(local_heads, group_blocks, window_rows // MASK_BLOCK_SIZE - group_blocks, base),
        grid_spec=grid_spec,
        out_shape=jax.ShapeDtypeStruct((group_rows, chunk_heads * head_size), queries.dtype),
    )(meta, queries, key_window, value_window, vert_keys, vert_values)


def per_device(query_rows, key_matrix, value_matrix, vertical, slash_offsets):
    tok_rows = query_rows.shape[0]
    heads_axes = ("inner", "grp")
    head_groups = lax.axis_size("inner") * lax.axis_size("grp")
    head_size = HEAD_DIMENSION
    block_size = MASK_BLOCK_SIZE
    local_heads = query_rows.shape[1] // (head_groups * head_size)
    local_kv = key_matrix.shape[1] // (head_groups * head_size)
    group_sharing_factor = local_heads // local_kv
    query_split = query_rows.reshape(tok_rows, head_groups, local_heads * head_size)
    key_split = key_matrix.reshape(tok_rows, head_groups, local_kv * head_size)
    value_split = value_matrix.reshape(tok_rows, head_groups, local_kv * head_size)
    seq_count = lax.axis_size("outer")
    kv_split = jnp.stack([key_split, value_split], 2)
    whole = seq_count * head_groups * kv_split.size * kv_split.dtype.itemsize // head_groups
    if whole <= FULL_GATHER_BYTES:
        spread = jnp.broadcast_to(
            kv_split.transpose(1, 0, 2, 3)[None], (seq_count,) + kv_split.transpose(1, 0, 2, 3).shape
        ).reshape((seq_count * head_groups,) + kv_split.transpose(1, 0, 2, 3).shape[1:])
        everything = lax.all_to_all(
            spread, ("outer",) + heads_axes, split_axis=0, concat_axis=0, tiled=True
        )
    else:
        kv_group = lax.all_to_all(kv_split, heads_axes, split_axis=1, concat_axis=0, tiled=True)
        key_group, value_group = kv_group[:, 0, 0], kv_group[:, 0, 1]
    me = lax.axis_index(heads_axes)
    received = [lax.dynamic_index_in_dim(query_split, me, 1, keepdims=False)]
    for shift in range(1, head_groups):
        sent = lax.dynamic_index_in_dim(query_split, (me + shift) % head_groups, 1, keepdims=False)
        received.append(
            lax.ppermute(sent, heads_axes, [(i, (i + shift) % head_groups) for i in range(head_groups)])
        )
    received = jnp.stack(received)
    group_rows = tok_rows * head_groups
    group_blocks = group_rows // block_size
    back = min(SLASH_REACH, group_blocks)
    seq_index = lax.axis_index("outer")
    head_group = lax.axis_index(heads_axes)
    head_offsets = lax.dynamic_slice_in_dim(slash_offsets, head_group * local_heads, local_heads, 0)
    head_verts = lax.dynamic_slice_in_dim(vertical, head_group * local_heads, local_heads, 0)
    first_block = (seq_index * group_blocks).astype(jnp.int32)
    meta = jnp.concatenate(
        [
            head_offsets.reshape(-1).astype(jnp.int32),
            head_verts.reshape(-1).astype(jnp.int32),
            first_block[None],
        ]
    )
    if whole <= FULL_GATHER_BYTES:
        everything = everything.reshape(-1, 2 * local_kv * head_size)
        queries = received.reshape(group_rows, local_heads * head_size)
        results = attend_full(
            jnp.concatenate([meta, me.astype(jnp.int32)[None]]), queries, everything,
            local_heads, group_sharing_factor, tok_rows,
        )
        merged = results.reshape(head_groups, tok_rows, local_heads * head_size)
        returned = lax.all_to_all(merged, heads_axes, split_axis=0, concat_axis=0, tiled=True)
        return returned.transpose(1, 0, 2).reshape(tok_rows, head_groups * local_heads * head_size)
    slab_shift = (me - jnp.arange(head_groups, dtype=jnp.int32)) % head_groups
    query_group = jnp.take(received, slab_shift, axis=0)
    key_local = key_group.reshape(group_rows, local_kv * head_size)
    value_local = value_group.reshape(group_rows, local_kv * head_size)
    key_before, value_before = passed_along(
        (key_local[group_rows - back * block_size:], value_local[group_rows - back * block_size:]),
        "outer", 1,
    )
    key_window = jnp.concatenate([key_before, key_local], 0)
    value_window = jnp.concatenate([value_before, value_local], 0)
    kv_index = jnp.arange(local_heads, dtype=jnp.int32) // group_sharing_factor
    owner_seq = head_verts // group_blocks
    local_block = head_verts % group_blocks
    key_blocks = key_local.reshape(group_blocks, block_size, local_kv, head_size)
    value_blocks = value_local.reshape(group_blocks, block_size, local_kv, head_size)
    picked_keys = key_blocks[local_block, :, kv_index[:, None], :]
    picked_values = value_blocks[local_block, :, kv_index[:, None], :]
    owned = (owner_seq == seq_index)[:, :, None, None]
    nothing = jnp.zeros((), picked_keys.dtype)
    mine = jnp.stack(
        [jnp.where(owned, picked_keys, nothing), jnp.where(owned, picked_values, nothing)]
    ).reshape(2, seq_count, -1, head_size).transpose(1, 0, 2, 3)
    part = lax.all_to_all(mine, "outer", split_axis=0, concat_axis=0, tiled=True).sum(
        0, dtype=picked_keys.dtype
    )
    spread = jnp.broadcast_to(part[None], (seq_count,) + part.shape)
    gathered = lax.all_to_all(spread, "outer", split_axis=0, concat_axis=0, tiled=True)
    vert = gathered.transpose(1, 0, 2, 3).reshape(2, local_heads, -1, head_size)
    queries = query_group.reshape(group_rows, local_heads * head_size)
    results = attend(
        meta, queries, key_window, value_window, vert[0], vert[1],
        local_heads, group_sharing_factor, 0,
    )
    merged = results.reshape(head_groups, tok_rows, local_heads * head_size)
    returned = lax.all_to_all(merged, heads_axes, split_axis=0, concat_axis=0, tiled=True)
    return returned.transpose(1, 0, 2).reshape(tok_rows, head_groups * local_heads * head_size)


def solution(mesh):
    seq_count = mesh.shape["seq"]
    inner = 2 if seq_count % 2 == 0 else 1
    work_mesh = Mesh(
        mesh.devices.reshape(seq_count // inner, inner, mesh.shape["grp"]), ("outer", "inner", "grp")
    )
    rows = P(("outer", "inner", "grp"), None)
    return jax.shard_map(
        per_device,
        mesh=work_mesh,
        in_specs=(rows, rows, rows, P(), P()),
        out_specs=rows,
        check_vma=False,
    )
```

```python
import jax
import jax.numpy as jnp
from jax import lax
from jax.experimental import pallas as pl
from jax.experimental.pallas import tpu as pltpu
from jax.sharding import Mesh, PartitionSpec as P

HEAD_DIMENSION = 128
MASK_BLOCK_SIZE = 64
SLASH_COUNT = 3
VERT_COUNT = 3
SLASH_REACH = 8
FULL_GATHER_BYTES = 4 << 20


def passed_along(shard, axis, by):
    length = lax.axis_size(axis)
    pairs = [(i, i + by) for i in range(length) if 0 <= i + by < length]
    return lax.ppermute(shard, axis, pairs)


def attention_kernel(local_heads, group_blocks, back, base):
    block = MASK_BLOCK_SIZE
    key_count = (SLASH_COUNT + VERT_COUNT) * block
    scale = HEAD_DIMENSION ** (-0.5)

    def kernel(meta_ref, q_ref, k_ref, v_ref, vk_ref, vv_ref, o_ref):
        h = pl.program_id(0) + base
        first = meta_ref[2 * local_heads * SLASH_COUNT]
        offs = [meta_ref[h * SLASH_COUNT + j] for j in range(SLASH_COUNT)]
        verts = [meta_ref[local_heads * SLASH_COUNT + h * VERT_COUNT + j] for j in range(VERT_COUNT)]
        vert_keys = vk_ref[0]
        vert_values = vv_ref[0]
        col = lax.broadcasted_iota(jnp.int32, (block, key_count), 1)
        row = lax.broadcasted_iota(jnp.int32, (block, key_count), 0)
        reach = col % block - row
        lane = lax.broadcasted_iota(jnp.int32, (1, key_count), 1) // block
        never = jnp.int32(-4 * block)
        for b in range(group_blocks):
            qb = first + b
            q = q_ref[pl.ds(b * block, block), :]
            starts = [pl.multiple_of((back + b - offs[j]) * block, block) for j in range(SLASH_COUNT)]
            keys = jnp.concatenate([k_ref[pl.ds(s, block), :] for s in starts] + [vert_keys], 0)
            values = jnp.concatenate([v_ref[pl.ds(s, block), :] for s in starts] + [vert_values], 0)
            limits = [jnp.where(qb - offs[j] >= 0, offs[j] * block, never) for j in range(SLASH_COUNT)]
            for v in verts:
                ok = v <= qb
                for o in offs:
                    ok = jnp.logical_and(ok, qb - v != o)
                limits.append(jnp.where(ok, (qb - v) * block, never))
            limit = jnp.full((1, key_count), limits[-1], jnp.int32)
            for i in range(len(limits) - 2, -1, -1):
                limit = jnp.where(lane == i, limits[i], limit)
            allowed = reach <= limit
            scores = lax.dot_general(
                q, keys, (((1,), (1,)), ((), ())), preferred_element_type=jnp.float32
            ) * scale
            masked = jnp.where(allowed, scores, -1e30)
            top = jnp.max(masked, axis=1, keepdims=True)
            weight = jnp.exp(masked - top)
            total = jnp.sum(weight, axis=1, keepdims=True)
            rounded = weight.astype(jnp.bfloat16)
            acc = jnp.dot(rounded, values, preferred_element_type=jnp.float32)
            o_ref[pl.ds(b * block, block), :] = (acc / total).astype(o_ref.dtype)

    return kernel


def full_kernel(local_heads, group_blocks, slab_rows, slabs):
    block = MASK_BLOCK_SIZE
    key_count = (SLASH_COUNT + VERT_COUNT) * block
    scale = HEAD_DIMENSION ** (-0.5)

    def kernel(meta_ref, q_ref, k_ref, v_ref, o_ref):
        h = pl.program_id(0)
        first = meta_ref[2 * local_heads * SLASH_COUNT]
        me = meta_ref[2 * local_heads * SLASH_COUNT + 1]
        offs = [meta_ref[h * SLASH_COUNT + j] for j in range(SLASH_COUNT)]
        verts = [meta_ref[local_heads * SLASH_COUNT + h * VERT_COUNT + j] for j in range(VERT_COUNT)]
        vert_starts = [pl.multiple_of(v * block, block) for v in verts]
        vert_keys = [k_ref[pl.ds(s, block), :] for s in vert_starts]
        vert_values = [v_ref[pl.ds(s, block), :] for s in vert_starts]
        col = lax.broadcasted_iota(jnp.int32, (block, key_count), 1)
        row = lax.broadcasted_iota(jnp.int32, (block, key_count), 0)
        reach = col % block - row
        lane = lax.broadcasted_iota(jnp.int32, (1, key_count), 1) // block
        never = jnp.int32(-4 * block)
        for b in range(group_blocks):
            qb = first + b
            slab_blocks = slab_rows // block
            slab = (me - b // slab_blocks + slabs) % slabs
            q = q_ref[pl.ds(pl.multiple_of(slab * slab_rows + (b % slab_blocks) * block, block), block), :]
            starts = [pl.multiple_of(jnp.maximum(qb - offs[j], 0) * block, block) for j in range(SLASH_COUNT)]
            keys = jnp.concatenate([k_ref[pl.ds(s, block), :] for s in starts] + vert_keys, 0)
            values = jnp.concatenate([v_ref[pl.ds(s, block), :] for s in starts] + vert_values, 0)
            limits = [jnp.where(qb - offs[j] >= 0, offs[j] * block, never) for j in range(SLASH_COUNT)]
            for v in verts:
                ok = v <= qb
                for o in offs:
                    ok = jnp.logical_and(ok, qb - v != o)
                limits.append(jnp.where(ok, (qb - v) * block, never))
            limit = jnp.full((1, key_count), limits[-1], jnp.int32)
            for i in range(len(limits) - 2, -1, -1):
                limit = jnp.where(lane == i, limits[i], limit)
            allowed = reach <= limit
            scores = lax.dot_general(
                q, keys, (((1,), (1,)), ((), ())), preferred_element_type=jnp.float32
            ) * scale
            masked = jnp.where(allowed, scores, -1e30)
            top = jnp.max(masked, axis=1, keepdims=True)
            weight = jnp.exp(masked - top)
            total = jnp.sum(weight, axis=1, keepdims=True)
            rounded = weight.astype(jnp.bfloat16)
            acc = jnp.dot(rounded, values, preferred_element_type=jnp.float32)
            o_ref[pl.ds(b * block, block), :] = (acc / total).astype(o_ref.dtype)

    return kernel


def attend_full(meta, queries, all_kv, local_heads, sharing, slab_rows):
    group_rows = queries.shape[0]
    group_blocks = group_rows // MASK_BLOCK_SIZE
    head_size = HEAD_DIMENSION
    total_rows = all_kv.shape[0]
    value_base = all_kv.shape[1] // (2 * head_size)
    grid_spec = pltpu.PrefetchScalarGridSpec(
        num_scalar_prefetch=1,
        grid=(local_heads,),
        in_specs=[
            pl.BlockSpec((group_rows, head_size), lambda h, m: (0, h)),
            pl.BlockSpec((total_rows, head_size), lambda h, m: (0, h // sharing)),
            pl.BlockSpec((total_rows, head_size), lambda h, m: (0, value_base + h // sharing)),
        ],
        out_specs=pl.BlockSpec((group_rows, head_size), lambda h, m: (0, h)),
    )
    return pl.pallas_call(
        full_kernel(local_heads, group_blocks, slab_rows, group_rows // slab_rows),
        grid_spec=grid_spec,
        out_shape=jax.ShapeDtypeStruct((group_rows, local_heads * head_size), queries.dtype),
    )(meta, queries, all_kv, all_kv)


def attend(meta, queries, key_window, value_window, vert_keys, vert_values, local_heads, sharing, base):
    group_rows = queries.shape[0]
    group_blocks = group_rows // MASK_BLOCK_SIZE
    head_size = HEAD_DIMENSION
    window_rows = key_window.shape[0]
    chunk_heads, vert_rows = vert_keys.shape[:2]
    grid_spec = pltpu.PrefetchScalarGridSpec(
        num_scalar_prefetch=1,
        grid=(chunk_heads,),
        in_specs=[
            pl.BlockSpec((group_rows, head_size), lambda h, m: (0, h + base)),
            pl.BlockSpec((window_rows, head_size), lambda h, m: (0, (h + base) // sharing)),
            pl.BlockSpec((window_rows, head_size), lambda h, m: (0, (h + base) // sharing)),
            pl.BlockSpec((1, vert_rows, head_size), lambda h, m: (h, 0, 0)),
            pl.BlockSpec((1, vert_rows, head_size), lambda h, m: (h, 0, 0)),
        ],
        out_specs=pl.BlockSpec((group_rows, head_size), lambda h, m: (0, h)),
    )
    return pl.pallas_call(
        attention_kernel(local_heads, group_blocks, window_rows // MASK_BLOCK_SIZE - group_blocks, base),
        grid_spec=grid_spec,
        out_shape=jax.ShapeDtypeStruct((group_rows, chunk_heads * head_size), queries.dtype),
    )(meta, queries, key_window, value_window, vert_keys, vert_values)


def per_device(query_rows, key_matrix, value_matrix, vertical, slash_offsets):
    tok_rows = query_rows.shape[0]
    heads_axes = ("inner", "grp")
    head_groups = lax.axis_size("inner") * lax.axis_size("grp")
    head_size = HEAD_DIMENSION
    block_size = MASK_BLOCK_SIZE
    local_heads = query_rows.shape[1] // (head_groups * head_size)
    local_kv = key_matrix.shape[1] // (head_groups * head_size)
    group_sharing_factor = local_heads // local_kv
    query_split = query_rows.reshape(tok_rows, head_groups, local_heads * head_size)
    key_split = key_matrix.reshape(tok_rows, head_groups, local_kv * head_size)
    value_split = value_matrix.reshape(tok_rows, head_groups, local_kv * head_size)
    seq_count = lax.axis_size("outer")
    whole = seq_count * (key_split.size + value_split.size) * key_split.dtype.itemsize
    if whole <= FULL_GATHER_BYTES:
        kv_rows = jnp.concatenate([key_split, value_split], 2).transpose(1, 0, 2)
        spread = jnp.broadcast_to(kv_rows[None], (seq_count,) + kv_rows.shape).reshape(
            (seq_count * head_groups,) + kv_rows.shape[1:]
        )
        everything = lax.all_to_all(
            spread, ("outer",) + heads_axes, split_axis=0, concat_axis=0, tiled=True
        )
    else:
        kv_split = jnp.stack([key_split, value_split], 2)
        kv_group = lax.all_to_all(kv_split, heads_axes, split_axis=1, concat_axis=0, tiled=True)
        key_group, value_group = kv_group[:, 0, 0], kv_group[:, 0, 1]
    me = lax.axis_index(heads_axes)
    received = [lax.dynamic_index_in_dim(query_split, me, 1, keepdims=False)]
    for shift in range(1, head_groups):
        sent = lax.dynamic_index_in_dim(query_split, (me + shift) % head_groups, 1, keepdims=False)
        received.append(
            lax.ppermute(sent, heads_axes, [(i, (i + shift) % head_groups) for i in range(head_groups)])
        )
    received = jnp.stack(received)
    group_rows = tok_rows * head_groups
    group_blocks = group_rows // block_size
    back = min(SLASH_REACH, group_blocks)
    seq_index = lax.axis_index("outer")
    head_group = lax.axis_index(heads_axes)
    head_offsets = lax.dynamic_slice_in_dim(slash_offsets, head_group * local_heads, local_heads, 0)
    head_verts = lax.dynamic_slice_in_dim(vertical, head_group * local_heads, local_heads, 0)
    first_block = (seq_index * group_blocks).astype(jnp.int32)
    meta = jnp.concatenate(
        [
            head_offsets.reshape(-1).astype(jnp.int32),
            head_verts.reshape(-1).astype(jnp.int32),
            first_block[None],
        ]
    )
    if whole <= FULL_GATHER_BYTES:
        everything = everything.reshape(-1, 2 * local_kv * head_size)
        queries = received.reshape(group_rows, local_heads * head_size)
        results = attend_full(
            jnp.concatenate([meta, me.astype(jnp.int32)[None]]), queries, everything,
            local_heads, group_sharing_factor, tok_rows,
        )
        merged = results.reshape(head_groups, tok_rows, local_heads * head_size)
        returned = lax.all_to_all(merged, heads_axes, split_axis=0, concat_axis=0, tiled=True)
        return returned.transpose(1, 0, 2).reshape(tok_rows, head_groups * local_heads * head_size)
    slab_shift = (me - jnp.arange(head_groups, dtype=jnp.int32)) % head_groups
    query_group = jnp.take(received, slab_shift, axis=0)
    key_local = key_group.reshape(group_rows, local_kv * head_size)
    value_local = value_group.reshape(group_rows, local_kv * head_size)
    key_before, value_before = passed_along(
        (key_local[group_rows - back * block_size:], value_local[group_rows - back * block_size:]),
        "outer", 1,
    )
    key_window = jnp.concatenate([key_before, key_local], 0)
    value_window = jnp.concatenate([value_before, value_local], 0)
    kv_index = jnp.arange(local_heads, dtype=jnp.int32) // group_sharing_factor
    owner_seq = head_verts // group_blocks
    local_block = head_verts % group_blocks
    key_blocks = key_local.reshape(group_blocks, block_size, local_kv, head_size)
    value_blocks = value_local.reshape(group_blocks, block_size, local_kv, head_size)
    picked_keys = key_blocks[local_block, :, kv_index[:, None], :]
    picked_values = value_blocks[local_block, :, kv_index[:, None], :]
    owned = (owner_seq == seq_index)[:, :, None, None]
    nothing = jnp.zeros((), picked_keys.dtype)
    mine = jnp.stack(
        [jnp.where(owned, picked_keys, nothing), jnp.where(owned, picked_values, nothing)]
    ).reshape(2, seq_count, -1, head_size).transpose(1, 0, 2, 3)
    part = lax.all_to_all(mine, "outer", split_axis=0, concat_axis=0, tiled=True).sum(
        0, dtype=picked_keys.dtype
    )
    spread = jnp.broadcast_to(part[None], (seq_count,) + part.shape)
    gathered = lax.all_to_all(spread, "outer", split_axis=0, concat_axis=0, tiled=True)
    vert = gathered.transpose(1, 0, 2, 3).reshape(2, local_heads, -1, head_size)
    queries = query_group.reshape(group_rows, local_heads * head_size)
    results = attend(
        meta, queries, key_window, value_window, vert[0], vert[1],
        local_heads, group_sharing_factor, 0,
    )
    merged = results.reshape(head_groups, tok_rows, local_heads * head_size)
    returned = lax.all_to_all(merged, heads_axes, split_axis=0, concat_axis=0, tiled=True)
    return returned.transpose(1, 0, 2).reshape(tok_rows, head_groups * local_heads * head_size)


def solution(mesh):
    seq_count = mesh.shape["seq"]
    inner = 2 if seq_count % 2 == 0 else 1
    work_mesh = Mesh(
        mesh.devices.reshape(seq_count // inner, inner, mesh.shape["grp"]), ("outer", "inner", "grp")
    )
    rows = P(("outer", "inner", "grp"), None)
    return jax.shard_map(
        per_device,
        mesh=work_mesh,
        in_specs=(rows, rows, rows, P(), P()),
        out_specs=rows,
        check_vma=False,
    )
```

```python
import jax
import jax.numpy as jnp
from jax import lax
from jax.experimental import pallas as pl
from jax.experimental.pallas import tpu as pltpu
from jax.sharding import Mesh, PartitionSpec as P

HEAD_DIMENSION = 128
MASK_BLOCK_SIZE = 64
SLASH_COUNT = 3
VERT_COUNT = 3
SLASH_REACH = 8
FULL_GATHER_BYTES = 4 << 20


def passed_along(shard, axis, by):
    length = lax.axis_size(axis)
    pairs = [(i, i + by) for i in range(length) if 0 <= i + by < length]
    return lax.ppermute(shard, axis, pairs)


def attention_kernel(local_heads, group_blocks, back, base):
    block = MASK_BLOCK_SIZE
    key_count = (SLASH_COUNT + VERT_COUNT) * block
    scale = HEAD_DIMENSION ** (-0.5)

    def kernel(meta_ref, q_ref, k_ref, v_ref, vk_ref, vv_ref, o_ref):
        h = pl.program_id(0) + base
        first = meta_ref[2 * local_heads * SLASH_COUNT]
        offs = [meta_ref[h * SLASH_COUNT + j] for j in range(SLASH_COUNT)]
        verts = [meta_ref[local_heads * SLASH_COUNT + h * VERT_COUNT + j] for j in range(VERT_COUNT)]
        vert_keys = vk_ref[0]
        vert_values = vv_ref[0]
        col = lax.broadcasted_iota(jnp.int32, (block, key_count), 1)
        row = lax.broadcasted_iota(jnp.int32, (block, key_count), 0)
        reach = col % block - row
        lane = lax.broadcasted_iota(jnp.int32, (1, key_count), 1) // block
        never = jnp.int32(-4 * block)
        for b in range(group_blocks):
            qb = first + b
            q = q_ref[pl.ds(b * block, block), :]
            starts = [pl.multiple_of((back + b - offs[j]) * block, block) for j in range(SLASH_COUNT)]
            keys = jnp.concatenate([k_ref[pl.ds(s, block), :] for s in starts] + [vert_keys], 0)
            values = jnp.concatenate([v_ref[pl.ds(s, block), :] for s in starts] + [vert_values], 0)
            limits = [jnp.where(qb - offs[j] >= 0, offs[j] * block, never) for j in range(SLASH_COUNT)]
            for v in verts:
                ok = v <= qb
                for o in offs:
                    ok = jnp.logical_and(ok, qb - v != o)
                limits.append(jnp.where(ok, (qb - v) * block, never))
            limit = jnp.full((1, key_count), limits[-1], jnp.int32)
            for i in range(len(limits) - 2, -1, -1):
                limit = jnp.where(lane == i, limits[i], limit)
            allowed = reach <= limit
            scores = lax.dot_general(
                q, keys, (((1,), (1,)), ((), ())), preferred_element_type=jnp.float32
            ) * scale
            masked = jnp.where(allowed, scores, -1e30)
            top = jnp.max(masked, axis=1, keepdims=True)
            weight = jnp.exp(masked - top)
            total = jnp.sum(weight, axis=1, keepdims=True)
            rounded = weight.astype(jnp.bfloat16)
            acc = jnp.dot(rounded, values, preferred_element_type=jnp.float32)
            o_ref[pl.ds(b * block, block), :] = (acc / total).astype(o_ref.dtype)

    return kernel


def full_kernel(local_heads, group_blocks, slab_rows, slabs):
    block = MASK_BLOCK_SIZE
    key_count = (SLASH_COUNT + VERT_COUNT) * block
    scale = HEAD_DIMENSION ** (-0.5)

    def kernel(meta_ref, q_ref, k_ref, v_ref, o_ref):
        h = pl.program_id(0)
        first = meta_ref[2 * local_heads * SLASH_COUNT]
        me = meta_ref[2 * local_heads * SLASH_COUNT + 1]
        offs = [meta_ref[h * SLASH_COUNT + j] for j in range(SLASH_COUNT)]
        verts = [meta_ref[local_heads * SLASH_COUNT + h * VERT_COUNT + j] for j in range(VERT_COUNT)]
        vert_starts = [pl.multiple_of(v * block, block) for v in verts]
        vert_keys = [k_ref[pl.ds(s, block), :] for s in vert_starts]
        vert_values = [v_ref[pl.ds(s, block), :] for s in vert_starts]
        col = lax.broadcasted_iota(jnp.int32, (block, key_count), 1)
        row = lax.broadcasted_iota(jnp.int32, (block, key_count), 0)
        reach = col % block - row
        lane = lax.broadcasted_iota(jnp.int32, (1, key_count), 1) // block
        never = jnp.int32(-4 * block)
        for b in range(group_blocks):
            qb = first + b
            slab_blocks = slab_rows // block
            slab = (me - b // slab_blocks + slabs) % slabs
            q = q_ref[pl.ds(pl.multiple_of(slab * slab_rows + (b % slab_blocks) * block, block), block), :]
            starts = [pl.multiple_of(jnp.maximum(qb - offs[j], 0) * block, block) for j in range(SLASH_COUNT)]
            keys = jnp.concatenate([k_ref[pl.ds(s, block), :] for s in starts] + vert_keys, 0)
            values = jnp.concatenate([v_ref[pl.ds(s, block), :] for s in starts] + vert_values, 0)
            limits = [jnp.where(qb - offs[j] >= 0, offs[j] * block, never) for j in range(SLASH_COUNT)]
            for v in verts:
                ok = v <= qb
                for o in offs:
                    ok = jnp.logical_and(ok, qb - v != o)
                limits.append(jnp.where(ok, (qb - v) * block, never))
            limit = jnp.full((1, key_count), limits[-1], jnp.int32)
            for i in range(len(limits) - 2, -1, -1):
                limit = jnp.where(lane == i, limits[i], limit)
            allowed = reach <= limit
            scores = lax.dot_general(
                q, keys, (((1,), (1,)), ((), ())), preferred_element_type=jnp.float32
            ) * scale
            masked = jnp.where(allowed, scores, -1e30)
            top = jnp.max(masked, axis=1, keepdims=True)
            weight = jnp.exp(masked - top)
            total = jnp.sum(weight, axis=1, keepdims=True)
            rounded = weight.astype(jnp.bfloat16)
            acc = jnp.dot(rounded, values, preferred_element_type=jnp.float32)
            o_ref[pl.ds(b * block, block), :] = (acc / total).astype(o_ref.dtype)

    return kernel


def attend_full(meta, queries, all_kv, local_heads, sharing, slab_rows):
    group_rows = queries.shape[0]
    group_blocks = group_rows // MASK_BLOCK_SIZE
    head_size = HEAD_DIMENSION
    total_rows = all_kv.shape[0]
    value_base = all_kv.shape[1] // (2 * head_size)
    grid_spec = pltpu.PrefetchScalarGridSpec(
        num_scalar_prefetch=1,
        grid=(local_heads,),
        in_specs=[
            pl.BlockSpec((group_rows, head_size), lambda h, m: (0, h)),
            pl.BlockSpec((total_rows, head_size), lambda h, m: (0, h // sharing)),
            pl.BlockSpec((total_rows, head_size), lambda h, m: (0, value_base + h // sharing)),
        ],
        out_specs=pl.BlockSpec((group_rows, head_size), lambda h, m: (0, h)),
    )
    return pl.pallas_call(
        full_kernel(local_heads, group_blocks, slab_rows, group_rows // slab_rows),
        grid_spec=grid_spec,
        out_shape=jax.ShapeDtypeStruct((group_rows, local_heads * head_size), queries.dtype),
    )(meta, queries, all_kv, all_kv)


def attend(meta, queries, key_window, value_window, vert_keys, vert_values, local_heads, sharing, base):
    group_rows = queries.shape[0]
    group_blocks = group_rows // MASK_BLOCK_SIZE
    head_size = HEAD_DIMENSION
    window_rows = key_window.shape[0]
    chunk_heads, vert_rows = vert_keys.shape[:2]
    grid_spec = pltpu.PrefetchScalarGridSpec(
        num_scalar_prefetch=1,
        grid=(chunk_heads,),
        in_specs=[
            pl.BlockSpec((group_rows, head_size), lambda h, m: (0, h + base)),
            pl.BlockSpec((window_rows, head_size), lambda h, m: (0, (h + base) // sharing)),
            pl.BlockSpec((window_rows, head_size), lambda h, m: (0, (h + base) // sharing)),
            pl.BlockSpec((1, vert_rows, head_size), lambda h, m: (h, 0, 0)),
            pl.BlockSpec((1, vert_rows, head_size), lambda h, m: (h, 0, 0)),
        ],
        out_specs=pl.BlockSpec((group_rows, head_size), lambda h, m: (0, h)),
    )
    return pl.pallas_call(
        attention_kernel(local_heads, group_blocks, window_rows // MASK_BLOCK_SIZE - group_blocks, base),
        grid_spec=grid_spec,
        out_shape=jax.ShapeDtypeStruct((group_rows, chunk_heads * head_size), queries.dtype),
    )(meta, queries, key_window, value_window, vert_keys, vert_values)


def per_device(query_rows, key_matrix, value_matrix, vertical, slash_offsets):
    tok_rows = query_rows.shape[0]
    heads_axes = ("inner", "grp")
    head_groups = lax.axis_size("inner") * lax.axis_size("grp")
    head_size = HEAD_DIMENSION
    block_size = MASK_BLOCK_SIZE
    local_heads = query_rows.shape[1] // (head_groups * head_size)
    local_kv = key_matrix.shape[1] // (head_groups * head_size)
    group_sharing_factor = local_heads // local_kv
    query_split = query_rows.reshape(tok_rows, head_groups, local_heads * head_size)
    key_split = key_matrix.reshape(tok_rows, head_groups, local_kv * head_size)
    value_split = value_matrix.reshape(tok_rows, head_groups, local_kv * head_size)
    seq_count = lax.axis_size("outer")
    whole = seq_count * (key_split.size + value_split.size) * key_split.dtype.itemsize
    if whole <= FULL_GATHER_BYTES:
        kv_rows = jnp.concatenate([key_split, value_split], 2).transpose(1, 0, 2)
        spread = jnp.broadcast_to(kv_rows[None], (seq_count,) + kv_rows.shape).reshape(
            (seq_count * head_groups,) + kv_rows.shape[1:]
        )
        everything = lax.all_to_all(
            spread, ("outer",) + heads_axes, split_axis=0, concat_axis=0, tiled=True
        )
    else:
        kv_split = jnp.stack([key_split, value_split], 2)
        kv_group = lax.all_to_all(kv_split, heads_axes, split_axis=1, concat_axis=0, tiled=True)
        key_group, value_group = kv_group[:, 0, 0], kv_group[:, 0, 1]
    me = lax.axis_index(heads_axes)
    received = [lax.dynamic_index_in_dim(query_split, me, 1, keepdims=False)]
    for shift in range(1, head_groups):
        sent = lax.dynamic_index_in_dim(query_split, (me + shift) % head_groups, 1, keepdims=False)
        received.append(
            lax.ppermute(sent, heads_axes, [(i, (i + shift) % head_groups) for i in range(head_groups)])
        )
    received = jnp.stack(received)
    slab_shift = (me - jnp.arange(head_groups, dtype=jnp.int32)) % head_groups
    group_rows = tok_rows * head_groups
    group_blocks = group_rows // block_size
    back = min(SLASH_REACH, group_blocks)
    seq_index = lax.axis_index("outer")
    head_group = lax.axis_index(heads_axes)
    head_offsets = lax.dynamic_slice_in_dim(slash_offsets, head_group * local_heads, local_heads, 0)
    head_verts = lax.dynamic_slice_in_dim(vertical, head_group * local_heads, local_heads, 0)
    first_block = (seq_index * group_blocks).astype(jnp.int32)
    meta = jnp.concatenate(
        [
            head_offsets.reshape(-1).astype(jnp.int32),
            head_verts.reshape(-1).astype(jnp.int32),
            first_block[None],
        ]
    )
    if whole <= FULL_GATHER_BYTES:
        everything = everything.reshape(-1, 2 * local_kv * head_size)
        queries = received.reshape(group_rows, local_heads * head_size)
        results = attend_full(
            jnp.concatenate([meta, me.astype(jnp.int32)[None]]), queries, everything,
            local_heads, group_sharing_factor, tok_rows,
        )
        half = local_heads // 2 * head_size
        merged = results.reshape(head_groups, tok_rows, local_heads * head_size)
        first_half = lax.all_to_all(merged[:, :, :half], heads_axes, split_axis=0, concat_axis=0, tiled=True)
        back_by_shift = [lax.dynamic_index_in_dim(merged[:, :, half:], me, 0, keepdims=False)]
        for shift in range(1, head_groups):
            sent = lax.dynamic_index_in_dim(merged[:, :, half:], (me + shift) % head_groups, 0, keepdims=False)
            back_by_shift.append(
                lax.ppermute(sent, heads_axes, [(i, (i + shift) % head_groups) for i in range(head_groups)])
            )
        second_half = jnp.take(jnp.stack(back_by_shift), slab_shift, axis=0)
        returned = jnp.concatenate([first_half, second_half], 2)
        return returned.transpose(1, 0, 2).reshape(tok_rows, head_groups * local_heads * head_size)
    query_group = jnp.take(received, slab_shift, axis=0)
    key_local = key_group.reshape(group_rows, local_kv * head_size)
    value_local = value_group.reshape(group_rows, local_kv * head_size)
    key_before, value_before = passed_along(
        (key_local[group_rows - back * block_size:], value_local[group_rows - back * block_size:]),
        "outer", 1,
    )
    key_window = jnp.concatenate([key_before, key_local], 0)
    value_window = jnp.concatenate([value_before, value_local], 0)
    kv_index = jnp.arange(local_heads, dtype=jnp.int32) // group_sharing_factor
    owner_seq = head_verts // group_blocks
    local_block = head_verts % group_blocks
    key_blocks = key_local.reshape(group_blocks, block_size, local_kv, head_size)
    value_blocks = value_local.reshape(group_blocks, block_size, local_kv, head_size)
    picked_keys = key_blocks[local_block, :, kv_index[:, None], :]
    picked_values = value_blocks[local_block, :, kv_index[:, None], :]
    owned = (owner_seq == seq_index)[:, :, None, None]
    nothing = jnp.zeros((), picked_keys.dtype)
    mine = jnp.stack(
        [jnp.where(owned, picked_keys, nothing), jnp.where(owned, picked_values, nothing)]
    ).reshape(2, seq_count, -1, head_size).transpose(1, 0, 2, 3)
    part = lax.all_to_all(mine, "outer", split_axis=0, concat_axis=0, tiled=True).sum(
        0, dtype=picked_keys.dtype
    )
    spread = jnp.broadcast_to(part[None], (seq_count,) + part.shape)
    gathered = lax.all_to_all(spread, "outer", split_axis=0, concat_axis=0, tiled=True)
    vert = gathered.transpose(1, 0, 2, 3).reshape(2, local_heads, -1, head_size)
    queries = query_group.reshape(group_rows, local_heads * head_size)
    results = attend(
        meta, queries, key_window, value_window, vert[0], vert[1],
        local_heads, group_sharing_factor, 0,
    )
    merged = results.reshape(head_groups, tok_rows, local_heads * head_size)
    returned = lax.all_to_all(merged, heads_axes, split_axis=0, concat_axis=0, tiled=True)
    return returned.transpose(1, 0, 2).reshape(tok_rows, head_groups * local_heads * head_size)


def solution(mesh):
    seq_count = mesh.shape["seq"]
    inner = 2 if seq_count % 2 == 0 else 1
    work_mesh = Mesh(
        mesh.devices.reshape(seq_count // inner, inner, mesh.shape["grp"]), ("outer", "inner", "grp")
    )
    rows = P(("outer", "inner", "grp"), None)
    return jax.shard_map(
        per_device,
        mesh=work_mesh,
        in_specs=(rows, rows, rows, P(), P()),
        out_specs=rows,
        check_vma=False,
    )
```

```python
import jax
import jax.numpy as jnp
from jax import lax
from jax.experimental import pallas as pl
from jax.experimental.pallas import tpu as pltpu
from jax.sharding import Mesh, PartitionSpec as P

HEAD_DIMENSION = 128
MASK_BLOCK_SIZE = 64
SLASH_COUNT = 3
VERT_COUNT = 3
SLASH_REACH = 8
FULL_GATHER_BYTES = 4 << 20
OUTPUT_CHUNKS = 2


def passed_along(shard, axis, by):
    length = lax.axis_size(axis)
    pairs = [(i, i + by) for i in range(length) if 0 <= i + by < length]
    return lax.ppermute(shard, axis, pairs)


def attention_kernel(local_heads, group_blocks, back, base):
    block = MASK_BLOCK_SIZE
    key_count = (SLASH_COUNT + VERT_COUNT) * block
    scale = HEAD_DIMENSION ** (-0.5)

    def kernel(meta_ref, q_ref, k_ref, v_ref, vk_ref, vv_ref, o_ref):
        h = pl.program_id(0) + base
        first = meta_ref[2 * local_heads * SLASH_COUNT]
        offs = [meta_ref[h * SLASH_COUNT + j] for j in range(SLASH_COUNT)]
        verts = [meta_ref[local_heads * SLASH_COUNT + h * VERT_COUNT + j] for j in range(VERT_COUNT)]
        vert_keys = vk_ref[0]
        vert_values = vv_ref[0]
        col = lax.broadcasted_iota(jnp.int32, (block, key_count), 1)
        row = lax.broadcasted_iota(jnp.int32, (block, key_count), 0)
        reach = col % block - row
        lane = lax.broadcasted_iota(jnp.int32, (1, key_count), 1) // block
        never = jnp.int32(-4 * block)
        for b in range(group_blocks):
            qb = first + b
            q = q_ref[pl.ds(b * block, block), :]
            starts = [pl.multiple_of((back + b - offs[j]) * block, block) for j in range(SLASH_COUNT)]
            keys = jnp.concatenate([k_ref[pl.ds(s, block), :] for s in starts] + [vert_keys], 0)
            values = jnp.concatenate([v_ref[pl.ds(s, block), :] for s in starts] + [vert_values], 0)
            limits = [jnp.where(qb - offs[j] >= 0, offs[j] * block, never) for j in range(SLASH_COUNT)]
            for v in verts:
                ok = v <= qb
                for o in offs:
                    ok = jnp.logical_and(ok, qb - v != o)
                limits.append(jnp.where(ok, (qb - v) * block, never))
            limit = jnp.full((1, key_count), limits[-1], jnp.int32)
            for i in range(len(limits) - 2, -1, -1):
                limit = jnp.where(lane == i, limits[i], limit)
            allowed = reach <= limit
            scores = lax.dot_general(
                q, keys, (((1,), (1,)), ((), ())), preferred_element_type=jnp.float32
            ) * scale
            masked = jnp.where(allowed, scores, -1e30)
            top = jnp.max(masked, axis=1, keepdims=True)
            weight = jnp.exp(masked - top)
            total = jnp.sum(weight, axis=1, keepdims=True)
            rounded = weight.astype(jnp.bfloat16)
            acc = jnp.dot(rounded, values, preferred_element_type=jnp.float32)
            o_ref[pl.ds(b * block, block), :] = (acc / total).astype(o_ref.dtype)

    return kernel


def full_kernel(local_heads, group_blocks, slab_rows, slabs, base):
    block = MASK_BLOCK_SIZE
    key_count = (SLASH_COUNT + VERT_COUNT) * block
    scale = HEAD_DIMENSION ** (-0.5)

    def kernel(meta_ref, q_ref, k_ref, v_ref, o_ref):
        h = pl.program_id(0) + base
        first = meta_ref[2 * local_heads * SLASH_COUNT]
        me = meta_ref[2 * local_heads * SLASH_COUNT + 1]
        offs = [meta_ref[h * SLASH_COUNT + j] for j in range(SLASH_COUNT)]
        verts = [meta_ref[local_heads * SLASH_COUNT + h * VERT_COUNT + j] for j in range(VERT_COUNT)]
        vert_starts = [pl.multiple_of(v * block, block) for v in verts]
        vert_keys = [k_ref[pl.ds(s, block), :] for s in vert_starts]
        vert_values = [v_ref[pl.ds(s, block), :] for s in vert_starts]
        col = lax.broadcasted_iota(jnp.int32, (block, key_count), 1)
        row = lax.broadcasted_iota(jnp.int32, (block, key_count), 0)
        reach = col % block - row
        lane = lax.broadcasted_iota(jnp.int32, (1, key_count), 1) // block
        never = jnp.int32(-4 * block)
        for b in range(group_blocks):
            qb = first + b
            slab_blocks = slab_rows // block
            slab = (me - b // slab_blocks + slabs) % slabs
            q = q_ref[pl.ds(pl.multiple_of(slab * slab_rows + (b % slab_blocks) * block, block), block), :]
            starts = [pl.multiple_of(jnp.maximum(qb - offs[j], 0) * block, block) for j in range(SLASH_COUNT)]
            keys = jnp.concatenate([k_ref[pl.ds(s, block), :] for s in starts] + vert_keys, 0)
            values = jnp.concatenate([v_ref[pl.ds(s, block), :] for s in starts] + vert_values, 0)
            limits = [jnp.where(qb - offs[j] >= 0, offs[j] * block, never) for j in range(SLASH_COUNT)]
            for v in verts:
                ok = v <= qb
                for o in offs:
                    ok = jnp.logical_and(ok, qb - v != o)
                limits.append(jnp.where(ok, (qb - v) * block, never))
            limit = jnp.full((1, key_count), limits[-1], jnp.int32)
            for i in range(len(limits) - 2, -1, -1):
                limit = jnp.where(lane == i, limits[i], limit)
            allowed = reach <= limit
            scores = lax.dot_general(
                q, keys, (((1,), (1,)), ((), ())), preferred_element_type=jnp.float32
            ) * scale
            masked = jnp.where(allowed, scores, -1e30)
            top = jnp.max(masked, axis=1, keepdims=True)
            weight = jnp.exp(masked - top)
            total = jnp.sum(weight, axis=1, keepdims=True)
            rounded = weight.astype(jnp.bfloat16)
            acc = jnp.dot(rounded, values, preferred_element_type=jnp.float32)
            o_ref[pl.ds(b * block, block), :] = (acc / total).astype(o_ref.dtype)

    return kernel


def attend_full(meta, queries, all_kv, local_heads, sharing, slab_rows, base, chunk_heads):
    group_rows = queries.shape[0]
    group_blocks = group_rows // MASK_BLOCK_SIZE
    head_size = HEAD_DIMENSION
    total_rows = all_kv.shape[0]
    value_base = all_kv.shape[1] // (2 * head_size)
    grid_spec = pltpu.PrefetchScalarGridSpec(
        num_scalar_prefetch=1,
        grid=(chunk_heads,),
        in_specs=[
            pl.BlockSpec((group_rows, head_size), lambda h, m: (0, h + base)),
            pl.BlockSpec((total_rows, head_size), lambda h, m: (0, (h + base) // sharing)),
            pl.BlockSpec((total_rows, head_size), lambda h, m: (0, value_base + (h + base) // sharing)),
        ],
        out_specs=pl.BlockSpec((group_rows, head_size), lambda h, m: (0, h)),
    )
    return pl.pallas_call(
        full_kernel(local_heads, group_blocks, slab_rows, group_rows // slab_rows, base),
        grid_spec=grid_spec,
        out_shape=jax.ShapeDtypeStruct((group_rows, chunk_heads * head_size), queries.dtype),
    )(meta, queries, all_kv, all_kv)


def attend(meta, queries, key_window, value_window, vert_keys, vert_values, local_heads, sharing, base):
    group_rows = queries.shape[0]
    group_blocks = group_rows // MASK_BLOCK_SIZE
    head_size = HEAD_DIMENSION
    window_rows = key_window.shape[0]
    chunk_heads, vert_rows = vert_keys.shape[:2]
    grid_spec = pltpu.PrefetchScalarGridSpec(
        num_scalar_prefetch=1,
        grid=(chunk_heads,),
        in_specs=[
            pl.BlockSpec((group_rows, head_size), lambda h, m: (0, h + base)),
            pl.BlockSpec((window_rows, head_size), lambda h, m: (0, (h + base) // sharing)),
            pl.BlockSpec((window_rows, head_size), lambda h, m: (0, (h + base) // sharing)),
            pl.BlockSpec((1, vert_rows, head_size), lambda h, m: (h, 0, 0)),
            pl.BlockSpec((1, vert_rows, head_size), lambda h, m: (h, 0, 0)),
        ],
        out_specs=pl.BlockSpec((group_rows, head_size), lambda h, m: (0, h)),
    )
    return pl.pallas_call(
        attention_kernel(local_heads, group_blocks, window_rows // MASK_BLOCK_SIZE - group_blocks, base),
        grid_spec=grid_spec,
        out_shape=jax.ShapeDtypeStruct((group_rows, chunk_heads * head_size), queries.dtype),
    )(meta, queries, key_window, value_window, vert_keys, vert_values)


def per_device(query_rows, key_matrix, value_matrix, vertical, slash_offsets):
    tok_rows = query_rows.shape[0]
    heads_axes = ("inner", "grp")
    head_groups = lax.axis_size("inner") * lax.axis_size("grp")
    head_size = HEAD_DIMENSION
    block_size = MASK_BLOCK_SIZE
    local_heads = query_rows.shape[1] // (head_groups * head_size)
    local_kv = key_matrix.shape[1] // (head_groups * head_size)
    group_sharing_factor = local_heads // local_kv
    query_split = query_rows.reshape(tok_rows, head_groups, local_heads * head_size)
    key_split = key_matrix.reshape(tok_rows, head_groups, local_kv * head_size)
    value_split = value_matrix.reshape(tok_rows, head_groups, local_kv * head_size)
    seq_count = lax.axis_size("outer")
    whole = seq_count * (key_split.size + value_split.size) * key_split.dtype.itemsize
    if whole <= FULL_GATHER_BYTES:
        kv_rows = jnp.concatenate([key_split, value_split], 2).transpose(1, 0, 2)
        spread = jnp.broadcast_to(kv_rows[None], (seq_count,) + kv_rows.shape).reshape(
            (seq_count * head_groups,) + kv_rows.shape[1:]
        )
        everything = lax.all_to_all(
            spread, ("outer",) + heads_axes, split_axis=0, concat_axis=0, tiled=True
        )
    else:
        kv_split = jnp.stack([key_split, value_split], 2)
        kv_group = lax.all_to_all(kv_split, heads_axes, split_axis=1, concat_axis=0, tiled=True)
        key_group, value_group = kv_group[:, 0, 0], kv_group[:, 0, 1]
    me = lax.axis_index(heads_axes)
    received = [lax.dynamic_index_in_dim(query_split, me, 1, keepdims=False)]
    for shift in range(1, head_groups):
        sent = lax.dynamic_index_in_dim(query_split, (me + shift) % head_groups, 1, keepdims=False)
        received.append(
            lax.ppermute(sent, heads_axes, [(i, (i + shift) % head_groups) for i in range(head_groups)])
        )
    received = jnp.stack(received)
    group_rows = tok_rows * head_groups
    group_blocks = group_rows // block_size
    back = min(SLASH_REACH, group_blocks)
    seq_index = lax.axis_index("outer")
    head_group = lax.axis_index(heads_axes)
    head_offsets = lax.dynamic_slice_in_dim(slash_offsets, head_group * local_heads, local_heads, 0)
    head_verts = lax.dynamic_slice_in_dim(vertical, head_group * local_heads, local_heads, 0)
    first_block = (seq_index * group_blocks).astype(jnp.int32)
    meta = jnp.concatenate(
        [
            head_offsets.reshape(-1).astype(jnp.int32),
            head_verts.reshape(-1).astype(jnp.int32),
            first_block[None],
        ]
    )
    if whole <= FULL_GATHER_BYTES:
        everything = everything.reshape(-1, 2 * local_kv * head_size)
        queries = received.reshape(group_rows, local_heads * head_size)
        chunk_heads = local_heads // OUTPUT_CHUNKS
        pieces = []
        for c in range(OUTPUT_CHUNKS):
            results = attend_full(
                jnp.concatenate([meta, me.astype(jnp.int32)[None]]), queries, everything,
                local_heads, group_sharing_factor, tok_rows, c * chunk_heads, chunk_heads,
            )
            merged = results.reshape(head_groups, tok_rows, chunk_heads * head_size)
            pieces.append(lax.all_to_all(merged, heads_axes, split_axis=0, concat_axis=0, tiled=True))
        returned = jnp.concatenate(pieces, 2)
        return returned.transpose(1, 0, 2).reshape(tok_rows, head_groups * local_heads * head_size)
    slab_shift = (me - jnp.arange(head_groups, dtype=jnp.int32)) % head_groups
    query_group = jnp.take(received, slab_shift, axis=0)
    key_local = key_group.reshape(group_rows, local_kv * head_size)
    value_local = value_group.reshape(group_rows, local_kv * head_size)
    key_before, value_before = passed_along(
        (key_local[group_rows - back * block_size:], value_local[group_rows - back * block_size:]),
        "outer", 1,
    )
    key_window = jnp.concatenate([key_before, key_local], 0)
    value_window = jnp.concatenate([value_before, value_local], 0)
    kv_index = jnp.arange(local_heads, dtype=jnp.int32) // group_sharing_factor
    owner_seq = head_verts // group_blocks
    local_block = head_verts % group_blocks
    key_blocks = key_local.reshape(group_blocks, block_size, local_kv, head_size)
    value_blocks = value_local.reshape(group_blocks, block_size, local_kv, head_size)
    picked_keys = key_blocks[local_block, :, kv_index[:, None], :]
    picked_values = value_blocks[local_block, :, kv_index[:, None], :]
    owned = (owner_seq == seq_index)[:, :, None, None]
    nothing = jnp.zeros((), picked_keys.dtype)
    mine = jnp.stack(
        [jnp.where(owned, picked_keys, nothing), jnp.where(owned, picked_values, nothing)]
    ).reshape(2, seq_count, -1, head_size).transpose(1, 0, 2, 3)
    part = lax.all_to_all(mine, "outer", split_axis=0, concat_axis=0, tiled=True).sum(
        0, dtype=picked_keys.dtype
    )
    spread = jnp.broadcast_to(part[None], (seq_count,) + part.shape)
    gathered = lax.all_to_all(spread, "outer", split_axis=0, concat_axis=0, tiled=True)
    vert = gathered.transpose(1, 0, 2, 3).reshape(2, local_heads, -1, head_size)
    queries = query_group.reshape(group_rows, local_heads * head_size)
    results = attend(
        meta, queries, key_window, value_window, vert[0], vert[1],
        local_heads, group_sharing_factor, 0,
    )
    merged = results.reshape(head_groups, tok_rows, local_heads * head_size)
    returned = lax.all_to_all(merged, heads_axes, split_axis=0, concat_axis=0, tiled=True)
    return returned.transpose(1, 0, 2).reshape(tok_rows, head_groups * local_heads * head_size)


def solution(mesh):
    seq_count = mesh.shape["seq"]
    inner = 2 if seq_count % 2 == 0 else 1
    work_mesh = Mesh(
        mesh.devices.reshape(seq_count // inner, inner, mesh.shape["grp"]), ("outer", "inner", "grp")
    )
    rows = P(("outer", "inner", "grp"), None)
    return jax.shard_map(
        per_device,
        mesh=work_mesh,
        in_specs=(rows, rows, rows, P(), P()),
        out_specs=rows,
        check_vma=False,
    )
```

```python
import jax
import jax.numpy as jnp
from jax import lax
from jax.experimental import pallas as pl
from jax.experimental.pallas import tpu as pltpu
from jax.sharding import Mesh, PartitionSpec as P

HEAD_DIMENSION = 128
MASK_BLOCK_SIZE = 64
SLASH_COUNT = 3
VERT_COUNT = 3
SLASH_REACH = 8
FULL_GATHER_BYTES = 4 << 20
OUTPUT_CHUNKS = 2


def passed_along(shard, axis, by):
    length = lax.axis_size(axis)
    pairs = [(i, i + by) for i in range(length) if 0 <= i + by < length]
    return lax.ppermute(shard, axis, pairs)


def attention_kernel(local_heads, group_blocks, back, base):
    block = MASK_BLOCK_SIZE
    key_count = (SLASH_COUNT + VERT_COUNT) * block
    scale = HEAD_DIMENSION ** (-0.5)

    def kernel(meta_ref, q_ref, k_ref, v_ref, vk_ref, vv_ref, o_ref):
        h = pl.program_id(0) + base
        first = meta_ref[2 * local_heads * SLASH_COUNT]
        offs = [meta_ref[h * SLASH_COUNT + j] for j in range(SLASH_COUNT)]
        verts = [meta_ref[local_heads * SLASH_COUNT + h * VERT_COUNT + j] for j in range(VERT_COUNT)]
        vert_keys = vk_ref[0]
        vert_values = vv_ref[0]
        col = lax.broadcasted_iota(jnp.int32, (block, key_count), 1)
        row = lax.broadcasted_iota(jnp.int32, (block, key_count), 0)
        reach = col % block - row
        lane = lax.broadcasted_iota(jnp.int32, (1, key_count), 1) // block
        never = jnp.int32(-4 * block)
        for b in range(group_blocks):
            qb = first + b
            q = q_ref[pl.ds(b * block, block), :]
            starts = [pl.multiple_of((back + b - offs[j]) * block, block) for j in range(SLASH_COUNT)]
            keys = jnp.concatenate([k_ref[pl.ds(s, block), :] for s in starts] + [vert_keys], 0)
            values = jnp.concatenate([v_ref[pl.ds(s, block), :] for s in starts] + [vert_values], 0)
            limits = [jnp.where(qb - offs[j] >= 0, offs[j] * block, never) for j in range(SLASH_COUNT)]
            for v in verts:
                ok = v <= qb
                for o in offs:
                    ok = jnp.logical_and(ok, qb - v != o)
                limits.append(jnp.where(ok, (qb - v) * block, never))
            limit = jnp.full((1, key_count), limits[-1], jnp.int32)
            for i in range(len(limits) - 2, -1, -1):
                limit = jnp.where(lane == i, limits[i], limit)
            allowed = reach <= limit
            scores = lax.dot_general(
                q, keys, (((1,), (1,)), ((), ())), preferred_element_type=jnp.float32
            ) * scale
            masked = jnp.where(allowed, scores, -1e30)
            top = jnp.max(masked, axis=1, keepdims=True)
            weight = jnp.exp(masked - top)
            total = jnp.sum(weight, axis=1, keepdims=True)
            rounded = weight.astype(jnp.bfloat16)
            acc = jnp.dot(rounded, values, preferred_element_type=jnp.float32)
            o_ref[pl.ds(b * block, block), :] = (acc / total).astype(o_ref.dtype)

    return kernel


def full_kernel(local_heads, group_blocks, slab_rows, slabs, base, kv_heads, sharing):
    block = MASK_BLOCK_SIZE
    key_count = (SLASH_COUNT + VERT_COUNT) * block
    scale = HEAD_DIMENSION ** (-0.5)

    def kernel(meta_ref, q_ref, kv_ref, o_ref):
        h = pl.program_id(0) + base
        first = meta_ref[2 * local_heads * SLASH_COUNT]
        me = meta_ref[2 * local_heads * SLASH_COUNT + 1]
        if kv_heads == 1:
            k_ref = kv_ref.at[:, pl.ds(0, HEAD_DIMENSION)]
            v_ref = kv_ref.at[:, pl.ds(HEAD_DIMENSION, HEAD_DIMENSION)]
        else:
            kv = h // sharing
            k_ref = kv_ref.at[:, pl.ds(pl.multiple_of(kv * HEAD_DIMENSION, HEAD_DIMENSION), HEAD_DIMENSION)]
            v_ref = kv_ref.at[
                :, pl.ds(pl.multiple_of((kv_heads + kv) * HEAD_DIMENSION, HEAD_DIMENSION), HEAD_DIMENSION)
            ]
        offs = [meta_ref[h * SLASH_COUNT + j] for j in range(SLASH_COUNT)]
        verts = [meta_ref[local_heads * SLASH_COUNT + h * VERT_COUNT + j] for j in range(VERT_COUNT)]
        vert_starts = [pl.multiple_of(v * block, block) for v in verts]
        vert_keys = [k_ref[pl.ds(s, block), :] for s in vert_starts]
        vert_values = [v_ref[pl.ds(s, block), :] for s in vert_starts]
        col = lax.broadcasted_iota(jnp.int32, (block, key_count), 1)
        row = lax.broadcasted_iota(jnp.int32, (block, key_count), 0)
        reach = col % block - row
        lane = lax.broadcasted_iota(jnp.int32, (1, key_count), 1) // block
        never = jnp.int32(-4 * block)
        for b in range(group_blocks):
            qb = first + b
            slab_blocks = slab_rows // block
            slab = (me - b // slab_blocks + slabs) % slabs
            q = q_ref[pl.ds(pl.multiple_of(slab * slab_rows + (b % slab_blocks) * block, block), block), :]
            starts = [pl.multiple_of(jnp.maximum(qb - offs[j], 0) * block, block) for j in range(SLASH_COUNT)]
            keys = jnp.concatenate([k_ref[pl.ds(s, block), :] for s in starts] + vert_keys, 0)
            values = jnp.concatenate([v_ref[pl.ds(s, block), :] for s in starts] + vert_values, 0)
            limits = [jnp.where(qb - offs[j] >= 0, offs[j] * block, never) for j in range(SLASH_COUNT)]
            for v in verts:
                ok = v <= qb
                for o in offs:
                    ok = jnp.logical_and(ok, qb - v != o)
                limits.append(jnp.where(ok, (qb - v) * block, never))
            limit = jnp.full((1, key_count), limits[-1], jnp.int32)
            for i in range(len(limits) - 2, -1, -1):
                limit = jnp.where(lane == i, limits[i], limit)
            allowed = reach <= limit
            scores = lax.dot_general(
                q, keys, (((1,), (1,)), ((), ())), preferred_element_type=jnp.float32
            ) * scale
            masked = jnp.where(allowed, scores, -1e30)
            top = jnp.max(masked, axis=1, keepdims=True)
            weight = jnp.exp(masked - top)
            total = jnp.sum(weight, axis=1, keepdims=True)
            rounded = weight.astype(jnp.bfloat16)
            acc = jnp.dot(rounded, values, preferred_element_type=jnp.float32)
            o_ref[pl.ds(b * block, block), :] = (acc / total).astype(o_ref.dtype)

    return kernel


def attend_full(meta, queries, all_kv, local_heads, sharing, slab_rows, base, chunk_heads):
    group_rows = queries.shape[0]
    group_blocks = group_rows // MASK_BLOCK_SIZE
    head_size = HEAD_DIMENSION
    value_base = all_kv.shape[1] // (2 * head_size)
    grid_spec = pltpu.PrefetchScalarGridSpec(
        num_scalar_prefetch=1,
        grid=(chunk_heads,),
        in_specs=[
            pl.BlockSpec((group_rows, head_size), lambda h, m: (0, h + base)),
            pl.BlockSpec(memory_space=pltpu.VMEM),
        ],
        out_specs=pl.BlockSpec((group_rows, head_size), lambda h, m: (0, h)),
    )
    return pl.pallas_call(
        full_kernel(local_heads, group_blocks, slab_rows, group_rows // slab_rows, base, value_base, sharing),
        grid_spec=grid_spec,
        out_shape=jax.ShapeDtypeStruct((group_rows, chunk_heads * head_size), queries.dtype),
    )(meta, queries, all_kv)


def attend(meta, queries, key_window, value_window, vert_keys, vert_values, local_heads, sharing, base):
    group_rows = queries.shape[0]
    group_blocks = group_rows // MASK_BLOCK_SIZE
    head_size = HEAD_DIMENSION
    window_rows = key_window.shape[0]
    chunk_heads, vert_rows = vert_keys.shape[:2]
    grid_spec = pltpu.PrefetchScalarGridSpec(
        num_scalar_prefetch=1,
        grid=(chunk_heads,),
        in_specs=[
            pl.BlockSpec((group_rows, head_size), lambda h, m: (0, h + base)),
            pl.BlockSpec((window_rows, head_size), lambda h, m: (0, (h + base) // sharing)),
            pl.BlockSpec((window_rows, head_size), lambda h, m: (0, (h + base) // sharing)),
            pl.BlockSpec((1, vert_rows, head_size), lambda h, m: (h, 0, 0)),
            pl.BlockSpec((1, vert_rows, head_size), lambda h, m: (h, 0, 0)),
        ],
        out_specs=pl.BlockSpec((group_rows, head_size), lambda h, m: (0, h)),
    )
    return pl.pallas_call(
        attention_kernel(local_heads, group_blocks, window_rows // MASK_BLOCK_SIZE - group_blocks, base),
        grid_spec=grid_spec,
        out_shape=jax.ShapeDtypeStruct((group_rows, chunk_heads * head_size), queries.dtype),
    )(meta, queries, key_window, value_window, vert_keys, vert_values)


def per_device(query_rows, key_matrix, value_matrix, vertical, slash_offsets):
    tok_rows = query_rows.shape[0]
    heads_axes = ("inner", "grp")
    head_groups = lax.axis_size("inner") * lax.axis_size("grp")
    head_size = HEAD_DIMENSION
    block_size = MASK_BLOCK_SIZE
    local_heads = query_rows.shape[1] // (head_groups * head_size)
    local_kv = key_matrix.shape[1] // (head_groups * head_size)
    group_sharing_factor = local_heads // local_kv
    query_split = query_rows.reshape(tok_rows, head_groups, local_heads * head_size)
    key_split = key_matrix.reshape(tok_rows, head_groups, local_kv * head_size)
    value_split = value_matrix.reshape(tok_rows, head_groups, local_kv * head_size)
    seq_count = lax.axis_size("outer")
    whole = seq_count * (key_split.size + value_split.size) * key_split.dtype.itemsize
    if whole <= FULL_GATHER_BYTES:
        kv_rows = jnp.concatenate([key_split, value_split], 2).transpose(1, 0, 2)
        spread = jnp.broadcast_to(kv_rows[None], (seq_count,) + kv_rows.shape).reshape(
            (seq_count * head_groups,) + kv_rows.shape[1:]
        )
        everything = lax.all_to_all(
            spread, ("outer",) + heads_axes, split_axis=0, concat_axis=0, tiled=True
        )
    else:
        kv_split = jnp.stack([key_split, value_split], 2)
        kv_group = lax.all_to_all(kv_split, heads_axes, split_axis=1, concat_axis=0, tiled=True)
        key_group, value_group = kv_group[:, 0, 0], kv_group[:, 0, 1]
    me = lax.axis_index(heads_axes)
    received = [lax.dynamic_index_in_dim(query_split, me, 1, keepdims=False)]
    for shift in range(1, head_groups):
        sent = lax.dynamic_index_in_dim(query_split, (me + shift) % head_groups, 1, keepdims=False)
        received.append(
            lax.ppermute(sent, heads_axes, [(i, (i + shift) % head_groups) for i in range(head_groups)])
        )
    received = jnp.stack(received)
    group_rows = tok_rows * head_groups
    group_blocks = group_rows // block_size
    back = min(SLASH_REACH, group_blocks)
    seq_index = lax.axis_index("outer")
    head_group = lax.axis_index(heads_axes)
    head_offsets = lax.dynamic_slice_in_dim(slash_offsets, head_group * local_heads, local_heads, 0)
    head_verts = lax.dynamic_slice_in_dim(vertical, head_group * local_heads, local_heads, 0)
    first_block = (seq_index * group_blocks).astype(jnp.int32)
    meta = jnp.concatenate(
        [
            head_offsets.reshape(-1).astype(jnp.int32),
            head_verts.reshape(-1).astype(jnp.int32),
            first_block[None],
        ]
    )
    if whole <= FULL_GATHER_BYTES:
        everything = everything.reshape(-1, 2 * local_kv * head_size)
        queries = received.reshape(group_rows, local_heads * head_size)
        chunk_heads = local_heads // OUTPUT_CHUNKS
        pieces = []
        for c in range(OUTPUT_CHUNKS):
            results = attend_full(
                jnp.concatenate([meta, me.astype(jnp.int32)[None]]), queries, everything,
                local_heads, group_sharing_factor, tok_rows, c * chunk_heads, chunk_heads,
            )
            merged = results.reshape(head_groups, tok_rows, chunk_heads * head_size)
            pieces.append(lax.all_to_all(merged, heads_axes, split_axis=0, concat_axis=0, tiled=True))
        returned = jnp.concatenate(pieces, 2)
        return returned.transpose(1, 0, 2).reshape(tok_rows, head_groups * local_heads * head_size)
    slab_shift = (me - jnp.arange(head_groups, dtype=jnp.int32)) % head_groups
    query_group = jnp.take(received, slab_shift, axis=0)
    key_local = key_group.reshape(group_rows, local_kv * head_size)
    value_local = value_group.reshape(group_rows, local_kv * head_size)
    key_before, value_before = passed_along(
        (key_local[group_rows - back * block_size:], value_local[group_rows - back * block_size:]),
        "outer", 1,
    )
    key_window = jnp.concatenate([key_before, key_local], 0)
    value_window = jnp.concatenate([value_before, value_local], 0)
    kv_index = jnp.arange(local_heads, dtype=jnp.int32) // group_sharing_factor
    owner_seq = head_verts // group_blocks
    local_block = head_verts % group_blocks
    key_blocks = key_local.reshape(group_blocks, block_size, local_kv, head_size)
    value_blocks = value_local.reshape(group_blocks, block_size, local_kv, head_size)
    picked_keys = key_blocks[local_block, :, kv_index[:, None], :]
    picked_values = value_blocks[local_block, :, kv_index[:, None], :]
    owned = (owner_seq == seq_index)[:, :, None, None]
    nothing = jnp.zeros((), picked_keys.dtype)
    mine = jnp.stack(
        [jnp.where(owned, picked_keys, nothing), jnp.where(owned, picked_values, nothing)]
    ).reshape(2, seq_count, -1, head_size).transpose(1, 0, 2, 3)
    part = lax.all_to_all(mine, "outer", split_axis=0, concat_axis=0, tiled=True).sum(
        0, dtype=picked_keys.dtype
    )
    spread = jnp.broadcast_to(part[None], (seq_count,) + part.shape)
    gathered = lax.all_to_all(spread, "outer", split_axis=0, concat_axis=0, tiled=True)
    vert = gathered.transpose(1, 0, 2, 3).reshape(2, local_heads, -1, head_size)
    queries = query_group.reshape(group_rows, local_heads * head_size)
    results = attend(
        meta, queries, key_window, value_window, vert[0], vert[1],
        local_heads, group_sharing_factor, 0,
    )
    merged = results.reshape(head_groups, tok_rows, local_heads * head_size)
    returned = lax.all_to_all(merged, heads_axes, split_axis=0, concat_axis=0, tiled=True)
    return returned.transpose(1, 0, 2).reshape(tok_rows, head_groups * local_heads * head_size)


def solution(mesh):
    seq_count = mesh.shape["seq"]
    inner = 2 if seq_count % 2 == 0 else 1
    work_mesh = Mesh(
        mesh.devices.reshape(seq_count // inner, inner, mesh.shape["grp"]), ("outer", "inner", "grp")
    )
    rows = P(("outer", "inner", "grp"), None)
    return jax.shard_map(
        per_device,
        mesh=work_mesh,
        in_specs=(rows, rows, rows, P(), P()),
        out_specs=rows,
        check_vma=False,
    )
```

```python
import jax
import jax.numpy as jnp
from jax import lax
from jax.experimental import pallas as pl
from jax.experimental.pallas import tpu as pltpu
from jax.sharding import Mesh, PartitionSpec as P

HEAD_DIMENSION = 128
MASK_BLOCK_SIZE = 64
SLASH_COUNT = 3
VERT_COUNT = 3
SLASH_REACH = 8
FULL_GATHER_BYTES = 4 << 20
OUTPUT_CHUNKS = 2


def passed_along(shard, axis, by):
    length = lax.axis_size(axis)
    pairs = [(i, i + by) for i in range(length) if 0 <= i + by < length]
    return lax.ppermute(shard, axis, pairs)


def attention_kernel(local_heads, group_blocks, back, base):
    block = MASK_BLOCK_SIZE
    key_count = (SLASH_COUNT + VERT_COUNT) * block
    scale = HEAD_DIMENSION ** (-0.5)

    def kernel(meta_ref, q_ref, k_ref, v_ref, vk_ref, vv_ref, o_ref):
        h = pl.program_id(0) + base
        first = meta_ref[2 * local_heads * SLASH_COUNT]
        offs = [meta_ref[h * SLASH_COUNT + j] for j in range(SLASH_COUNT)]
        verts = [meta_ref[local_heads * SLASH_COUNT + h * VERT_COUNT + j] for j in range(VERT_COUNT)]
        vert_keys = vk_ref[0]
        vert_values = vv_ref[0]
        col = lax.broadcasted_iota(jnp.int32, (block, key_count), 1)
        row = lax.broadcasted_iota(jnp.int32, (block, key_count), 0)
        reach = col % block - row
        lane = lax.broadcasted_iota(jnp.int32, (1, key_count), 1) // block
        never = jnp.int32(-4 * block)
        for b in range(group_blocks):
            qb = first + b
            q = q_ref[pl.ds(b * block, block), :]
            starts = [pl.multiple_of((back + b - offs[j]) * block, block) for j in range(SLASH_COUNT)]
            keys = jnp.concatenate([k_ref[pl.ds(s, block), :] for s in starts] + [vert_keys], 0)
            values = jnp.concatenate([v_ref[pl.ds(s, block), :] for s in starts] + [vert_values], 0)
            limits = [jnp.where(qb - offs[j] >= 0, offs[j] * block, never) for j in range(SLASH_COUNT)]
            for v in verts:
                ok = v <= qb
                for o in offs:
                    ok = jnp.logical_and(ok, qb - v != o)
                limits.append(jnp.where(ok, (qb - v) * block, never))
            limit = jnp.full((1, key_count), limits[-1], jnp.int32)
            for i in range(len(limits) - 2, -1, -1):
                limit = jnp.where(lane == i, limits[i], limit)
            allowed = reach <= limit
            scores = lax.dot_general(
                q, keys, (((1,), (1,)), ((), ())), preferred_element_type=jnp.float32
            ) * scale
            masked = jnp.where(allowed, scores, -1e30)
            top = jnp.max(masked, axis=1, keepdims=True)
            weight = jnp.exp(masked - top)
            total = jnp.sum(weight, axis=1, keepdims=True)
            rounded = weight.astype(jnp.bfloat16)
            acc = jnp.dot(rounded, values, preferred_element_type=jnp.float32)
            o_ref[pl.ds(b * block, block), :] = (acc / total).astype(o_ref.dtype)

    return kernel


def full_kernel(local_heads, group_blocks, slab_rows, slabs, base, kv_heads, sharing):
    block = MASK_BLOCK_SIZE
    key_count = (SLASH_COUNT + VERT_COUNT) * block
    scale = HEAD_DIMENSION ** (-0.5)

    def kernel(meta_ref, q_ref, kv_ref, o_ref):
        h = pl.program_id(0) + base
        first = meta_ref[2 * local_heads * SLASH_COUNT]
        me = meta_ref[2 * local_heads * SLASH_COUNT + 1]
        kv_cols = pl.ds(pl.multiple_of((h // sharing) * HEAD_DIMENSION, HEAD_DIMENSION), HEAD_DIMENSION)

        def rows(which, start):
            return kv_ref[start // slab_rows, which, pl.ds(pl.multiple_of(start % slab_rows, block), block), kv_cols]

        offs = [meta_ref[h * SLASH_COUNT + j] for j in range(SLASH_COUNT)]
        verts = [meta_ref[local_heads * SLASH_COUNT + h * VERT_COUNT + j] for j in range(VERT_COUNT)]
        vert_starts = [pl.multiple_of(v * block, block) for v in verts]
        vert_keys = [rows(0, s) for s in vert_starts]
        vert_values = [rows(1, s) for s in vert_starts]
        col = lax.broadcasted_iota(jnp.int32, (block, key_count), 1)
        row = lax.broadcasted_iota(jnp.int32, (block, key_count), 0)
        reach = col % block - row
        lane = lax.broadcasted_iota(jnp.int32, (1, key_count), 1) // block
        never = jnp.int32(-4 * block)
        for b in range(group_blocks):
            qb = first + b
            slab_blocks = slab_rows // block
            slab = (me - b // slab_blocks + slabs) % slabs
            q = q_ref[pl.ds(pl.multiple_of(slab * slab_rows + (b % slab_blocks) * block, block), block), :]
            starts = [pl.multiple_of(jnp.maximum(qb - offs[j], 0) * block, block) for j in range(SLASH_COUNT)]
            keys = jnp.concatenate([rows(0, s) for s in starts] + vert_keys, 0)
            values = jnp.concatenate([rows(1, s) for s in starts] + vert_values, 0)
            limits = [jnp.where(qb - offs[j] >= 0, offs[j] * block, never) for j in range(SLASH_COUNT)]
            for v in verts:
                ok = v <= qb
                for o in offs:
                    ok = jnp.logical_and(ok, qb - v != o)
                limits.append(jnp.where(ok, (qb - v) * block, never))
            limit = jnp.full((1, key_count), limits[-1], jnp.int32)
            for i in range(len(limits) - 2, -1, -1):
                limit = jnp.where(lane == i, limits[i], limit)
            allowed = reach <= limit
            scores = lax.dot_general(
                q, keys, (((1,), (1,)), ((), ())), preferred_element_type=jnp.float32
            ) * scale
            masked = jnp.where(allowed, scores, -1e30)
            top = jnp.max(masked, axis=1, keepdims=True)
            weight = jnp.exp(masked - top)
            total = jnp.sum(weight, axis=1, keepdims=True)
            rounded = weight.astype(jnp.bfloat16)
            acc = jnp.dot(rounded, values, preferred_element_type=jnp.float32)
            o_ref[pl.ds(b * block, block), :] = (acc / total).astype(o_ref.dtype)

    return kernel


def attend_full(meta, queries, all_kv, local_heads, sharing, slab_rows, base, chunk_heads):
    group_rows = queries.shape[0]
    group_blocks = group_rows // MASK_BLOCK_SIZE
    head_size = HEAD_DIMENSION
    value_base = all_kv.shape[-1] // head_size
    grid_spec = pltpu.PrefetchScalarGridSpec(
        num_scalar_prefetch=1,
        grid=(chunk_heads,),
        in_specs=[
            pl.BlockSpec((group_rows, head_size), lambda h, m: (0, h + base)),
            pl.BlockSpec(memory_space=pltpu.VMEM),
        ],
        out_specs=pl.BlockSpec((group_rows, head_size), lambda h, m: (0, h)),
    )
    return pl.pallas_call(
        full_kernel(local_heads, group_blocks, slab_rows, group_rows // slab_rows, base, value_base, sharing),
        grid_spec=grid_spec,
        out_shape=jax.ShapeDtypeStruct((group_rows, chunk_heads * head_size), queries.dtype),
    )(meta, queries, all_kv)


def attend(meta, queries, key_window, value_window, vert_keys, vert_values, local_heads, sharing, base):
    group_rows = queries.shape[0]
    group_blocks = group_rows // MASK_BLOCK_SIZE
    head_size = HEAD_DIMENSION
    window_rows = key_window.shape[0]
    chunk_heads, vert_rows = vert_keys.shape[:2]
    grid_spec = pltpu.PrefetchScalarGridSpec(
        num_scalar_prefetch=1,
        grid=(chunk_heads,),
        in_specs=[
            pl.BlockSpec((group_rows, head_size), lambda h, m: (0, h + base)),
            pl.BlockSpec((window_rows, head_size), lambda h, m: (0, (h + base) // sharing)),
            pl.BlockSpec((window_rows, head_size), lambda h, m: (0, (h + base) // sharing)),
            pl.BlockSpec((1, vert_rows, head_size), lambda h, m: (h, 0, 0)),
            pl.BlockSpec((1, vert_rows, head_size), lambda h, m: (h, 0, 0)),
        ],
        out_specs=pl.BlockSpec((group_rows, head_size), lambda h, m: (0, h)),
    )
    return pl.pallas_call(
        attention_kernel(local_heads, group_blocks, window_rows // MASK_BLOCK_SIZE - group_blocks, base),
        grid_spec=grid_spec,
        out_shape=jax.ShapeDtypeStruct((group_rows, chunk_heads * head_size), queries.dtype),
    )(meta, queries, key_window, value_window, vert_keys, vert_values)


def per_device(query_rows, key_matrix, value_matrix, vertical, slash_offsets):
    tok_rows = query_rows.shape[0]
    heads_axes = ("inner", "grp")
    head_groups = lax.axis_size("inner") * lax.axis_size("grp")
    head_size = HEAD_DIMENSION
    block_size = MASK_BLOCK_SIZE
    local_heads = query_rows.shape[1] // (head_groups * head_size)
    local_kv = key_matrix.shape[1] // (head_groups * head_size)
    group_sharing_factor = local_heads // local_kv
    query_split = query_rows.reshape(tok_rows, head_groups, local_heads * head_size)
    key_split = key_matrix.reshape(tok_rows, head_groups, local_kv * head_size)
    value_split = value_matrix.reshape(tok_rows, head_groups, local_kv * head_size)
    seq_count = lax.axis_size("outer")
    whole = seq_count * (key_split.size + value_split.size) * key_split.dtype.itemsize
    if whole <= FULL_GATHER_BYTES:
        kv_rows = jnp.stack([key_split, value_split], 0).transpose(2, 0, 1, 3)
        spread = jnp.broadcast_to(kv_rows[None], (seq_count,) + kv_rows.shape).reshape(
            (seq_count * head_groups,) + kv_rows.shape[1:]
        )
        everything = lax.all_to_all(
            spread, ("outer",) + heads_axes, split_axis=0, concat_axis=0, tiled=True
        )
    else:
        kv_split = jnp.stack([key_split, value_split], 2)
        kv_group = lax.all_to_all(kv_split, heads_axes, split_axis=1, concat_axis=0, tiled=True)
        key_group, value_group = kv_group[:, 0, 0], kv_group[:, 0, 1]
    me = lax.axis_index(heads_axes)
    received = [lax.dynamic_index_in_dim(query_split, me, 1, keepdims=False)]
    for shift in range(1, head_groups):
        sent = lax.dynamic_index_in_dim(query_split, (me + shift) % head_groups, 1, keepdims=False)
        received.append(
            lax.ppermute(sent, heads_axes, [(i, (i + shift) % head_groups) for i in range(head_groups)])
        )
    received = jnp.stack(received)
    group_rows = tok_rows * head_groups
    group_blocks = group_rows // block_size
    back = min(SLASH_REACH, group_blocks)
    seq_index = lax.axis_index("outer")
    head_group = lax.axis_index(heads_axes)
    head_offsets = lax.dynamic_slice_in_dim(slash_offsets, head_group * local_heads, local_heads, 0)
    head_verts = lax.dynamic_slice_in_dim(vertical, head_group * local_heads, local_heads, 0)
    first_block = (seq_index * group_blocks).astype(jnp.int32)
    meta = jnp.concatenate(
        [
            head_offsets.reshape(-1).astype(jnp.int32),
            head_verts.reshape(-1).astype(jnp.int32),
            first_block[None],
        ]
    )
    if whole <= FULL_GATHER_BYTES:
        queries = received.reshape(group_rows, local_heads * head_size)
        chunk_heads = local_heads // OUTPUT_CHUNKS
        pieces = []
        for c in range(OUTPUT_CHUNKS):
            results = attend_full(
                jnp.concatenate([meta, me.astype(jnp.int32)[None]]), queries, everything,
                local_heads, group_sharing_factor, tok_rows, c * chunk_heads, chunk_heads,
            )
            merged = results.reshape(head_groups, tok_rows, chunk_heads * head_size)
            pieces.append(lax.all_to_all(merged, heads_axes, split_axis=0, concat_axis=0, tiled=True))
        returned = jnp.concatenate(pieces, 2)
        return returned.transpose(1, 0, 2).reshape(tok_rows, head_groups * local_heads * head_size)
    slab_shift = (me - jnp.arange(head_groups, dtype=jnp.int32)) % head_groups
    query_group = jnp.take(received, slab_shift, axis=0)
    key_local = key_group.reshape(group_rows, local_kv * head_size)
    value_local = value_group.reshape(group_rows, local_kv * head_size)
    key_before, value_before = passed_along(
        (key_local[group_rows - back * block_size:], value_local[group_rows - back * block_size:]),
        "outer", 1,
    )
    key_window = jnp.concatenate([key_before, key_local], 0)
    value_window = jnp.concatenate([value_before, value_local], 0)
    kv_index = jnp.arange(local_heads, dtype=jnp.int32) // group_sharing_factor
    owner_seq = head_verts // group_blocks
    local_block = head_verts % group_blocks
    key_blocks = key_local.reshape(group_blocks, block_size, local_kv, head_size)
    value_blocks = value_local.reshape(group_blocks, block_size, local_kv, head_size)
    picked_keys = key_blocks[local_block, :, kv_index[:, None], :]
    picked_values = value_blocks[local_block, :, kv_index[:, None], :]
    owned = (owner_seq == seq_index)[:, :, None, None]
    nothing = jnp.zeros((), picked_keys.dtype)
    mine = jnp.stack(
        [jnp.where(owned, picked_keys, nothing), jnp.where(owned, picked_values, nothing)]
    ).reshape(2, seq_count, -1, head_size).transpose(1, 0, 2, 3)
    part = lax.all_to_all(mine, "outer", split_axis=0, concat_axis=0, tiled=True).sum(
        0, dtype=picked_keys.dtype
    )
    spread = jnp.broadcast_to(part[None], (seq_count,) + part.shape)
    gathered = lax.all_to_all(spread, "outer", split_axis=0, concat_axis=0, tiled=True)
    vert = gathered.transpose(1, 0, 2, 3).reshape(2, local_heads, -1, head_size)
    queries = query_group.reshape(group_rows, local_heads * head_size)
    results = attend(
        meta, queries, key_window, value_window, vert[0], vert[1],
        local_heads, group_sharing_factor, 0,
    )
    merged = results.reshape(head_groups, tok_rows, local_heads * head_size)
    returned = lax.all_to_all(merged, heads_axes, split_axis=0, concat_axis=0, tiled=True)
    return returned.transpose(1, 0, 2).reshape(tok_rows, head_groups * local_heads * head_size)


def solution(mesh):
    seq_count = mesh.shape["seq"]
    inner = 2 if seq_count % 2 == 0 else 1
    work_mesh = Mesh(
        mesh.devices.reshape(seq_count // inner, inner, mesh.shape["grp"]), ("outer", "inner", "grp")
    )
    rows = P(("outer", "inner", "grp"), None)
    return jax.shard_map(
        per_device,
        mesh=work_mesh,
        in_specs=(rows, rows, rows, P(), P()),
        out_specs=rows,
        check_vma=False,
    )
```
